32 devices in a mesh: dp: 16 (over z, x, core), tm: 2 (over y).
Axes of the slice: x: 2, y: 2, z: 4, core: 2. Of those that a mesh axis runs over, the one named last changes fastest.
Arguments:
- src_mel: bfloat16 [2, 128, 640], P('tm', 'dp'), may hold values from -6 to 6
- owner: int32 [2, 128], P('tm', 'dp'), may hold values from 0 to 15, as said below
- dst_pos: int32 [2, 128], P('tm', 'dp'), may hold values from 0 to 7, as said below
- keep: int32 [2, 128], P('tm', 'dp'), may hold values 0 or 1
- cotangent: bfloat16 [16, 1024, 256], P('dp', 'tm'), may hold values from -0.125 to 0.125
- w_pre: bfloat16 [560, 512], replicated, may hold values from -0.25 to 0.25
- b_pre: float32 [512], replicated, may hold values from -3 to 3
- w_ups: bfloat16 [512, 4096], P('tm'), may hold values from -0.1875 to 0.1875
- upsample_bias: float32 [256], replicated, may hold values from -3 to 3
- w_res: bfloat16 [768, 256], replicated, may hold values from -0.21875 to 0.21875
- b_res: float32 [256], replicated, may hold values from -3 to 3
Outputs:
- section_out: bfloat16 [16, 1024, 256], P('dp', 'tm')
- grad_w_pre: float32 [560, 512], replicated
- grad_b_pre: float32 [512], replicated
- grad_w_res: float32 [768, 256], replicated
- grad_b_res: float32 [256], replicated
The draws below stay inside these ranges and needn't reach their ends.
Inputs may be any that keep to these rules, and one draw needn't show every extreme that they name: Within one tm column, every dp index sends at most one of its segments to each owner, and every owner receives exactly 8 segments. `dst_pos`: the segments received by one owner in one column have positions 0 to 7, each once.
All inputs are finite; a program needn't handle non-finite values. No bound on the sum of `keep` on one device may be relied on, other than what follows from the above.
Results may differ from the reference program's by a relative error of at most 0.009.
The reference program's roundings to bfloat16 on the way count: a program that leaves them out, or rounds other values in their place, can miss the bound.
Values may be sent and summed in bfloat16 or wider, within the bound.
No kernel may reach another device: no remote copies, remote signals or barrier semaphores. Data moves between devices by JAX's collectives and lax.ppermute only.
A program may use at most 64 MiB of HBM per device.

```python
import jax
import jax.numpy as jnp
from jax import lax

MEL = 80
C0 = 512
C1 = 256
KPRE = 7
UPSAMPLE_FACTOR = 8
KUP = 16
KRES = 3
DILATION_SIZE = 3
FR_SEG = 8
SEG_DEV = 8
FRAMES = 128
SAMPLES = 1024
SEGS = 128
N_DP = 16
N_TM = 2


def route_tables(key):
    base = jax.random.fold_in(key, 7)
    column_keys = jax.random.split(base, N_TM)

    def column(ckey):
        keys = jax.random.split(ckey, 3)
        offsets = jax.random.permutation(keys[0], N_DP)[:SEG_DEV]
        relabel = jax.random.permutation(keys[1], N_DP)
        sources = jax.random.permutation(keys[2], N_DP)
        return relabel[(sources[:, None] + offsets[None, :]) % N_DP]
    owners = jax.vmap(column)(column_keys)
    pos_keys = jax.random.split(jax.random.fold_in(key, 11), N_TM * N_DP)
    orders = jax.vmap(lambda kernel_index: jax.random.permutation(kernel_index, SEG_DEV))(pos_keys).reshape(N_TM, N_DP, SEG_DEV)
    slot = jnp.broadcast_to(jnp.arange(SEG_DEV, dtype=jnp.int32)[None, None, :], owners.shape)
    col = jnp.broadcast_to(jnp.arange(N_TM, dtype=jnp.int32)[:, None, None], owners.shape)
    positions = orders[col, owners, slot]
    return (owners.reshape(N_TM, SEGS).astype(jnp.int32), positions.reshape(N_TM, SEGS).astype(jnp.int32))


def draw_owner(key, part):
    return route_tables(key)[0]


def draw_dst_pos(key, part):
    return route_tables(key)[1]


def with_ends(values, stream_key, least, largest):
    extent = values.shape
    spot = [jax.random.randint(jax.random.fold_in(stream_key, axis), (), 0, extent[axis]) for axis in range(len(extent))]
    values = values.at[tuple(spot)].set(least)
    longest = extent.index(max(extent))
    spot[longest] = (spot[longest] + 1) % extent[longest]
    return values.at[tuple(spot)].set(largest)


def shard_levels(stream_key, extent, shards, smallest, top_value):
    factor_of, own = 1.0, jax.random.fold_in(stream_key, 6)
    for axis_at, blocks in shards:
        draws = jnp.exp(jax.random.uniform(jax.random.fold_in(own, axis_at), (blocks,), jnp.float32, smallest / len(shards), top_value / len(shards)))
        factor_of = factor_of * jnp.repeat(draws, extent[axis_at] // blocks).reshape([-1 if axis == axis_at else 1 for axis in range(len(extent))])
    return factor_of


def normal_values(stream_key, extent, spread, reach, cuts=(), held_as=jnp.bfloat16):
    loudness = shard_levels(stream_key, extent, cuts, -0.22, 0.18) if cuts else 1.0
    entries = jax.random.normal(stream_key, extent, jnp.float32) * spread * loudness
    return jnp.minimum(jnp.maximum(entries, -reach), reach).astype(held_as)


def setup_inputs(seed: int = 0) -> dict:
    arg_keys = jax.random.split(jax.random.key(seed), 12)
    return {
        "src_mel": normal_values(arg_keys[0], (N_TM, SEGS, FR_SEG * MEL), 1.0, 6.0, ((0, 2), (1, 16))),
        "owner": draw_owner(jax.random.fold_in(arg_keys[11], 71), 0),
        "dst_pos": draw_dst_pos(jax.random.fold_in(arg_keys[11], 71), 0),
        "keep": with_ends((jax.random.randint(arg_keys[3], (N_TM, SEGS), 0, 4) < 3).astype(jnp.int32), jax.random.fold_in(arg_keys[3], 1), 0, 1),
        "cotangent": normal_values(arg_keys[4], (N_DP, SAMPLES, C1), ((SAMPLES * N_DP) ** -0.5), 0.125, ((0, 16), (1, 2))),
        "w_pre": normal_values(arg_keys[5], (KPRE * MEL, C0), (KPRE * MEL) ** -0.5, 0.25),
        "b_pre": normal_values(arg_keys[6], (C0,), 0.5, 3.0, (), jnp.float32),
        "w_ups": normal_values(arg_keys[7], (C0, KUP * C1), (2 * C0) ** -0.5, 0.1875, ((0, 2),)),
        "upsample_bias": normal_values(arg_keys[8], (C1,), 0.5, 3.0, (), jnp.float32),
        "w_res": normal_values(arg_keys[9], (KRES * C1, C1), (KRES * C1) ** -0.5, 0.21875),
        "b_res": normal_values(arg_keys[10], (C1,), 0.5, 3.0, (), jnp.float32),
    }


def leaky(value):
    return jnp.where(value > 0, value, 0.1 * value)


def negative_slope(value):
    return jnp.where(value > 0, 1.0, 0.1).astype(jnp.float32)


def local_pass(mel_ext, gradient_value, first_frame0, total, w_pre, b_pre, ups_forward, ups_backward, upsample_bias, w_res, b_res):
    mel_bins = mel_ext.shape[1]
    kpre = w_pre.shape[0] // mel_bins
    edge = kpre // 2 + 1
    frame_count = mel_ext.shape[0] - 2 * edge
    window_width = upsample_bias.shape[0]
    residual_kernel = w_res.shape[0] // window_width
    patches = jnp.concatenate([mel_ext[i:i + frame_count + 2] for i in range(kpre)], axis=1)
    pre = jnp.dot(patches, w_pre, preferred_element_type=jnp.float32) + b_pre
    frame_idx = first_frame0 - 1 + jnp.arange(frame_count + 2, dtype=jnp.int32)
    inside_f = ((frame_idx >= 0) & (frame_idx < total))[:, None]
    act = jnp.where(inside_f, leaky(pre), 0.0).astype(jnp.bfloat16)
    taps = ups_forward(act).reshape(frame_count + 2, 2 * UPSAMPLE_FACTOR, window_width)
    upper_output = taps[1:, :UPSAMPLE_FACTOR] + taps[:-1, UPSAMPLE_FACTOR:]
    sample_count = UPSAMPLE_FACTOR * frame_count
    start_offset = UPSAMPLE_FACTOR // 2 - DILATION_SIZE
    waveform = upper_output.reshape(UPSAMPLE_FACTOR * (frame_count + 1), window_width)[start_offset:start_offset + sample_count + 2 * DILATION_SIZE] + upsample_bias
    step_index = UPSAMPLE_FACTOR * first_frame0 - DILATION_SIZE + jnp.arange(sample_count + 2 * DILATION_SIZE, dtype=jnp.int32)
    inside_samples = ((step_index >= 0) & (step_index < UPSAMPLE_FACTOR * total))[:, None]
    hidden_state = jnp.where(inside_samples, leaky(waveform), 0.0).astype(jnp.bfloat16)
    column_block = jnp.concatenate([hidden_state[kernel_index * DILATION_SIZE:kernel_index * DILATION_SIZE + sample_count] for kernel_index in range(residual_kernel)], axis=1)
    convolve_fn = jnp.dot(column_block, w_res, preferred_element_type=jnp.float32) + b_res
    output_rows = (waveform[DILATION_SIZE:DILATION_SIZE + sample_count] + convolve_fn).astype(jnp.bfloat16)
    g_wres = jnp.dot(column_block.T, gradient_value, preferred_element_type=jnp.float32)
    g_bres = jnp.sum(gradient_value.astype(jnp.float32), axis=0)
    backward_pass = jnp.dot(gradient_value, w_res.T, preferred_element_type=jnp.float32)
    hidden_gradient = jnp.zeros((sample_count + 2 * DILATION_SIZE, window_width), jnp.float32)
    for kernel_index in range(residual_kernel):
        hidden_gradient = hidden_gradient + jnp.pad(backward_pass[:, kernel_index * window_width:(kernel_index + 1) * window_width], ((kernel_index * DILATION_SIZE, (residual_kernel - 1 - kernel_index) * DILATION_SIZE), (0, 0)))
    waveform_gradient = jnp.where(inside_samples, hidden_gradient * negative_slope(waveform), 0.0) + jnp.pad(gradient_value.astype(jnp.float32), ((DILATION_SIZE, DILATION_SIZE), (0, 0)))
    waveform_gradient = waveform_gradient.astype(jnp.bfloat16)
    d_upper = jnp.pad(waveform_gradient, ((start_offset, start_offset), (0, 0))).reshape(frame_count + 1, UPSAMPLE_FACTOR, window_width)
    zero_row = jnp.zeros((1, UPSAMPLE_FACTOR, window_width), jnp.bfloat16)
    d_taps = jnp.concatenate([jnp.concatenate([zero_row, d_upper], axis=0), jnp.concatenate([d_upper, zero_row], axis=0)], axis=1)
    d_act = ups_backward(d_taps.reshape(frame_count + 2, 2 * UPSAMPLE_FACTOR * window_width))
    d_pre = jnp.where(inside_f, d_act * negative_slope(pre), 0.0).astype(jnp.bfloat16)
    g_wpre = jnp.dot(patches.T, d_pre, preferred_element_type=jnp.float32)
    g_bpre = jnp.sum(d_pre.astype(jnp.float32), axis=0)
    return output_rows, (g_wpre, g_bpre, g_wres, g_bres)


def reference(src_mel, owner, dst_pos, keep, cotangent, w_pre, b_pre, w_ups, upsample_bias, w_res, b_res):
    column = jnp.broadcast_to(jnp.arange(N_TM, dtype=jnp.int32)[:, None], owner.shape)
    placed = jnp.zeros((N_DP, N_TM, SEG_DEV, FR_SEG * MEL), jnp.bfloat16).at[owner, column, dst_pos].set(src_mel)
    kept = jnp.zeros((N_DP, N_TM, SEG_DEV), jnp.int32).at[owner, column, dst_pos].set(keep)
    mel_all = placed.reshape(N_DP, FRAMES, MEL)
    keep_steps = jnp.repeat(kept.reshape(N_DP, N_TM * SEG_DEV), FR_SEG * UPSAMPLE_FACTOR, axis=1)
    edge = KPRE // 2 + 1

    def ups_forward(act):
        return jnp.dot(act, w_ups, preferred_element_type=jnp.float32)

    def ups_backward(d_taps):
        return jnp.dot(d_taps, w_ups.T, preferred_element_type=jnp.float32)

    def one(carry, item):
        mel, cot, marks = item
        mel_ext = jnp.pad(mel, ((edge, edge), (0, 0)))
        gradient_value = jnp.where(marks[:, None] > 0, cot, jnp.zeros_like(cot)).astype(jnp.bfloat16)
        output_rows, grads = local_pass(mel_ext, gradient_value, 0, FRAMES, w_pre, b_pre, ups_forward, ups_backward, upsample_bias, w_res, b_res)
        carry = tuple(a + b for a, b in zip(carry, grads))
        return carry, output_rows

    init = (jnp.zeros(w_pre.shape, jnp.float32), jnp.zeros(b_pre.shape, jnp.float32),
            jnp.zeros(w_res.shape, jnp.float32), jnp.zeros(b_res.shape, jnp.float32))
    totals, outs = lax.scan(one, init, (mel_all, cotangent, keep_steps))
    return outs, totals[0], totals[1], totals[2], totals[3]
```

```python
import jax
import jax.numpy as jnp
from jax import lax
from jax.sharding import PartitionSpec as P

KPRE = 7
UPSAMPLE_FACTOR = 8
DILATION_SIZE = 3


def with_halo(block, sides, width):
    for axis, dim in sides:
        count = lax.axis_size(axis)
        forward = [(i, i + 1) for i in range(count - 1)]
        backward = [(target, source) for source, target in forward]
        low = lax.ppermute(
            lax.slice_in_dim(block, block.shape[dim] - width, None, axis=dim), axis, forward
        )
        high = lax.ppermute(lax.slice_in_dim(block, 0, width, axis=dim), axis, backward)
        block = jnp.concatenate([low, block, high], axis=dim)
    return block


def leaky(value):
    return jnp.where(value > 0, value, 0.1 * value)


def negative_slope(value):
    return jnp.where(value > 0, 1.0, 0.1).astype(jnp.float32)


def contract_rows(left, right):
    return lax.dot_general(
        left, right, (((0,), (0,)), ((), ())), preferred_element_type=jnp.float32
    )


def contract_cols(left, right):
    return lax.dot_general(
        left, right, (((1,), (1,)), ((), ())), preferred_element_type=jnp.float32
    )


def local_pass(
    mel_ext,
    gradient_value,
    first_frame0,
    total,
    w_pre,
    b_pre,
    ups_forward,
    ups_backward,
    upsample_bias,
    w_res,
    b_res,
):
    mel_bins = mel_ext.shape[1]
    kpre = w_pre.shape[0] // mel_bins
    edge = kpre // 2 + 1
    frame_count = mel_ext.shape[0] - 2 * edge
    window_width = upsample_bias.shape[0]
    residual_kernel = w_res.shape[0] // window_width
    patches = jnp.concatenate([mel_ext[i : i + frame_count + 2] for i in range(kpre)], axis=1)
    pre = jnp.dot(patches, w_pre, preferred_element_type=jnp.float32) + b_pre
    frame_idx = first_frame0 - 1 + jnp.arange(frame_count + 2, dtype=jnp.int32)
    inside_f = ((frame_idx >= 0) & (frame_idx < total))[:, None]
    act = jnp.where(inside_f, leaky(pre), 0.0).astype(jnp.bfloat16)
    taps = ups_forward(act).reshape(frame_count + 2, 2 * UPSAMPLE_FACTOR, window_width)
    upper_output = taps[1:, :UPSAMPLE_FACTOR] + taps[:-1, UPSAMPLE_FACTOR:]
    sample_count = UPSAMPLE_FACTOR * frame_count
    start_offset = UPSAMPLE_FACTOR // 2 - DILATION_SIZE
    waveform = (
        upper_output.reshape(UPSAMPLE_FACTOR * (frame_count + 1), window_width)[
            start_offset : start_offset + sample_count + 2 * DILATION_SIZE
        ]
        + upsample_bias
    )
    step_index = (
        UPSAMPLE_FACTOR * first_frame0
        - DILATION_SIZE
        + jnp.arange(sample_count + 2 * DILATION_SIZE, dtype=jnp.int32)
    )
    inside_samples = ((step_index >= 0) & (step_index < UPSAMPLE_FACTOR * total))[:, None]
    hidden_state = jnp.where(inside_samples, leaky(waveform), 0.0).astype(jnp.bfloat16)
    column_block = jnp.concatenate(
        [
            hidden_state[kernel_index * DILATION_SIZE : kernel_index * DILATION_SIZE + sample_count]
            for kernel_index in range(residual_kernel)
        ],
        axis=1,
    )
    convolve_fn = jnp.dot(column_block, w_res, preferred_element_type=jnp.float32) + b_res
    output_rows = (waveform[DILATION_SIZE : DILATION_SIZE + sample_count] + convolve_fn).astype(
        jnp.bfloat16
    )
    g_wres = contract_rows(column_block, gradient_value)
    g_bres = jnp.sum(gradient_value.astype(jnp.float32), axis=0)
    backward_pass = contract_cols(gradient_value, w_res)
    hidden_gradient = jnp.zeros((sample_count + 2 * DILATION_SIZE, window_width), jnp.float32)
    for kernel_index in range(residual_kernel):
        hidden_gradient = hidden_gradient + jnp.pad(
            backward_pass[:, kernel_index * window_width : (kernel_index + 1) * window_width],
            (
                (
                    kernel_index * DILATION_SIZE,
                    (residual_kernel - 1 - kernel_index) * DILATION_SIZE,
                ),
                (0, 0),
            ),
        )
    waveform_gradient = jnp.where(
        inside_samples, hidden_gradient * negative_slope(waveform), 0.0
    ) + jnp.pad(gradient_value.astype(jnp.float32), ((DILATION_SIZE, DILATION_SIZE), (0, 0)))
    waveform_gradient = waveform_gradient.astype(jnp.bfloat16)
    d_upper = jnp.pad(waveform_gradient, ((start_offset, start_offset), (0, 0))).reshape(
        frame_count + 1, UPSAMPLE_FACTOR, window_width
    )
    zero_row = jnp.zeros((1, UPSAMPLE_FACTOR, window_width), jnp.bfloat16)
    d_taps = jnp.concatenate(
        [
            jnp.concatenate([zero_row, d_upper], axis=0),
            jnp.concatenate([d_upper, zero_row], axis=0),
        ],
        axis=1,
    )
    d_act = ups_backward(d_taps.reshape(frame_count + 2, 2 * UPSAMPLE_FACTOR * window_width))
    d_pre = jnp.where(inside_f, d_act * negative_slope(pre), 0.0).astype(jnp.bfloat16)
    g_wpre = contract_rows(patches, d_pre)
    g_bpre = jnp.sum(d_pre.astype(jnp.float32), axis=0)
    return (output_rows, (g_wpre, g_bpre, g_wres, g_bres))


def on_device(
    src_mel, owner, dst_pos, keep, cotangent, w_pre, b_pre, w_ups, upsample_bias, w_res, b_res
):
    owners_count = lax.axis_size("dp")
    seg_rows = src_mel[0]
    seg_count = seg_rows.shape[0]
    mel_bins = w_pre.shape[0] // KPRE
    pick = jnp.arange(owners_count, dtype=jnp.int32)[:, None] == owner[0][None, :]
    seg_width = seg_rows.shape[1]
    header = jnp.stack([dst_pos[0] + 1, keep[0]], axis=1).astype(jnp.bfloat16)
    seg_ext = jnp.concatenate([seg_rows, header], axis=1)
    outgoing = jnp.dot(
        pick.astype(jnp.bfloat16), seg_ext, preferred_element_type=jnp.float32
    ).astype(jnp.bfloat16)
    arrived = lax.all_to_all(outgoing, "dp", split_axis=0, concat_axis=0, tiled=True)
    slot_code = arrived[:, seg_width].astype(jnp.int32)
    keep_code = arrived[:, seg_width + 1].astype(jnp.int32)
    place = (slot_code - 1)[:, None] == jnp.arange(seg_count, dtype=jnp.int32)[None, :]
    mel_segs = contract_rows(place.astype(jnp.bfloat16), arrived[:, :seg_width]).astype(
        jnp.bfloat16
    )
    keep_segs = jnp.sum(jnp.where(place, keep_code[:, None], 0), axis=0)
    mel = mel_segs.reshape(seg_count * (mel_segs.shape[1] // mel_bins), mel_bins)
    frame_count = mel.shape[0]
    mel_ext = with_halo(mel, (("tm", 0),), KPRE // 2 + 1)
    first_frame0 = lax.axis_index("tm") * frame_count
    total = lax.axis_size("tm") * frame_count
    cot = cotangent[0]
    marks = jnp.repeat(keep_segs, cot.shape[0] // seg_count)
    gradient_value = jnp.where(marks[:, None] > 0, cot, jnp.zeros_like(cot))
    whole = lax.all_gather(w_ups, "tm", axis=0, tiled=True)

    def ups_forward(act):
        return jnp.dot(act, whole, preferred_element_type=jnp.float32)

    def ups_backward(d_taps):
        return contract_cols(d_taps, whole)

    output_rows, grads = local_pass(
        mel_ext,
        gradient_value,
        first_frame0,
        total,
        w_pre,
        b_pre,
        ups_forward,
        ups_backward,
        upsample_bias,
        w_res,
        b_res,
    )
    summed = lax.psum(grads, ("dp", "tm"))
    return (output_rows[None], summed[0], summed[1], summed[2], summed[3])


def solution(mesh):
    in_specs = (
        P("tm", "dp", None),
        P("tm", "dp"),
        P("tm", "dp"),
        P("tm", "dp"),
        P("dp", "tm", None),
        P(),
        P(),
        P("tm", None),
        P(),
        P(),
        P(),
    )
    out_specs = (P("dp", "tm", None), P(), P(), P(), P())
    return jax.shard_map(
        on_device, mesh=mesh, in_specs=in_specs, out_specs=out_specs, check_vma=False
    )
```

```python
import jax
import jax.numpy as jnp
from jax import lax
from jax.sharding import PartitionSpec as P

KPRE = 7
UPSAMPLE_FACTOR = 8
DILATION_SIZE = 3


def with_halo(block, sides, width):
    for axis, dim in sides:
        count = lax.axis_size(axis)
        forward = [(i, i + 1) for i in range(count - 1)]
        backward = [(target, source) for source, target in forward]
        low = lax.ppermute(
            lax.slice_in_dim(block, block.shape[dim] - width, None, axis=dim), axis, forward
        )
        high = lax.ppermute(lax.slice_in_dim(block, 0, width, axis=dim), axis, backward)
        block = jnp.concatenate([low, block, high], axis=dim)
    return block


def leaky(value):
    return jnp.where(value > 0, value, 0.1 * value)


def negative_slope(value):
    return jnp.where(value > 0, 1.0, 0.1).astype(jnp.float32)


def contract_rows(left, right):
    return lax.dot_general(
        left, right, (((0,), (0,)), ((), ())), preferred_element_type=jnp.float32
    )


def contract_cols(left, right):
    return lax.dot_general(
        left, right, (((1,), (1,)), ((), ())), preferred_element_type=jnp.float32
    )


def local_pass(
    mel_ext,
    gradient_value,
    first_frame0,
    total,
    w_pre,
    b_pre,
    ups_forward,
    ups_backward,
    upsample_bias,
    w_res,
    b_res,
):
    mel_bins = mel_ext.shape[1]
    kpre = w_pre.shape[0] // mel_bins
    edge = kpre // 2 + 1
    frame_count = mel_ext.shape[0] - 2 * edge
    window_width = upsample_bias.shape[0]
    residual_kernel = w_res.shape[0] // window_width
    patches = jnp.concatenate([mel_ext[i : i + frame_count + 2] for i in range(kpre)], axis=1)
    pre = jnp.dot(patches, w_pre, preferred_element_type=jnp.float32) + b_pre
    frame_idx = first_frame0 - 1 + jnp.arange(frame_count + 2, dtype=jnp.int32)
    inside_f = ((frame_idx >= 0) & (frame_idx < total))[:, None]
    act = jnp.where(inside_f, leaky(pre), 0.0).astype(jnp.bfloat16)
    taps = ups_forward(act).reshape(frame_count + 2, 2 * UPSAMPLE_FACTOR, window_width)
    upper_output = taps[1:, :UPSAMPLE_FACTOR] + taps[:-1, UPSAMPLE_FACTOR:]
    sample_count = UPSAMPLE_FACTOR * frame_count
    start_offset = UPSAMPLE_FACTOR // 2 - DILATION_SIZE
    waveform = (
        upper_output.reshape(UPSAMPLE_FACTOR * (frame_count + 1), window_width)[
            start_offset : start_offset + sample_count + 2 * DILATION_SIZE
        ]
        + upsample_bias
    )
    step_index = (
        UPSAMPLE_FACTOR * first_frame0
        - DILATION_SIZE
        + jnp.arange(sample_count + 2 * DILATION_SIZE, dtype=jnp.int32)
    )
    inside_samples = ((step_index >= 0) & (step_index < UPSAMPLE_FACTOR * total))[:, None]
    hidden_state = jnp.where(inside_samples, leaky(waveform), 0.0).astype(jnp.bfloat16)
    column_block = jnp.concatenate(
        [
            hidden_state[kernel_index * DILATION_SIZE : kernel_index * DILATION_SIZE + sample_count]
            for kernel_index in range(residual_kernel)
        ],
        axis=1,
    )
    convolve_fn = jnp.dot(column_block, w_res, preferred_element_type=jnp.float32) + b_res
    output_rows = (waveform[DILATION_SIZE : DILATION_SIZE + sample_count] + convolve_fn).astype(
        jnp.bfloat16
    )
    g_wres = contract_rows(column_block, gradient_value)
    g_bres = jnp.sum(gradient_value.astype(jnp.float32), axis=0)
    backward_pass = contract_cols(gradient_value, w_res)
    hidden_gradient = jnp.zeros((sample_count + 2 * DILATION_SIZE, window_width), jnp.float32)
    for kernel_index in range(residual_kernel):
        hidden_gradient = hidden_gradient + jnp.pad(
            backward_pass[:, kernel_index * window_width : (kernel_index + 1) * window_width],
            (
                (
                    kernel_index * DILATION_SIZE,
                    (residual_kernel - 1 - kernel_index) * DILATION_SIZE,
                ),
                (0, 0),
            ),
        )
    waveform_gradient = jnp.where(
        inside_samples, hidden_gradient * negative_slope(waveform), 0.0
    ) + jnp.pad(gradient_value.astype(jnp.float32), ((DILATION_SIZE, DILATION_SIZE), (0, 0)))
    waveform_gradient = waveform_gradient.astype(jnp.bfloat16)
    d_upper = jnp.pad(waveform_gradient, ((start_offset, start_offset), (0, 0))).reshape(
        frame_count + 1, UPSAMPLE_FACTOR, window_width
    )
    zero_row = jnp.zeros((1, UPSAMPLE_FACTOR, window_width), jnp.bfloat16)
    d_taps = jnp.concatenate(
        [
            jnp.concatenate([zero_row, d_upper], axis=0),
            jnp.concatenate([d_upper, zero_row], axis=0),
        ],
        axis=1,
    )
    d_act = ups_backward(d_taps.reshape(frame_count + 2, 2 * UPSAMPLE_FACTOR * window_width))
    d_pre = jnp.where(inside_f, d_act * negative_slope(pre), 0.0).astype(jnp.bfloat16)
    g_wpre = contract_rows(patches, d_pre)
    g_bpre = jnp.sum(d_pre.astype(jnp.float32), axis=0)
    return (output_rows, (g_wpre, g_bpre, g_wres, g_bres))


def butterfly_psum(parts):
    dp_size = lax.axis_size("dp")
    tm_size = lax.axis_size("tm")
    steps = [("dp", 1)]
    steps += [("tm", 1 << k) for k in range(tm_size.bit_length() - 1)]
    steps += [("dp", 1 << k) for k in range(1, dp_size.bit_length() - 1)]
    flat = jnp.concatenate([p.reshape(-1) for p in parts])
    unit = 8 * 128 * dp_size * tm_size
    padded = -(-flat.shape[0] // unit) * unit
    x = jnp.pad(flat, (0, padded - flat.shape[0])).reshape(padded // 128, 128)
    for axis, bit in steps:
        half = x.shape[0] // 2
        upper = (lax.axis_index(axis) // bit) % 2
        send = lax.dynamic_slice_in_dim(x, (1 - upper) * half, half)
        keep = lax.dynamic_slice_in_dim(x, upper * half, half)
        perm = [(i, i ^ bit) for i in range(lax.axis_size(axis))]
        x = keep + lax.ppermute(send, axis, perm)
    for axis, bit in reversed(steps):
        rows = x.shape[0]
        upper = (lax.axis_index(axis) // bit) % 2
        perm = [(i, i ^ bit) for i in range(lax.axis_size(axis))]
        recv = lax.ppermute(x, axis, perm)
        both = jnp.zeros((2 * rows, 128), x.dtype)
        both = lax.dynamic_update_slice_in_dim(both, x, upper * rows, 0)
        x = lax.dynamic_update_slice_in_dim(both, recv, (1 - upper) * rows, 0)
    flat = x.reshape(-1)
    out, at = [], 0
    for p in parts:
        out.append(flat[at : at + p.size].reshape(p.shape))
        at += p.size
    return tuple(out)


def on_device(
    src_mel, owner, dst_pos, keep, cotangent, w_pre, b_pre, w_ups, upsample_bias, w_res, b_res
):
    owners_count = lax.axis_size("dp")
    seg_rows = src_mel[0]
    seg_count = seg_rows.shape[0]
    mel_bins = w_pre.shape[0] // KPRE
    pick = jnp.arange(owners_count, dtype=jnp.int32)[:, None] == owner[0][None, :]
    seg_width = seg_rows.shape[1]
    header = jnp.stack([dst_pos[0] + 1, keep[0]], axis=1).astype(jnp.bfloat16)
    seg_ext = jnp.concatenate([seg_rows, header], axis=1)
    outgoing = jnp.dot(
        pick.astype(jnp.bfloat16), seg_ext, preferred_element_type=jnp.float32
    ).astype(jnp.bfloat16)
    arrived = lax.all_to_all(outgoing, "dp", split_axis=0, concat_axis=0, tiled=True)
    slot_code = arrived[:, seg_width].astype(jnp.int32)
    keep_code = arrived[:, seg_width + 1].astype(jnp.int32)
    place = (slot_code - 1)[:, None] == jnp.arange(seg_count, dtype=jnp.int32)[None, :]
    mel_segs = contract_rows(place.astype(jnp.bfloat16), arrived[:, :seg_width]).astype(
        jnp.bfloat16
    )
    keep_segs = jnp.sum(jnp.where(place, keep_code[:, None], 0), axis=0)
    mel = mel_segs.reshape(seg_count * (mel_segs.shape[1] // mel_bins), mel_bins)
    frame_count = mel.shape[0]
    mel_ext = with_halo(mel, (("tm", 0),), KPRE // 2 + 1)
    first_frame0 = lax.axis_index("tm") * frame_count
    total = lax.axis_size("tm") * frame_count
    cot = cotangent[0]
    marks = jnp.repeat(keep_segs, cot.shape[0] // seg_count)
    gradient_value = jnp.where(marks[:, None] > 0, cot, jnp.zeros_like(cot))
    whole = lax.all_gather(w_ups, "tm", axis=0, tiled=True)

    def ups_forward(act):
        return jnp.dot(act, whole, preferred_element_type=jnp.float32)

    def ups_backward(d_taps):
        return contract_cols(d_taps, whole)

    output_rows, grads = local_pass(
        mel_ext,
        gradient_value,
        first_frame0,
        total,
        w_pre,
        b_pre,
        ups_forward,
        ups_backward,
        upsample_bias,
        w_res,
        b_res,
    )
    summed = butterfly_psum(grads)
    return (output_rows[None], summed[0], summed[1], summed[2], summed[3])


def solution(mesh):
    in_specs = (
        P("tm", "dp", None),
        P("tm", "dp"),
        P("tm", "dp"),
        P("tm", "dp"),
        P("dp", "tm", None),
        P(),
        P(),
        P("tm", None),
        P(),
        P(),
        P(),
    )
    out_specs = (P("dp", "tm", None), P(), P(), P(), P())
    return jax.shard_map(
        on_device, mesh=mesh, in_specs=in_specs, out_specs=out_specs, check_vma=False
    )
```

```python
import jax
import jax.numpy as jnp
from jax import lax
from jax.sharding import PartitionSpec as P

KPRE = 7
UPSAMPLE_FACTOR = 8
DILATION_SIZE = 3


def with_halo(block, sides, width):
    for axis, dim in sides:
        count = lax.axis_size(axis)
        forward = [(i, i + 1) for i in range(count - 1)]
        backward = [(target, source) for source, target in forward]
        low = lax.ppermute(
            lax.slice_in_dim(block, block.shape[dim] - width, None, axis=dim), axis, forward
        )
        high = lax.ppermute(lax.slice_in_dim(block, 0, width, axis=dim), axis, backward)
        block = jnp.concatenate([low, block, high], axis=dim)
    return block


def leaky(value):
    return jnp.where(value > 0, value, 0.1 * value)


def negative_slope(value):
    return jnp.where(value > 0, 1.0, 0.1).astype(jnp.float32)


def contract_rows(left, right):
    return lax.dot_general(
        left, right, (((0,), (0,)), ((), ())), preferred_element_type=jnp.float32
    )


def contract_cols(left, right):
    return lax.dot_general(
        left, right, (((1,), (1,)), ((), ())), preferred_element_type=jnp.float32
    )


def local_pass(
    mel_ext,
    gradient_value,
    first_frame0,
    total,
    w_pre,
    b_pre,
    ups_forward,
    ups_backward,
    upsample_bias,
    w_res,
    b_res,
):
    mel_bins = mel_ext.shape[1]
    kpre = w_pre.shape[0] // mel_bins
    edge = kpre // 2 + 1
    frame_count = mel_ext.shape[0] - 2 * edge
    window_width = upsample_bias.shape[0]
    residual_kernel = w_res.shape[0] // window_width
    patches = jnp.concatenate([mel_ext[i : i + frame_count + 2] for i in range(kpre)], axis=1)
    pre = jnp.dot(patches, w_pre, preferred_element_type=jnp.float32) + b_pre
    frame_idx = first_frame0 - 1 + jnp.arange(frame_count + 2, dtype=jnp.int32)
    inside_f = ((frame_idx >= 0) & (frame_idx < total))[:, None]
    act = jnp.where(inside_f, leaky(pre), 0.0).astype(jnp.bfloat16)
    taps = ups_forward(act).reshape(frame_count + 2, 2 * UPSAMPLE_FACTOR, window_width)
    upper_output = taps[1:, :UPSAMPLE_FACTOR] + taps[:-1, UPSAMPLE_FACTOR:]
    sample_count = UPSAMPLE_FACTOR * frame_count
    start_offset = UPSAMPLE_FACTOR // 2 - DILATION_SIZE
    waveform = (
        upper_output.reshape(UPSAMPLE_FACTOR * (frame_count + 1), window_width)[
            start_offset : start_offset + sample_count + 2 * DILATION_SIZE
        ]
        + upsample_bias
    )
    step_index = (
        UPSAMPLE_FACTOR * first_frame0
        - DILATION_SIZE
        + jnp.arange(sample_count + 2 * DILATION_SIZE, dtype=jnp.int32)
    )
    inside_samples = ((step_index >= 0) & (step_index < UPSAMPLE_FACTOR * total))[:, None]
    hidden_state = jnp.where(inside_samples, leaky(waveform), 0.0).astype(jnp.bfloat16)
    column_block = jnp.concatenate(
        [
            hidden_state[kernel_index * DILATION_SIZE : kernel_index * DILATION_SIZE + sample_count]
            for kernel_index in range(residual_kernel)
        ],
        axis=1,
    )
    convolve_fn = jnp.dot(column_block, w_res, preferred_element_type=jnp.float32) + b_res
    output_rows = (waveform[DILATION_SIZE : DILATION_SIZE + sample_count] + convolve_fn).astype(
        jnp.bfloat16
    )
    g_wres = contract_rows(column_block, gradient_value)
    g_bres = jnp.sum(gradient_value.astype(jnp.float32), axis=0)
    backward_pass = contract_cols(gradient_value, w_res)
    hidden_gradient = jnp.zeros((sample_count + 2 * DILATION_SIZE, window_width), jnp.float32)
    for kernel_index in range(residual_kernel):
        hidden_gradient = hidden_gradient + jnp.pad(
            backward_pass[:, kernel_index * window_width : (kernel_index + 1) * window_width],
            (
                (
                    kernel_index * DILATION_SIZE,
                    (residual_kernel - 1 - kernel_index) * DILATION_SIZE,
                ),
                (0, 0),
            ),
        )
    waveform_gradient = jnp.where(
        inside_samples, hidden_gradient * negative_slope(waveform), 0.0
    ) + jnp.pad(gradient_value.astype(jnp.float32), ((DILATION_SIZE, DILATION_SIZE), (0, 0)))
    waveform_gradient = waveform_gradient.astype(jnp.bfloat16)
    d_upper = jnp.pad(waveform_gradient, ((start_offset, start_offset), (0, 0))).reshape(
        frame_count + 1, UPSAMPLE_FACTOR, window_width
    )
    zero_row = jnp.zeros((1, UPSAMPLE_FACTOR, window_width), jnp.bfloat16)
    d_taps = jnp.concatenate(
        [
            jnp.concatenate([zero_row, d_upper], axis=0),
            jnp.concatenate([d_upper, zero_row], axis=0),
        ],
        axis=1,
    )
    d_act = ups_backward(d_taps.reshape(frame_count + 2, 2 * UPSAMPLE_FACTOR * window_width))
    d_pre = jnp.where(inside_f, d_act * negative_slope(pre), 0.0).astype(jnp.bfloat16)
    g_wpre = contract_rows(patches, d_pre)
    g_bpre = jnp.sum(d_pre.astype(jnp.float32), axis=0)
    return (output_rows, (g_wpre, g_bpre, g_wres, g_bres))


def butterfly_psum(parts):
    dp_size = lax.axis_size("dp")
    tm_size = lax.axis_size("tm")
    steps = [("dp", 1)]
    steps += [("tm", 1 << k) for k in range(tm_size.bit_length() - 1)]
    steps += [("dp", 1 << k) for k in range(1, dp_size.bit_length() - 1)]
    flat = jnp.concatenate([p.reshape(-1) for p in parts])
    unit = 8 * 128 * dp_size * tm_size
    padded = -(-flat.shape[0] // unit) * unit
    x = jnp.pad(flat, (0, padded - flat.shape[0])).reshape(padded // 128, 128)
    for axis, bit in steps:
        half = x.shape[0] // 2
        upper = (lax.axis_index(axis) // bit) % 2
        send = lax.dynamic_slice_in_dim(x, (1 - upper) * half, half)
        keep = lax.dynamic_slice_in_dim(x, upper * half, half)
        perm = [(i, i ^ bit) for i in range(lax.axis_size(axis))]
        x = keep + lax.ppermute(send, axis, perm)
    for axis, bit in reversed(steps):
        rows = x.shape[0]
        upper = (lax.axis_index(axis) // bit) % 2
        perm = [(i, i ^ bit) for i in range(lax.axis_size(axis))]
        recv = lax.ppermute(x, axis, perm)
        both = jnp.zeros((2 * rows, 128), x.dtype)
        both = lax.dynamic_update_slice_in_dim(both, x, upper * rows, 0)
        x = lax.dynamic_update_slice_in_dim(both, recv, (1 - upper) * rows, 0)
    flat = x.reshape(-1)
    out, at = [], 0
    for p in parts:
        out.append(flat[at : at + p.size].reshape(p.shape))
        at += p.size
    return tuple(out)


def gather_rows(w_ups):
    dp_size = lax.axis_size("dp")
    if lax.axis_size("tm") != 2 or dp_size % 2:
        return lax.all_gather(w_ups, "tm", axis=0, tiled=True)
    rows, width = w_ups.shape
    cols = width // 2
    core = lax.axis_index("dp") % 2
    tm = lax.axis_index("tm")
    mine = lax.dynamic_slice_in_dim(w_ups, core * cols, cols, axis=1)
    got = lax.ppermute(mine, "tm", [(0, 1), (1, 0)])
    partner = lax.ppermute(got, "dp", [(i, i ^ 1) for i in range(dp_size)])
    whole = jnp.zeros((2 * rows, width), w_ups.dtype)
    whole = lax.dynamic_update_slice(whole, w_ups, (tm * rows, 0))
    whole = lax.dynamic_update_slice(whole, got, ((1 - tm) * rows, core * cols))
    return lax.dynamic_update_slice(whole, partner, ((1 - tm) * rows, (1 - core) * cols))


def on_device(
    src_mel, owner, dst_pos, keep, cotangent, w_pre, b_pre, w_ups, upsample_bias, w_res, b_res
):
    owners_count = lax.axis_size("dp")
    seg_rows = src_mel[0]
    seg_count = seg_rows.shape[0]
    mel_bins = w_pre.shape[0] // KPRE
    pick = jnp.arange(owners_count, dtype=jnp.int32)[:, None] == owner[0][None, :]
    seg_width = seg_rows.shape[1]
    header = jnp.stack([dst_pos[0] + 1, keep[0]], axis=1).astype(jnp.bfloat16)
    seg_ext = jnp.concatenate([seg_rows, header], axis=1)
    outgoing = jnp.dot(
        pick.astype(jnp.bfloat16), seg_ext, preferred_element_type=jnp.float32
    ).astype(jnp.bfloat16)
    arrived = lax.all_to_all(outgoing, "dp", split_axis=0, concat_axis=0, tiled=True)
    slot_code = arrived[:, seg_width].astype(jnp.int32)
    keep_code = arrived[:, seg_width + 1].astype(jnp.int32)
    place = (slot_code - 1)[:, None] == jnp.arange(seg_count, dtype=jnp.int32)[None, :]
    mel_segs = contract_rows(place.astype(jnp.bfloat16), arrived[:, :seg_width]).astype(
        jnp.bfloat16
    )
    keep_segs = jnp.sum(jnp.where(place, keep_code[:, None], 0), axis=0)
    mel = mel_segs.reshape(seg_count * (mel_segs.shape[1] // mel_bins), mel_bins)
    frame_count = mel.shape[0]
    mel_ext = with_halo(mel, (("tm", 0),), KPRE // 2 + 1)
    first_frame0 = lax.axis_index("tm") * frame_count
    total = lax.axis_size("tm") * frame_count
    cot = cotangent[0]
    marks = jnp.repeat(keep_segs, cot.shape[0] // seg_count)
    gradient_value = jnp.where(marks[:, None] > 0, cot, jnp.zeros_like(cot))
    whole = gather_rows(w_ups)

    def ups_forward(act):
        return jnp.dot(act, whole, preferred_element_type=jnp.float32)

    def ups_backward(d_taps):
        return contract_cols(d_taps, whole)

    output_rows, grads = local_pass(
        mel_ext,
        gradient_value,
        first_frame0,
        total,
        w_pre,
        b_pre,
        ups_forward,
        ups_backward,
        upsample_bias,
        w_res,
        b_res,
    )
    summed = butterfly_psum(grads)
    return (output_rows[None], summed[0], summed[1], summed[2], summed[3])


def solution(mesh):
    in_specs = (
        P("tm", "dp", None),
        P("tm", "dp"),
        P("tm", "dp"),
        P("tm", "dp"),
        P("dp", "tm", None),
        P(),
        P(),
        P("tm", None),
        P(),
        P(),
        P(),
    )
    out_specs = (P("dp", "tm", None), P(), P(), P(), P())
    return jax.shard_map(
        on_device, mesh=mesh, in_specs=in_specs, out_specs=out_specs, check_vma=False
    )
```

```python
import jax
import jax.numpy as jnp
from jax import lax
from jax.sharding import PartitionSpec as P

KPRE = 7
UPSAMPLE_FACTOR = 8
DILATION_SIZE = 3


def with_halo(block, sides, width):
    for axis, dim in sides:
        count = lax.axis_size(axis)
        forward = [(i, i + 1) for i in range(count - 1)]
        backward = [(target, source) for source, target in forward]
        low = lax.ppermute(
            lax.slice_in_dim(block, block.shape[dim] - width, None, axis=dim), axis, forward
        )
        high = lax.ppermute(lax.slice_in_dim(block, 0, width, axis=dim), axis, backward)
        block = jnp.concatenate([low, block, high], axis=dim)
    return block


def leaky(value):
    return jnp.where(value > 0, value, 0.1 * value)


def negative_slope(value):
    return jnp.where(value > 0, 1.0, 0.1).astype(jnp.float32)


def contract_rows(left, right):
    return lax.dot_general(
        left, right, (((0,), (0,)), ((), ())), preferred_element_type=jnp.float32
    )


def contract_cols(left, right):
    return lax.dot_general(
        left, right, (((1,), (1,)), ((), ())), preferred_element_type=jnp.float32
    )


def local_pass(
    mel_ext,
    gradient_value,
    first_frame0,
    total,
    w_pre,
    b_pre,
    ups_forward,
    ups_backward,
    upsample_bias,
    w_res,
    b_res,
):
    mel_bins = mel_ext.shape[1]
    kpre = w_pre.shape[0] // mel_bins
    edge = kpre // 2 + 1
    frame_count = mel_ext.shape[0] - 2 * edge
    window_width = upsample_bias.shape[0]
    residual_kernel = w_res.shape[0] // window_width
    patches = jnp.concatenate([mel_ext[i : i + frame_count + 2] for i in range(kpre)], axis=1)
    pre = jnp.dot(patches, w_pre, preferred_element_type=jnp.float32) + b_pre
    frame_idx = first_frame0 - 1 + jnp.arange(frame_count + 2, dtype=jnp.int32)
    inside_f = ((frame_idx >= 0) & (frame_idx < total))[:, None]
    act = jnp.where(inside_f, leaky(pre), 0.0).astype(jnp.bfloat16)
    taps = ups_forward(act).reshape(frame_count + 2, 2 * UPSAMPLE_FACTOR, window_width)
    upper_output = taps[1:, :UPSAMPLE_FACTOR] + taps[:-1, UPSAMPLE_FACTOR:]
    sample_count = UPSAMPLE_FACTOR * frame_count
    start_offset = UPSAMPLE_FACTOR // 2 - DILATION_SIZE
    waveform = (
        upper_output.reshape(UPSAMPLE_FACTOR * (frame_count + 1), window_width)[
            start_offset : start_offset + sample_count + 2 * DILATION_SIZE
        ]
        + upsample_bias
    )
    step_index = (
        UPSAMPLE_FACTOR * first_frame0
        - DILATION_SIZE
        + jnp.arange(sample_count + 2 * DILATION_SIZE, dtype=jnp.int32)
    )
    inside_samples = ((step_index >= 0) & (step_index < UPSAMPLE_FACTOR * total))[:, None]
    hidden_state = jnp.where(inside_samples, leaky(waveform), 0.0).astype(jnp.bfloat16)
    column_block = jnp.concatenate(
        [
            hidden_state[kernel_index * DILATION_SIZE : kernel_index * DILATION_SIZE + sample_count]
            for kernel_index in range(residual_kernel)
        ],
        axis=1,
    )
    convolve_fn = jnp.dot(column_block, w_res, preferred_element_type=jnp.float32) + b_res
    output_rows = (waveform[DILATION_SIZE : DILATION_SIZE + sample_count] + convolve_fn).astype(
        jnp.bfloat16
    )
    g_wres = contract_rows(column_block, gradient_value)
    g_bres = jnp.sum(gradient_value.astype(jnp.float32), axis=0)
    backward_pass = contract_cols(gradient_value, w_res)
    hidden_gradient = jnp.zeros((sample_count + 2 * DILATION_SIZE, window_width), jnp.float32)
    for kernel_index in range(residual_kernel):
        hidden_gradient = hidden_gradient + jnp.pad(
            backward_pass[:, kernel_index * window_width : (kernel_index + 1) * window_width],
            (
                (
                    kernel_index * DILATION_SIZE,
                    (residual_kernel - 1 - kernel_index) * DILATION_SIZE,
                ),
                (0, 0),
            ),
        )
    waveform_gradient = jnp.where(
        inside_samples, hidden_gradient * negative_slope(waveform), 0.0
    ) + jnp.pad(gradient_value.astype(jnp.float32), ((DILATION_SIZE, DILATION_SIZE), (0, 0)))
    waveform_gradient = waveform_gradient.astype(jnp.bfloat16)
    d_upper = jnp.pad(waveform_gradient, ((start_offset, start_offset), (0, 0))).reshape(
        frame_count + 1, UPSAMPLE_FACTOR, window_width
    )
    zero_row = jnp.zeros((1, UPSAMPLE_FACTOR, window_width), jnp.bfloat16)
    d_taps = jnp.concatenate(
        [
            jnp.concatenate([zero_row, d_upper], axis=0),
            jnp.concatenate([d_upper, zero_row], axis=0),
        ],
        axis=1,
    )
    d_act = ups_backward(d_taps.reshape(frame_count + 2, 2 * UPSAMPLE_FACTOR * window_width))
    d_pre = jnp.where(inside_f, d_act * negative_slope(pre), 0.0).astype(jnp.bfloat16)
    g_wpre = contract_rows(patches, d_pre)
    g_bpre = jnp.sum(d_pre.astype(jnp.float32), axis=0)
    return (output_rows, (g_wpre, g_bpre, g_wres, g_bres))


def butterfly_psum(parts):
    dp_size = lax.axis_size("dp")
    tm_size = lax.axis_size("tm")
    steps = [("dp", 1)]
    steps += [("tm", 1 << k) for k in range(tm_size.bit_length() - 1)]
    steps += [("dp", 1 << k) for k in range(1, dp_size.bit_length() - 1)]
    flat = jnp.concatenate([p.reshape(-1) for p in parts])
    unit = 8 * 128 * dp_size * tm_size
    padded = -(-flat.shape[0] // unit) * unit
    x = jnp.pad(flat, (0, padded - flat.shape[0])).reshape(padded // 128, 128)
    for axis, bit in steps:
        half = x.shape[0] // 2
        upper = (lax.axis_index(axis) // bit) % 2
        send = lax.dynamic_slice_in_dim(x, (1 - upper) * half, half)
        keep = lax.dynamic_slice_in_dim(x, upper * half, half)
        perm = [(i, i ^ bit) for i in range(lax.axis_size(axis))]
        x = keep + lax.ppermute(send, axis, perm)
    for axis, bit in reversed(steps):
        rows = x.shape[0]
        upper = (lax.axis_index(axis) // bit) % 2
        perm = [(i, i ^ bit) for i in range(lax.axis_size(axis))]
        recv = lax.ppermute(x, axis, perm)
        both = jnp.zeros((2 * rows, 128), x.dtype)
        both = lax.dynamic_update_slice_in_dim(both, x, upper * rows, 0)
        x = lax.dynamic_update_slice_in_dim(both, recv, (1 - upper) * rows, 0)
    flat = x.reshape(-1)
    out, at = [], 0
    for p in parts:
        out.append(flat[at : at + p.size].reshape(p.shape))
        at += p.size
    return tuple(out)


def ups_functions(w_ups):
    dp_size = lax.axis_size("dp")
    if lax.axis_size("tm") != 2 or dp_size % 2:
        whole = lax.all_gather(w_ups, "tm", axis=0, tiled=True)
        return (
            lambda act: jnp.dot(act, whole, preferred_element_type=jnp.float32),
            lambda d_taps: contract_cols(d_taps, whole),
        )
    rows, width = w_ups.shape
    cols = width // 2
    core = lax.axis_index("dp") % 2
    tm = lax.axis_index("tm")
    mine = jnp.where(core == 0, w_ups[:, :cols], w_ups[:, cols:])
    got = lax.ppermute(mine, "tm", [(0, 1), (1, 0)])
    partner = lax.ppermute(got, "dp", [(i, i ^ 1) for i in range(dp_size)])
    low = jnp.where(core == 0, got, partner)
    high = jnp.where(core == 0, partner, got)

    def forward(act):
        own_act = lax.dynamic_slice_in_dim(act, tm * rows, rows, axis=1)
        other_act = lax.dynamic_slice_in_dim(act, (1 - tm) * rows, rows, axis=1)
        own = jnp.dot(own_act, w_ups, preferred_element_type=jnp.float32)
        other = jnp.concatenate(
            [
                jnp.dot(other_act, low, preferred_element_type=jnp.float32),
                jnp.dot(other_act, high, preferred_element_type=jnp.float32),
            ],
            axis=1,
        )
        return own + other

    def backward(d_taps):
        own = contract_cols(d_taps, w_ups)
        other = contract_cols(d_taps[:, :cols], low) + contract_cols(d_taps[:, cols:], high)
        return jnp.where(
            tm == 0, jnp.concatenate([own, other], axis=1), jnp.concatenate([other, own], axis=1)
        )

    return forward, backward


def on_device(
    src_mel, owner, dst_pos, keep, cotangent, w_pre, b_pre, w_ups, upsample_bias, w_res, b_res
):
    owners_count = lax.axis_size("dp")
    seg_rows = src_mel[0]
    seg_count = seg_rows.shape[0]
    mel_bins = w_pre.shape[0] // KPRE
    pick = jnp.arange(owners_count, dtype=jnp.int32)[:, None] == owner[0][None, :]
    seg_width = seg_rows.shape[1]
    header = jnp.stack([dst_pos[0] + 1, keep[0]], axis=1).astype(jnp.bfloat16)
    seg_ext = jnp.concatenate([seg_rows, header], axis=1)
    outgoing = jnp.dot(
        pick.astype(jnp.bfloat16), seg_ext, preferred_element_type=jnp.float32
    ).astype(jnp.bfloat16)
    arrived = lax.all_to_all(outgoing, "dp", split_axis=0, concat_axis=0, tiled=True)
    slot_code = arrived[:, seg_width].astype(jnp.int32)
    keep_code = arrived[:, seg_width + 1].astype(jnp.int32)
    place = (slot_code - 1)[:, None] == jnp.arange(seg_count, dtype=jnp.int32)[None, :]
    mel_segs = contract_rows(place.astype(jnp.bfloat16), arrived[:, :seg_width]).astype(
        jnp.bfloat16
    )
    keep_segs = jnp.sum(jnp.where(place, keep_code[:, None], 0), axis=0)
    mel = mel_segs.reshape(seg_count * (mel_segs.shape[1] // mel_bins), mel_bins)
    frame_count = mel.shape[0]
    mel_ext = with_halo(mel, (("tm", 0),), KPRE // 2 + 1)
    first_frame0 = lax.axis_index("tm") * frame_count
    total = lax.axis_size("tm") * frame_count
    cot = cotangent[0]
    marks = jnp.repeat(keep_segs, cot.shape[0] // seg_count)
    gradient_value = jnp.where(marks[:, None] > 0, cot, jnp.zeros_like(cot))
    ups_forward, ups_backward = ups_functions(w_ups)

    output_rows, grads = local_pass(
        mel_ext,
        gradient_value,
        first_frame0,
        total,
        w_pre,
        b_pre,
        ups_forward,
        ups_backward,
        upsample_bias,
        w_res,
        b_res,
    )
    summed = butterfly_psum(grads)
    return (output_rows[None], summed[0], summed[1], summed[2], summed[3])


def solution(mesh):
    in_specs = (
        P("tm", "dp", None),
        P("tm", "dp"),
        P("tm", "dp"),
        P("tm", "dp"),
        P("dp", "tm", None),
        P(),
        P(),
        P("tm", None),
        P(),
        P(),
        P(),
    )
    out_specs = (P("dp", "tm", None), P(), P(), P(), P())
    return jax.shard_map(
        on_device, mesh=mesh, in_specs=in_specs, out_specs=out_specs, check_vma=False
    )
```

```python
import jax
import jax.numpy as jnp
from jax import lax
from jax.sharding import PartitionSpec as P

KPRE = 7
UPSAMPLE_FACTOR = 8
DILATION_SIZE = 3


def with_halo(block, sides, width):
    for axis, dim in sides:
        count = lax.axis_size(axis)
        forward = [(i, i + 1) for i in range(count - 1)]
        backward = [(target, source) for source, target in forward]
        low = lax.ppermute(
            lax.slice_in_dim(block, block.shape[dim] - width, None, axis=dim), axis, forward
        )
        high = lax.ppermute(lax.slice_in_dim(block, 0, width, axis=dim), axis, backward)
        block = jnp.concatenate([low, block, high], axis=dim)
    return block


def leaky(value):
    return jnp.where(value > 0, value, 0.1 * value)


def negative_slope(value):
    return jnp.where(value > 0, 1.0, 0.1).astype(jnp.float32)


def contract_rows(left, right):
    return lax.dot_general(
        left, right, (((0,), (0,)), ((), ())), preferred_element_type=jnp.float32
    )


def contract_cols(left, right):
    return lax.dot_general(
        left, right, (((1,), (1,)), ((), ())), preferred_element_type=jnp.float32
    )


def local_pass(
    mel_ext,
    gradient_value,
    first_frame0,
    total,
    w_pre,
    b_pre,
    ups_forward,
    ups_backward,
    upsample_bias,
    w_res,
    b_res,
):
    mel_bins = mel_ext.shape[1]
    kpre = w_pre.shape[0] // mel_bins
    edge = kpre // 2 + 1
    frame_count = mel_ext.shape[0] - 2 * edge
    window_width = upsample_bias.shape[0]
    residual_kernel = w_res.shape[0] // window_width
    patches = jnp.concatenate([mel_ext[i : i + frame_count + 2] for i in range(kpre)], axis=1)
    pre = jnp.dot(patches, w_pre, preferred_element_type=jnp.float32) + b_pre
    frame_idx = first_frame0 - 1 + jnp.arange(frame_count + 2, dtype=jnp.int32)
    inside_f = ((frame_idx >= 0) & (frame_idx < total))[:, None]
    act = jnp.where(inside_f, leaky(pre), 0.0).astype(jnp.bfloat16)
    taps = ups_forward(act).reshape(frame_count + 2, 2 * UPSAMPLE_FACTOR, window_width)
    upper_output = taps[1:, :UPSAMPLE_FACTOR] + taps[:-1, UPSAMPLE_FACTOR:]
    sample_count = UPSAMPLE_FACTOR * frame_count
    start_offset = UPSAMPLE_FACTOR // 2 - DILATION_SIZE
    waveform = (
        upper_output.reshape(UPSAMPLE_FACTOR * (frame_count + 1), window_width)[
            start_offset : start_offset + sample_count + 2 * DILATION_SIZE
        ]
        + upsample_bias
    )
    step_index = (
        UPSAMPLE_FACTOR * first_frame0
        - DILATION_SIZE
        + jnp.arange(sample_count + 2 * DILATION_SIZE, dtype=jnp.int32)
    )
    inside_samples = ((step_index >= 0) & (step_index < UPSAMPLE_FACTOR * total))[:, None]
    hidden_state = jnp.where(inside_samples, leaky(waveform), 0.0).astype(jnp.bfloat16)
    column_block = jnp.concatenate(
        [
            hidden_state[kernel_index * DILATION_SIZE : kernel_index * DILATION_SIZE + sample_count]
            for kernel_index in range(residual_kernel)
        ],
        axis=1,
    )
    convolve_fn = jnp.dot(column_block, w_res, preferred_element_type=jnp.float32) + b_res
    output_rows = (waveform[DILATION_SIZE : DILATION_SIZE + sample_count] + convolve_fn).astype(
        jnp.bfloat16
    )
    g_wres = contract_rows(column_block, gradient_value)
    g_bres = jnp.sum(gradient_value.astype(jnp.float32), axis=0)
    backward_pass = contract_cols(gradient_value, w_res)
    hidden_gradient = jnp.zeros((sample_count + 2 * DILATION_SIZE, window_width), jnp.float32)
    for kernel_index in range(residual_kernel):
        hidden_gradient = hidden_gradient + jnp.pad(
            backward_pass[:, kernel_index * window_width : (kernel_index + 1) * window_width],
            (
                (
                    kernel_index * DILATION_SIZE,
                    (residual_kernel - 1 - kernel_index) * DILATION_SIZE,
                ),
                (0, 0),
            ),
        )
    waveform_gradient = jnp.where(
        inside_samples, hidden_gradient * negative_slope(waveform), 0.0
    ) + jnp.pad(gradient_value.astype(jnp.float32), ((DILATION_SIZE, DILATION_SIZE), (0, 0)))
    waveform_gradient = waveform_gradient.astype(jnp.bfloat16)
    d_upper = jnp.pad(waveform_gradient, ((start_offset, start_offset), (0, 0))).reshape(
        frame_count + 1, UPSAMPLE_FACTOR, window_width
    )
    zero_row = jnp.zeros((1, UPSAMPLE_FACTOR, window_width), jnp.bfloat16)
    d_taps = jnp.concatenate(
        [
            jnp.concatenate([zero_row, d_upper], axis=0),
            jnp.concatenate([d_upper, zero_row], axis=0),
        ],
        axis=1,
    )
    d_act = ups_backward(d_taps.reshape(frame_count + 2, 2 * UPSAMPLE_FACTOR * window_width))
    d_pre = jnp.where(inside_f, d_act * negative_slope(pre), 0.0).astype(jnp.bfloat16)
    g_wpre = contract_rows(patches, d_pre)
    g_bpre = jnp.sum(d_pre.astype(jnp.float32), axis=0)
    return (output_rows, (g_wpre, g_bpre, g_wres, g_bres))


def butterfly_psum(parts):
    dp_size = lax.axis_size("dp")
    tm_size = lax.axis_size("tm")
    axes = ("dp", "tm")
    later = [("tm", 1 << k) for k in range(tm_size.bit_length() - 1)]
    later += [("dp", 1 << k) for k in range(1, dp_size.bit_length() - 1)]
    swapped = list(later)
    for i in range(0, len(swapped) - 1, 2):
        swapped[i], swapped[i + 1] = swapped[i + 1], swapped[i]
    sizes = {"dp": dp_size, "tm": tm_size}

    def linear(idx):
        return idx["dp"] * tm_size + idx["tm"]

    def pairs(choice):
        out = []
        for d in range(dp_size):
            for t in range(tm_size):
                idx = {"dp": d, "tm": t}
                axis, bit = choice(d % 2)
                other = dict(idx)
                other[axis] = idx[axis] ^ bit
                out.append((linear(idx), linear(other)))
        return out

    core = lax.axis_index("dp") % 2
    position = {"dp": lax.axis_index("dp"), "tm": lax.axis_index("tm")}

    def upper_of(step):
        a0, b0 = later[step]
        a1, b1 = swapped[step]
        return jnp.where(
            core == 0, (position[a0] // b0) % 2, (position[a1] // b1) % 2
        )

    flat = jnp.concatenate([p.reshape(-1) for p in parts])
    unit = 8 * 128 * dp_size * tm_size
    padded = -(-flat.shape[0] // unit) * unit
    x = jnp.pad(flat, (0, padded - flat.shape[0])).reshape(padded // 128, 128)
    halving = [None] + list(range(len(later) - 1))
    for step in halving:
        half = x.shape[0] // 2
        if step is None:
            upper = core
            perm = [(i, i ^ tm_size) for i in range(dp_size * tm_size)]
        else:
            upper = upper_of(step)
            perm = pairs(lambda c, s=step: (later if c == 0 else swapped)[s])
        send = lax.dynamic_slice_in_dim(x, (1 - upper) * half, half)
        keep = lax.dynamic_slice_in_dim(x, upper * half, half)
        x = keep + lax.ppermute(send, axes, perm)
    if later:
        last = len(later) - 1
        perm = pairs(lambda c: (later if c == 0 else swapped)[last])
        x = x + lax.ppermute(x, axes, perm)
    for step in reversed(halving):
        rows = x.shape[0]
        if step is None:
            upper = core
            perm = [(i, i ^ tm_size) for i in range(dp_size * tm_size)]
        else:
            upper = upper_of(step)
            perm = pairs(lambda c, s=step: (later if c == 0 else swapped)[s])
        recv = lax.ppermute(x, axes, perm)
        x = jnp.where(
            upper == 0, jnp.concatenate([x, recv]), jnp.concatenate([recv, x])
        )
    flat = x.reshape(-1)
    out, at = [], 0
    for p in parts:
        out.append(flat[at : at + p.size].reshape(p.shape))
        at += p.size
    return tuple(out)

def ups_functions(w_ups):
    dp_size = lax.axis_size("dp")
    if lax.axis_size("tm") != 2 or dp_size % 2:
        whole = lax.all_gather(w_ups, "tm", axis=0, tiled=True)
        return (
            lambda act: jnp.dot(act, whole, preferred_element_type=jnp.float32),
            lambda d_taps: contract_cols(d_taps, whole),
        )
    rows, width = w_ups.shape
    cols = width // 2
    core = lax.axis_index("dp") % 2
    tm = lax.axis_index("tm")
    mine = jnp.where(core == 0, w_ups[:, :cols], w_ups[:, cols:])
    got = lax.ppermute(mine, "tm", [(0, 1), (1, 0)])
    partner = lax.ppermute(got, "dp", [(i, i ^ 1) for i in range(dp_size)])
    low = jnp.where(core == 0, got, partner)
    high = jnp.where(core == 0, partner, got)

    def forward(act):
        own_act = lax.dynamic_slice_in_dim(act, tm * rows, rows, axis=1)
        other_act = lax.dynamic_slice_in_dim(act, (1 - tm) * rows, rows, axis=1)
        own = jnp.dot(own_act, w_ups, preferred_element_type=jnp.float32)
        other = jnp.concatenate(
            [
                jnp.dot(other_act, low, preferred_element_type=jnp.float32),
                jnp.dot(other_act, high, preferred_element_type=jnp.float32),
            ],
            axis=1,
        )
        return own + other

    def backward(d_taps):
        own = contract_cols(d_taps, w_ups)
        other = contract_cols(d_taps[:, :cols], low) + contract_cols(d_taps[:, cols:], high)
        return jnp.where(
            tm == 0, jnp.concatenate([own, other], axis=1), jnp.concatenate([other, own], axis=1)
        )

    return forward, backward


def on_device(
    src_mel, owner, dst_pos, keep, cotangent, w_pre, b_pre, w_ups, upsample_bias, w_res, b_res
):
    owners_count = lax.axis_size("dp")
    seg_rows = src_mel[0]
    seg_count = seg_rows.shape[0]
    mel_bins = w_pre.shape[0] // KPRE
    pick = jnp.arange(owners_count, dtype=jnp.int32)[:, None] == owner[0][None, :]
    seg_width = seg_rows.shape[1]
    header = jnp.stack([dst_pos[0] + 1, keep[0]], axis=1).astype(jnp.bfloat16)
    seg_ext = jnp.concatenate([seg_rows, header], axis=1)
    outgoing = jnp.dot(
        pick.astype(jnp.bfloat16), seg_ext, preferred_element_type=jnp.float32
    ).astype(jnp.bfloat16)
    arrived = lax.all_to_all(outgoing, "dp", split_axis=0, concat_axis=0, tiled=True)
    slot_code = arrived[:, seg_width].astype(jnp.int32)
    keep_code = arrived[:, seg_width + 1].astype(jnp.int32)
    place = (slot_code - 1)[:, None] == jnp.arange(seg_count, dtype=jnp.int32)[None, :]
    mel_segs = contract_rows(place.astype(jnp.bfloat16), arrived[:, :seg_width]).astype(
        jnp.bfloat16
    )
    keep_segs = jnp.sum(jnp.where(place, keep_code[:, None], 0), axis=0)
    mel = mel_segs.reshape(seg_count * (mel_segs.shape[1] // mel_bins), mel_bins)
    frame_count = mel.shape[0]
    mel_ext = with_halo(mel, (("tm", 0),), KPRE // 2 + 1)
    first_frame0 = lax.axis_index("tm") * frame_count
    total = lax.axis_size("tm") * frame_count
    cot = cotangent[0]
    marks = jnp.repeat(keep_segs, cot.shape[0] // seg_count)
    gradient_value = jnp.where(marks[:, None] > 0, cot, jnp.zeros_like(cot))
    ups_forward, ups_backward = ups_functions(w_ups)

    output_rows, grads = local_pass(
        mel_ext,
        gradient_value,
        first_frame0,
        total,
        w_pre,
        b_pre,
        ups_forward,
        ups_backward,
        upsample_bias,
        w_res,
        b_res,
    )
    summed = butterfly_psum(grads)
    return (output_rows[None], summed[0], summed[1], summed[2], summed[3])


def solution(mesh):
    in_specs = (
        P("tm", "dp", None),
        P("tm", "dp"),
        P("tm", "dp"),
        P("tm", "dp"),
        P("dp", "tm", None),
        P(),
        P(),
        P("tm", None),
        P(),
        P(),
        P(),
    )
    out_specs = (P("dp", "tm", None), P(), P(), P(), P())
    return jax.shard_map(
        on_device, mesh=mesh, in_specs=in_specs, out_specs=out_specs, check_vma=False
    )
```

```python
import jax
import jax.numpy as jnp
from jax import lax
from jax.sharding import PartitionSpec as P

KPRE = 7
UPSAMPLE_FACTOR = 8
DILATION_SIZE = 3


def with_halo(block, sides, width):
    for axis, dim in sides:
        count = lax.axis_size(axis)
        forward = [(i, i + 1) for i in range(count - 1)]
        backward = [(target, source) for source, target in forward]
        low = lax.ppermute(
            lax.slice_in_dim(block, block.shape[dim] - width, None, axis=dim), axis, forward
        )
        high = lax.ppermute(lax.slice_in_dim(block, 0, width, axis=dim), axis, backward)
        block = jnp.concatenate([low, block, high], axis=dim)
    return block


def leaky(value):
    return jnp.where(value > 0, value, 0.1 * value)


def negative_slope(value):
    return jnp.where(value > 0, 1.0, 0.1).astype(jnp.float32)


def contract_rows(left, right):
    return lax.dot_general(
        left, right, (((0,), (0,)), ((), ())), preferred_element_type=jnp.float32
    )


def contract_cols(left, right):
    return lax.dot_general(
        left, right, (((1,), (1,)), ((), ())), preferred_element_type=jnp.float32
    )


def local_pass(
    mel_ext,
    gradient_value,
    first_frame0,
    total,
    w_pre,
    b_pre,
    ups_forward,
    ups_backward,
    upsample_bias,
    w_res,
    b_res,
):
    mel_bins = mel_ext.shape[1]
    kpre = w_pre.shape[0] // mel_bins
    edge = kpre // 2 + 1
    frame_count = mel_ext.shape[0] - 2 * edge
    window_width = upsample_bias.shape[0]
    residual_kernel = w_res.shape[0] // window_width
    patches = jnp.concatenate([mel_ext[i : i + frame_count + 2] for i in range(kpre)], axis=1)
    pre = jnp.dot(patches, w_pre, preferred_element_type=jnp.float32) + b_pre
    frame_idx = first_frame0 - 1 + jnp.arange(frame_count + 2, dtype=jnp.int32)
    inside_f = ((frame_idx >= 0) & (frame_idx < total))[:, None]
    act = jnp.where(inside_f, leaky(pre), 0.0).astype(jnp.bfloat16)
    taps = ups_forward(act).reshape(frame_count + 2, 2 * UPSAMPLE_FACTOR, window_width)
    upper_output = taps[1:, :UPSAMPLE_FACTOR] + taps[:-1, UPSAMPLE_FACTOR:]
    sample_count = UPSAMPLE_FACTOR * frame_count
    start_offset = UPSAMPLE_FACTOR // 2 - DILATION_SIZE
    waveform = (
        upper_output.reshape(UPSAMPLE_FACTOR * (frame_count + 1), window_width)[
            start_offset : start_offset + sample_count + 2 * DILATION_SIZE
        ]
        + upsample_bias
    )
    step_index = (
        UPSAMPLE_FACTOR * first_frame0
        - DILATION_SIZE
        + jnp.arange(sample_count + 2 * DILATION_SIZE, dtype=jnp.int32)
    )
    inside_samples = ((step_index >= 0) & (step_index < UPSAMPLE_FACTOR * total))[:, None]
    hidden_state = jnp.where(inside_samples, leaky(waveform), 0.0).astype(jnp.bfloat16)
    column_block = jnp.concatenate(
        [
            hidden_state[kernel_index * DILATION_SIZE : kernel_index * DILATION_SIZE + sample_count]
            for kernel_index in range(residual_kernel)
        ],
        axis=1,
    )
    convolve_fn = jnp.dot(column_block, w_res, preferred_element_type=jnp.float32) + b_res
    output_rows = (waveform[DILATION_SIZE : DILATION_SIZE + sample_count] + convolve_fn).astype(
        jnp.bfloat16
    )
    g_wres = contract_rows(column_block, gradient_value)
    g_bres = jnp.sum(gradient_value.astype(jnp.float32), axis=0)
    backward_pass = contract_cols(gradient_value, w_res)
    hidden_gradient = jnp.zeros((sample_count + 2 * DILATION_SIZE, window_width), jnp.float32)
    for kernel_index in range(residual_kernel):
        hidden_gradient = hidden_gradient + jnp.pad(
            backward_pass[:, kernel_index * window_width : (kernel_index + 1) * window_width],
            (
                (
                    kernel_index * DILATION_SIZE,
                    (residual_kernel - 1 - kernel_index) * DILATION_SIZE,
                ),
                (0, 0),
            ),
        )
    waveform_gradient = jnp.where(
        inside_samples, hidden_gradient * negative_slope(waveform), 0.0
    ) + jnp.pad(gradient_value.astype(jnp.float32), ((DILATION_SIZE, DILATION_SIZE), (0, 0)))
    waveform_gradient = waveform_gradient.astype(jnp.bfloat16)
    d_upper = jnp.pad(waveform_gradient, ((start_offset, start_offset), (0, 0))).reshape(
        frame_count + 1, UPSAMPLE_FACTOR, window_width
    )
    zero_row = jnp.zeros((1, UPSAMPLE_FACTOR, window_width), jnp.bfloat16)
    d_taps = jnp.concatenate(
        [
            jnp.concatenate([zero_row, d_upper], axis=0),
            jnp.concatenate([d_upper, zero_row], axis=0),
        ],
        axis=1,
    )
    d_act = ups_backward(d_taps.reshape(frame_count + 2, 2 * UPSAMPLE_FACTOR * window_width))
    d_pre = jnp.where(inside_f, d_act * negative_slope(pre), 0.0).astype(jnp.bfloat16)
    g_wpre = contract_rows(patches, d_pre)
    g_bpre = jnp.sum(d_pre.astype(jnp.float32), axis=0)
    return (output_rows, (g_wpre, g_bpre, g_wres, g_bres))


def butterfly_psum(parts):
    dp_size = lax.axis_size("dp")
    tm_size = lax.axis_size("tm")
    axes = ("dp", "tm")
    levels = [("tm", 1 << k) for k in range(tm_size.bit_length() - 1)]
    levels += [("dp", 1 << k) for k in range(1, dp_size.bit_length() - 1)]
    groups = [levels[i : i + 2] for i in range(0, len(levels), 2)]
    orders = (groups, groups[::-1])
    count = dp_size * tm_size

    def perm_of(step, offset):
        out = []
        for d in range(dp_size):
            for t in range(tm_size):
                idx = {"dp": d, "tm": t}
                for j, (axis, bit) in enumerate(orders[d % 2][step]):
                    if (offset >> j) & 1:
                        idx[axis] = idx[axis] ^ bit
                out.append((d * tm_size + t, idx["dp"] * tm_size + idx["tm"]))
        return out

    core = lax.axis_index("dp") % 2
    position = {"dp": lax.axis_index("dp"), "tm": lax.axis_index("tm")}

    def slot_of(step):
        def one(group):
            return sum(((position[a] // b) % 2) << j for j, (a, b) in enumerate(group))

        return jnp.where(core == 0, one(orders[0][step]), one(orders[1][step]))

    flat = jnp.concatenate([p.reshape(-1) for p in parts])
    unit = 8 * 128 * count
    padded = -(-flat.shape[0] // unit) * unit
    x = jnp.pad(flat, (0, padded - flat.shape[0])).reshape(padded // 128, 128)
    core_perm = [(i, i ^ tm_size) for i in range(count)]
    half = x.shape[0] // 2
    send = lax.dynamic_slice_in_dim(x, (1 - core) * half, half)
    x = lax.dynamic_slice_in_dim(x, core * half, half) + lax.ppermute(send, axes, core_perm)
    for step in range(len(groups)):
        radix = 1 << len(groups[step])
        piece = x.shape[0] // radix
        slot = slot_of(step)
        total = lax.dynamic_slice_in_dim(x, slot * piece, piece)
        for offset in range(1, radix):
            send = lax.dynamic_slice_in_dim(x, (slot ^ offset) * piece, piece)
            total = total + lax.ppermute(send, axes, perm_of(step, offset))
        x = total
    for step in reversed(range(len(groups))):
        radix = 1 << len(groups[step])
        slot = slot_of(step)
        got = [x] + [lax.ppermute(x, axes, perm_of(step, o)) for o in range(1, radix)]
        pieces = []
        for q in range(radix):
            source = slot ^ q
            chosen = got[radix - 1]
            for o in range(radix - 2, -1, -1):
                chosen = jnp.where(source == o, got[o], chosen)
            pieces.append(chosen)
        x = jnp.concatenate(pieces)
    recv = lax.ppermute(x, axes, core_perm)
    x = jnp.where(core == 0, jnp.concatenate([x, recv]), jnp.concatenate([recv, x]))
    flat = x.reshape(-1)
    out, at = [], 0
    for p in parts:
        out.append(flat[at : at + p.size].reshape(p.shape))
        at += p.size
    return tuple(out)

def ups_functions(w_ups):
    dp_size = lax.axis_size("dp")
    if lax.axis_size("tm") != 2 or dp_size % 2:
        whole = lax.all_gather(w_ups, "tm", axis=0, tiled=True)
        return (
            lambda act: jnp.dot(act, whole, preferred_element_type=jnp.float32),
            lambda d_taps: contract_cols(d_taps, whole),
        )
    rows, width = w_ups.shape
    cols = width // 2
    core = lax.axis_index("dp") % 2
    tm = lax.axis_index("tm")
    mine = jnp.where(core == 0, w_ups[:, :cols], w_ups[:, cols:])
    got = lax.ppermute(mine, "tm", [(0, 1), (1, 0)])
    partner = lax.ppermute(got, "dp", [(i, i ^ 1) for i in range(dp_size)])
    low = jnp.where(core == 0, got, partner)
    high = jnp.where(core == 0, partner, got)

    def forward(act):
        own_act = lax.dynamic_slice_in_dim(act, tm * rows, rows, axis=1)
        other_act = lax.dynamic_slice_in_dim(act, (1 - tm) * rows, rows, axis=1)
        own = jnp.dot(own_act, w_ups, preferred_element_type=jnp.float32)
        other = jnp.concatenate(
            [
                jnp.dot(other_act, low, preferred_element_type=jnp.float32),
                jnp.dot(other_act, high, preferred_element_type=jnp.float32),
            ],
            axis=1,
        )
        return own + other

    def backward(d_taps):
        own = contract_cols(d_taps, w_ups)
        other = contract_cols(d_taps[:, :cols], low) + contract_cols(d_taps[:, cols:], high)
        return jnp.where(
            tm == 0, jnp.concatenate([own, other], axis=1), jnp.concatenate([other, own], axis=1)
        )

    return forward, backward


def on_device(
    src_mel, owner, dst_pos, keep, cotangent, w_pre, b_pre, w_ups, upsample_bias, w_res, b_res
):
    owners_count = lax.axis_size("dp")
    seg_rows = src_mel[0]
    seg_count = seg_rows.shape[0]
    mel_bins = w_pre.shape[0] // KPRE
    pick = jnp.arange(owners_count, dtype=jnp.int32)[:, None] == owner[0][None, :]
    seg_width = seg_rows.shape[1]
    header = jnp.stack([dst_pos[0] + 1, keep[0]], axis=1).astype(jnp.bfloat16)
    seg_ext = jnp.concatenate([seg_rows, header], axis=1)
    outgoing = jnp.dot(
        pick.astype(jnp.bfloat16), seg_ext, preferred_element_type=jnp.float32
    ).astype(jnp.bfloat16)
    arrived = lax.all_to_all(outgoing, "dp", split_axis=0, concat_axis=0, tiled=True)
    slot_code = arrived[:, seg_width].astype(jnp.int32)
    keep_code = arrived[:, seg_width + 1].astype(jnp.int32)
    place = (slot_code - 1)[:, None] == jnp.arange(seg_count, dtype=jnp.int32)[None, :]
    mel_segs = contract_rows(place.astype(jnp.bfloat16), arrived[:, :seg_width]).astype(
        jnp.bfloat16
    )
    keep_segs = jnp.sum(jnp.where(place, keep_code[:, None], 0), axis=0)
    mel = mel_segs.reshape(seg_count * (mel_segs.shape[1] // mel_bins), mel_bins)
    frame_count = mel.shape[0]
    mel_ext = with_halo(mel, (("tm", 0),), KPRE // 2 + 1)
    first_frame0 = lax.axis_index("tm") * frame_count
    total = lax.axis_size("tm") * frame_count
    cot = cotangent[0]
    marks = jnp.repeat(keep_segs, cot.shape[0] // seg_count)
    gradient_value = jnp.where(marks[:, None] > 0, cot, jnp.zeros_like(cot))
    ups_forward, ups_backward = ups_functions(w_ups)

    output_rows, grads = local_pass(
        mel_ext,
        gradient_value,
        first_frame0,
        total,
        w_pre,
        b_pre,
        ups_forward,
        ups_backward,
        upsample_bias,
        w_res,
        b_res,
    )
    summed = butterfly_psum(grads)
    return (output_rows[None], summed[0], summed[1], summed[2], summed[3])


def solution(mesh):
    in_specs = (
        P("tm", "dp", None),
        P("tm", "dp"),
        P("tm", "dp"),
        P("tm", "dp"),
        P("dp", "tm", None),
        P(),
        P(),
        P("tm", None),
        P(),
        P(),
        P(),
    )
    out_specs = (P("dp", "tm", None), P(), P(), P(), P())
    return jax.shard_map(
        on_device, mesh=mesh, in_specs=in_specs, out_specs=out_specs, check_vma=False
    )
```

```python
import jax
import jax.numpy as jnp
from jax import lax
from jax.sharding import PartitionSpec as P

KPRE = 7
UPSAMPLE_FACTOR = 8
DILATION_SIZE = 3


def with_halo(block, sides, width):
    for axis, dim in sides:
        count = lax.axis_size(axis)
        forward = [(i, i + 1) for i in range(count - 1)]
        backward = [(target, source) for source, target in forward]
        low = lax.ppermute(
            lax.slice_in_dim(block, block.shape[dim] - width, None, axis=dim), axis, forward
        )
        high = lax.ppermute(lax.slice_in_dim(block, 0, width, axis=dim), axis, backward)
        block = jnp.concatenate([low, block, high], axis=dim)
    return block


def leaky(value):
    return jnp.where(value > 0, value, 0.1 * value)


def negative_slope(value):
    return jnp.where(value > 0, 1.0, 0.1).astype(jnp.float32)


def contract_rows(left, right):
    return lax.dot_general(
        left, right, (((0,), (0,)), ((), ())), preferred_element_type=jnp.float32
    )


def contract_cols(left, right):
    return lax.dot_general(
        left, right, (((1,), (1,)), ((), ())), preferred_element_type=jnp.float32
    )


def local_pass(
    mel_ext,
    gradient_value,
    first_frame0,
    total,
    w_pre,
    b_pre,
    ups_forward,
    ups_backward,
    upsample_bias,
    w_res,
    b_res,
):
    mel_bins = mel_ext.shape[1]
    kpre = w_pre.shape[0] // mel_bins
    edge = kpre // 2 + 1
    frame_count = mel_ext.shape[0] - 2 * edge
    window_width = upsample_bias.shape[0]
    residual_kernel = w_res.shape[0] // window_width
    patches = jnp.concatenate([mel_ext[i : i + frame_count + 2] for i in range(kpre)], axis=1)
    pre = jnp.dot(patches, w_pre, preferred_element_type=jnp.float32) + b_pre
    frame_idx = first_frame0 - 1 + jnp.arange(frame_count + 2, dtype=jnp.int32)
    inside_f = ((frame_idx >= 0) & (frame_idx < total))[:, None]
    act = jnp.where(inside_f, leaky(pre), 0.0).astype(jnp.bfloat16)
    taps = ups_forward(act).reshape(frame_count + 2, 2 * UPSAMPLE_FACTOR, window_width)
    upper_output = taps[1:, :UPSAMPLE_FACTOR] + taps[:-1, UPSAMPLE_FACTOR:]
    sample_count = UPSAMPLE_FACTOR * frame_count
    start_offset = UPSAMPLE_FACTOR // 2 - DILATION_SIZE
    waveform = (
        upper_output.reshape(UPSAMPLE_FACTOR * (frame_count + 1), window_width)[
            start_offset : start_offset + sample_count + 2 * DILATION_SIZE
        ]
        + upsample_bias
    )
    step_index = (
        UPSAMPLE_FACTOR * first_frame0
        - DILATION_SIZE
        + jnp.arange(sample_count + 2 * DILATION_SIZE, dtype=jnp.int32)
    )
    inside_samples = ((step_index >= 0) & (step_index < UPSAMPLE_FACTOR * total))[:, None]
    hidden_state = jnp.where(inside_samples, leaky(waveform), 0.0).astype(jnp.bfloat16)
    column_block = jnp.concatenate(
        [
            hidden_state[kernel_index * DILATION_SIZE : kernel_index * DILATION_SIZE + sample_count]
            for kernel_index in range(residual_kernel)
        ],
        axis=1,
    )
    convolve_fn = jnp.dot(column_block, w_res, preferred_element_type=jnp.float32) + b_res
    output_rows = (waveform[DILATION_SIZE : DILATION_SIZE + sample_count] + convolve_fn).astype(
        jnp.bfloat16
    )
    g_wres = contract_rows(column_block, gradient_value)
    g_bres = jnp.sum(gradient_value.astype(jnp.float32), axis=0)
    backward_pass = contract_cols(gradient_value, w_res)
    hidden_gradient = jnp.zeros((sample_count + 2 * DILATION_SIZE, window_width), jnp.float32)
    for kernel_index in range(residual_kernel):
        hidden_gradient = hidden_gradient + jnp.pad(
            backward_pass[:, kernel_index * window_width : (kernel_index + 1) * window_width],
            (
                (
                    kernel_index * DILATION_SIZE,
                    (residual_kernel - 1 - kernel_index) * DILATION_SIZE,
                ),
                (0, 0),
            ),
        )
    waveform_gradient = jnp.where(
        inside_samples, hidden_gradient * negative_slope(waveform), 0.0
    ) + jnp.pad(gradient_value.astype(jnp.float32), ((DILATION_SIZE, DILATION_SIZE), (0, 0)))
    waveform_gradient = waveform_gradient.astype(jnp.bfloat16)
    d_upper = jnp.pad(waveform_gradient, ((start_offset, start_offset), (0, 0))).reshape(
        frame_count + 1, UPSAMPLE_FACTOR, window_width
    )
    zero_row = jnp.zeros((1, UPSAMPLE_FACTOR, window_width), jnp.bfloat16)
    d_taps = jnp.concatenate(
        [
            jnp.concatenate([zero_row, d_upper], axis=0),
            jnp.concatenate([d_upper, zero_row], axis=0),
        ],
        axis=1,
    )
    d_act = ups_backward(d_taps.reshape(frame_count + 2, 2 * UPSAMPLE_FACTOR * window_width))
    d_pre = jnp.where(inside_f, d_act * negative_slope(pre), 0.0).astype(jnp.bfloat16)
    g_wpre = contract_rows(patches, d_pre)
    g_bpre = jnp.sum(d_pre.astype(jnp.float32), axis=0)
    return (output_rows, (g_wpre, g_bpre, g_wres, g_bres))


def butterfly_psum(parts):
    dp_size = lax.axis_size("dp")
    tm_size = lax.axis_size("tm")
    axes = ("dp", "tm")
    levels = [("tm", 1 << k) for k in range(tm_size.bit_length() - 1)]
    levels += [("dp", 1 << k) for k in range(1, dp_size.bit_length() - 1)]
    groups = [levels[i : i + 2] for i in range(0, len(levels), 2)]
    orders = (groups, groups[::-1])
    count = dp_size * tm_size

    def perm_of(step, offset):
        out = []
        for d in range(dp_size):
            for t in range(tm_size):
                idx = {"dp": d, "tm": t}
                for j, (axis, bit) in enumerate(orders[d % 2][step]):
                    if (offset >> j) & 1:
                        idx[axis] = idx[axis] ^ bit
                out.append((d * tm_size + t, idx["dp"] * tm_size + idx["tm"]))
        return out

    core = lax.axis_index("dp") % 2
    position = {"dp": lax.axis_index("dp"), "tm": lax.axis_index("tm")}

    def slot_of(step):
        def one(group):
            return sum(((position[a] // b) % 2) << j for j, (a, b) in enumerate(group))

        return jnp.where(core == 0, one(orders[0][step]), one(orders[1][step]))

    flat = jnp.concatenate([p.reshape(-1) for p in parts])
    unit = 8 * 128 * count
    padded = -(-flat.shape[0] // unit) * unit
    x = jnp.pad(flat, (0, padded - flat.shape[0])).reshape(padded // 128, 128)
    core_perm = [(i, i ^ tm_size) for i in range(count)]
    half = x.shape[0] // 2
    send = lax.dynamic_slice_in_dim(x, (1 - core) * half, half)
    x = lax.dynamic_slice_in_dim(x, core * half, half) + lax.ppermute(send, axes, core_perm)
    for step in range(len(groups)):
        radix = 1 << len(groups[step])
        piece = x.shape[0] // radix
        slot = slot_of(step)
        total = lax.dynamic_slice_in_dim(x, slot * piece, piece)
        for offset in range(1, radix):
            send = lax.dynamic_slice_in_dim(x, (slot ^ offset) * piece, piece)
            total = total + lax.ppermute(send, axes, perm_of(step, offset))
        x = total
    for step in reversed(range(len(groups))):
        radix = 1 << len(groups[step])
        slot = slot_of(step)
        got = [x] + [lax.ppermute(x, axes, perm_of(step, o)) for o in range(1, radix)]
        pieces = []
        for q in range(radix):
            source = slot ^ q
            chosen = got[radix - 1]
            for o in range(radix - 2, -1, -1):
                chosen = jnp.where(source == o, got[o], chosen)
            pieces.append(chosen)
        x = jnp.concatenate(pieces)
    recv = lax.ppermute(x, axes, core_perm)
    x = jnp.where(core == 0, jnp.concatenate([x, recv]), jnp.concatenate([recv, x]))
    flat = x.reshape(-1)
    out, at = [], 0
    for p in parts:
        out.append(flat[at : at + p.size].reshape(p.shape))
        at += p.size
    return tuple(out)

def ups_functions(w_ups):
    dp_size = lax.axis_size("dp")
    if lax.axis_size("tm") != 2 or dp_size % 2:
        whole = lax.all_gather(w_ups, "tm", axis=0, tiled=True)
        return (
            lambda act: jnp.dot(act, whole, preferred_element_type=jnp.float32),
            lambda d_taps: contract_cols(d_taps, whole),
        )
    rows, width = w_ups.shape
    cols = width // 2
    core = lax.axis_index("dp") % 2
    tm = lax.axis_index("tm")
    mine = jnp.where(core == 0, w_ups[:, :cols], w_ups[:, cols:])
    got = lax.ppermute(mine, "tm", [(0, 1), (1, 0)])
    partner = lax.ppermute(got, "dp", [(i, i ^ 1) for i in range(dp_size)])
    low = jnp.where(core == 0, got, partner)
    high = jnp.where(core == 0, partner, got)

    def forward(act):
        own_act = lax.dynamic_slice_in_dim(act, tm * rows, rows, axis=1)
        other_act = lax.dynamic_slice_in_dim(act, (1 - tm) * rows, rows, axis=1)
        own = jnp.dot(own_act, w_ups, preferred_element_type=jnp.float32)
        other = jnp.concatenate(
            [
                jnp.dot(other_act, low, preferred_element_type=jnp.float32),
                jnp.dot(other_act, high, preferred_element_type=jnp.float32),
            ],
            axis=1,
        )
        return own + other

    def backward(d_taps):
        own = contract_cols(d_taps, w_ups)
        other = contract_cols(d_taps[:, :cols], low) + contract_cols(d_taps[:, cols:], high)
        return jnp.where(
            tm == 0, jnp.concatenate([own, other], axis=1), jnp.concatenate([other, own], axis=1)
        )

    return forward, backward


def on_device(
    src_mel, owner, dst_pos, keep, cotangent, w_pre, b_pre, w_ups, upsample_bias, w_res, b_res
):
    seg_rows = src_mel[0]
    seg_count = seg_rows.shape[0]
    mel_bins = w_pre.shape[0] // KPRE
    seg_width = seg_rows.shape[1]
    header = jnp.stack([dst_pos[0] + 1, keep[0], owner[0]], axis=1).astype(jnp.bfloat16)
    seg_ext = jnp.concatenate([seg_rows, header], axis=1)
    gathered = lax.all_gather(seg_ext, "dp", axis=0, tiled=True)
    slot_code = gathered[:, seg_width].astype(jnp.int32)
    keep_code = gathered[:, seg_width + 1].astype(jnp.int32)
    mine = gathered[:, seg_width + 2].astype(jnp.int32) == lax.axis_index("dp")
    place = mine[:, None] & (
        (slot_code - 1)[:, None] == jnp.arange(seg_count, dtype=jnp.int32)[None, :]
    )
    mel_segs = contract_rows(place.astype(jnp.bfloat16), gathered[:, :seg_width]).astype(
        jnp.bfloat16
    )
    keep_segs = jnp.sum(jnp.where(place, keep_code[:, None], 0), axis=0)
    mel = mel_segs.reshape(seg_count * (mel_segs.shape[1] // mel_bins), mel_bins)
    frame_count = mel.shape[0]
    mel_ext = with_halo(mel, (("tm", 0),), KPRE // 2 + 1)
    first_frame0 = lax.axis_index("tm") * frame_count
    total = lax.axis_size("tm") * frame_count
    cot = cotangent[0]
    marks = jnp.repeat(keep_segs, cot.shape[0] // seg_count)
    gradient_value = jnp.where(marks[:, None] > 0, cot, jnp.zeros_like(cot))
    ups_forward, ups_backward = ups_functions(w_ups)

    output_rows, grads = local_pass(
        mel_ext,
        gradient_value,
        first_frame0,
        total,
        w_pre,
        b_pre,
        ups_forward,
        ups_backward,
        upsample_bias,
        w_res,
        b_res,
    )
    summed = butterfly_psum(grads)
    return (output_rows[None], summed[0], summed[1], summed[2], summed[3])


def solution(mesh):
    in_specs = (
        P("tm", "dp", None),
        P("tm", "dp"),
        P("tm", "dp"),
        P("tm", "dp"),
        P("dp", "tm", None),
        P(),
        P(),
        P("tm", None),
        P(),
        P(),
        P(),
    )
    out_specs = (P("dp", "tm", None), P(), P(), P(), P())
    return jax.shard_map(
        on_device, mesh=mesh, in_specs=in_specs, out_specs=out_specs, check_vma=False
    )
```

```python
import jax
import jax.numpy as jnp
from jax import lax
from jax.sharding import PartitionSpec as P

KPRE = 7
UPSAMPLE_FACTOR = 8
DILATION_SIZE = 3


def with_halo(block, sides, width):
    for axis, dim in sides:
        count = lax.axis_size(axis)
        forward = [(i, i + 1) for i in range(count - 1)]
        backward = [(target, source) for source, target in forward]
        low = lax.ppermute(
            lax.slice_in_dim(block, block.shape[dim] - width, None, axis=dim), axis, forward
        )
        high = lax.ppermute(lax.slice_in_dim(block, 0, width, axis=dim), axis, backward)
        block = jnp.concatenate([low, block, high], axis=dim)
    return block


def leaky(value):
    return jnp.where(value > 0, value, 0.1 * value)


def negative_slope(value):
    return jnp.where(value > 0, 1.0, 0.1).astype(jnp.float32)


def contract_rows(left, right):
    return lax.dot_general(
        left, right, (((0,), (0,)), ((), ())), preferred_element_type=jnp.float32
    )


def contract_cols(left, right):
    return lax.dot_general(
        left, right, (((1,), (1,)), ((), ())), preferred_element_type=jnp.float32
    )


def local_pass(
    mel_ext,
    gradient_value,
    first_frame0,
    total,
    w_pre,
    b_pre,
    ups_forward,
    ups_backward,
    upsample_bias,
    w_res,
    b_res,
):
    mel_bins = mel_ext.shape[1]
    kpre = w_pre.shape[0] // mel_bins
    edge = kpre // 2 + 1
    frame_count = mel_ext.shape[0] - 2 * edge
    window_width = upsample_bias.shape[0]
    residual_kernel = w_res.shape[0] // window_width
    patches = jnp.concatenate([mel_ext[i : i + frame_count + 2] for i in range(kpre)], axis=1)
    pre = jnp.dot(patches, w_pre, preferred_element_type=jnp.float32) + b_pre
    frame_idx = first_frame0 - 1 + jnp.arange(frame_count + 2, dtype=jnp.int32)
    inside_f = ((frame_idx >= 0) & (frame_idx < total))[:, None]
    act = jnp.where(inside_f, leaky(pre), 0.0).astype(jnp.bfloat16)
    taps = ups_forward(act).reshape(frame_count + 2, 2 * UPSAMPLE_FACTOR, window_width)
    upper_output = taps[1:, :UPSAMPLE_FACTOR] + taps[:-1, UPSAMPLE_FACTOR:]
    sample_count = UPSAMPLE_FACTOR * frame_count
    start_offset = UPSAMPLE_FACTOR // 2 - DILATION_SIZE
    waveform = (
        upper_output.reshape(UPSAMPLE_FACTOR * (frame_count + 1), window_width)[
            start_offset : start_offset + sample_count + 2 * DILATION_SIZE
        ]
        + upsample_bias
    )
    step_index = (
        UPSAMPLE_FACTOR * first_frame0
        - DILATION_SIZE
        + jnp.arange(sample_count + 2 * DILATION_SIZE, dtype=jnp.int32)
    )
    inside_samples = ((step_index >= 0) & (step_index < UPSAMPLE_FACTOR * total))[:, None]
    hidden_state = jnp.where(inside_samples, leaky(waveform), 0.0).astype(jnp.bfloat16)
    column_block = jnp.concatenate(
        [
            hidden_state[kernel_index * DILATION_SIZE : kernel_index * DILATION_SIZE + sample_count]
            for kernel_index in range(residual_kernel)
        ],
        axis=1,
    )
    convolve_fn = jnp.dot(column_block, w_res, preferred_element_type=jnp.float32) + b_res
    output_rows = (waveform[DILATION_SIZE : DILATION_SIZE + sample_count] + convolve_fn).astype(
        jnp.bfloat16
    )
    g_wres = contract_rows(column_block, gradient_value)
    g_bres = jnp.sum(gradient_value.astype(jnp.float32), axis=0)
    backward_pass = contract_cols(gradient_value, w_res)
    hidden_gradient = jnp.zeros((sample_count + 2 * DILATION_SIZE, window_width), jnp.float32)
    for kernel_index in range(residual_kernel):
        hidden_gradient = hidden_gradient + jnp.pad(
            backward_pass[:, kernel_index * window_width : (kernel_index + 1) * window_width],
            (
                (
                    kernel_index * DILATION_SIZE,
                    (residual_kernel - 1 - kernel_index) * DILATION_SIZE,
                ),
                (0, 0),
            ),
        )
    waveform_gradient = jnp.where(
        inside_samples, hidden_gradient * negative_slope(waveform), 0.0
    ) + jnp.pad(gradient_value.astype(jnp.float32), ((DILATION_SIZE, DILATION_SIZE), (0, 0)))
    waveform_gradient = waveform_gradient.astype(jnp.bfloat16)
    d_upper = jnp.pad(waveform_gradient, ((start_offset, start_offset), (0, 0))).reshape(
        frame_count + 1, UPSAMPLE_FACTOR, window_width
    )
    zero_row = jnp.zeros((1, UPSAMPLE_FACTOR, window_width), jnp.bfloat16)
    d_taps = jnp.concatenate(
        [
            jnp.concatenate([zero_row, d_upper], axis=0),
            jnp.concatenate([d_upper, zero_row], axis=0),
        ],
        axis=1,
    )
    d_act = ups_backward(d_taps.reshape(frame_count + 2, 2 * UPSAMPLE_FACTOR * window_width))
    d_pre = jnp.where(inside_f, d_act * negative_slope(pre), 0.0).astype(jnp.bfloat16)
    g_wpre = contract_rows(patches, d_pre)
    g_bpre = jnp.sum(d_pre.astype(jnp.float32), axis=0)
    return (output_rows, (g_wpre, g_bpre, g_wres, g_bres))


def butterfly_psum(parts):
    dp_size = lax.axis_size("dp")
    tm_size = lax.axis_size("tm")
    axes = ("dp", "tm")
    levels = [("tm", 1 << k) for k in range(tm_size.bit_length() - 1)]
    levels += [("dp", 1 << k) for k in range(1, dp_size.bit_length() - 1)]
    groups = [levels[i : i + 2] for i in range(0, len(levels), 2)]
    orders = (groups, groups[::-1])
    count = dp_size * tm_size

    def perm_of(step, offset):
        out = []
        for d in range(dp_size):
            for t in range(tm_size):
                idx = {"dp": d, "tm": t}
                for j, (axis, bit) in enumerate(orders[d % 2][step]):
                    if (offset >> j) & 1:
                        idx[axis] = idx[axis] ^ bit
                out.append((d * tm_size + t, idx["dp"] * tm_size + idx["tm"]))
        return out

    core = lax.axis_index("dp") % 2
    position = {"dp": lax.axis_index("dp"), "tm": lax.axis_index("tm")}

    def slot_of(step):
        def one(group):
            return sum(((position[a] // b) % 2) << j for j, (a, b) in enumerate(group))

        return jnp.where(core == 0, one(orders[0][step]), one(orders[1][step]))

    flat = jnp.concatenate([p.reshape(-1) for p in parts])
    unit = 8 * 128 * count
    padded = -(-flat.shape[0] // unit) * unit
    x = jnp.pad(flat, (0, padded - flat.shape[0])).reshape(padded // 128, 128)
    core_perm = [(i, i ^ tm_size) for i in range(count)]
    half = x.shape[0] // 2
    send = lax.dynamic_slice_in_dim(x, (1 - core) * half, half)
    x = lax.dynamic_slice_in_dim(x, core * half, half) + lax.ppermute(send, axes, core_perm)
    for step in range(len(groups)):
        radix = 1 << len(groups[step])
        piece = x.shape[0] // radix
        slot = slot_of(step)
        total = lax.dynamic_slice_in_dim(x, slot * piece, piece)
        for offset in range(1, radix):
            send = lax.dynamic_slice_in_dim(x, (slot ^ offset) * piece, piece)
            total = total + lax.ppermute(send, axes, perm_of(step, offset))
        x = total
    for step in reversed(range(len(groups))):
        radix = 1 << len(groups[step])
        slot = slot_of(step)
        got = [x] + [lax.ppermute(x, axes, perm_of(step, o)) for o in range(1, radix)]
        pieces = []
        for q in range(radix):
            source = slot ^ q
            chosen = got[radix - 1]
            for o in range(radix - 2, -1, -1):
                chosen = jnp.where(source == o, got[o], chosen)
            pieces.append(chosen)
        x = jnp.concatenate(pieces)
    recv = lax.ppermute(x, axes, core_perm)
    x = jnp.where(core == 0, jnp.concatenate([x, recv]), jnp.concatenate([recv, x]))
    flat = x.reshape(-1)
    out, at = [], 0
    for p in parts:
        out.append(flat[at : at + p.size].reshape(p.shape))
        at += p.size
    return tuple(out)

def ups_functions(w_ups):
    dp_size = lax.axis_size("dp")
    if lax.axis_size("tm") != 2 or dp_size % 2:
        whole = lax.all_gather(w_ups, "tm", axis=0, tiled=True)
        return (
            lambda act: jnp.dot(act, whole, preferred_element_type=jnp.float32),
            lambda d_taps: contract_cols(d_taps, whole),
        )
    rows, width = w_ups.shape
    cols = width // 2
    core = lax.axis_index("dp") % 2
    tm = lax.axis_index("tm")
    mine = jnp.where(core == 0, w_ups[:, :cols], w_ups[:, cols:])
    split = rows // 2
    got_parts = [
        lax.ppermute(mine[:split], "tm", [(0, 1), (1, 0)]),
        lax.ppermute(mine[split:], "tm", [(0, 1), (1, 0)]),
    ]
    swap = [(i, i ^ 1) for i in range(dp_size)]
    partner = jnp.concatenate([lax.ppermute(part, "dp", swap) for part in got_parts])
    got = jnp.concatenate(got_parts)
    low = jnp.where(core == 0, got, partner)
    high = jnp.where(core == 0, partner, got)

    def forward(act):
        own_act = lax.dynamic_slice_in_dim(act, tm * rows, rows, axis=1)
        other_act = lax.dynamic_slice_in_dim(act, (1 - tm) * rows, rows, axis=1)
        own = jnp.dot(own_act, w_ups, preferred_element_type=jnp.float32)
        other = jnp.concatenate(
            [
                jnp.dot(other_act, low, preferred_element_type=jnp.float32),
                jnp.dot(other_act, high, preferred_element_type=jnp.float32),
            ],
            axis=1,
        )
        return own + other

    def backward(d_taps):
        own = contract_cols(d_taps, w_ups)
        other = contract_cols(d_taps[:, :cols], low) + contract_cols(d_taps[:, cols:], high)
        return jnp.where(
            tm == 0, jnp.concatenate([own, other], axis=1), jnp.concatenate([other, own], axis=1)
        )

    return forward, backward


def on_device(
    src_mel, owner, dst_pos, keep, cotangent, w_pre, b_pre, w_ups, upsample_bias, w_res, b_res
):
    owners_count = lax.axis_size("dp")
    seg_rows = src_mel[0]
    seg_count = seg_rows.shape[0]
    mel_bins = w_pre.shape[0] // KPRE
    pick = jnp.arange(owners_count, dtype=jnp.int32)[:, None] == owner[0][None, :]
    seg_width = seg_rows.shape[1]
    header = jnp.stack([dst_pos[0] + 1, keep[0]], axis=1).astype(jnp.bfloat16)
    seg_ext = jnp.concatenate([seg_rows, header], axis=1)
    outgoing = jnp.dot(
        pick.astype(jnp.bfloat16), seg_ext, preferred_element_type=jnp.float32
    ).astype(jnp.bfloat16)
    arrived = lax.all_to_all(outgoing, "dp", split_axis=0, concat_axis=0, tiled=True)
    slot_code = arrived[:, seg_width].astype(jnp.int32)
    keep_code = arrived[:, seg_width + 1].astype(jnp.int32)
    place = (slot_code - 1)[:, None] == jnp.arange(seg_count, dtype=jnp.int32)[None, :]
    mel_segs = contract_rows(place.astype(jnp.bfloat16), arrived[:, :seg_width]).astype(
        jnp.bfloat16
    )
    keep_segs = jnp.sum(jnp.where(place, keep_code[:, None], 0), axis=0)
    mel = mel_segs.reshape(seg_count * (mel_segs.shape[1] // mel_bins), mel_bins)
    frame_count = mel.shape[0]
    mel_ext = with_halo(mel, (("tm", 0),), KPRE // 2 + 1)
    first_frame0 = lax.axis_index("tm") * frame_count
    total = lax.axis_size("tm") * frame_count
    cot = cotangent[0]
    marks = jnp.repeat(keep_segs, cot.shape[0] // seg_count)
    gradient_value = jnp.where(marks[:, None] > 0, cot, jnp.zeros_like(cot))
    ups_forward, ups_backward = ups_functions(w_ups)

    output_rows, grads = local_pass(
        mel_ext,
        gradient_value,
        first_frame0,
        total,
        w_pre,
        b_pre,
        ups_forward,
        ups_backward,
        upsample_bias,
        w_res,
        b_res,
    )
    summed = butterfly_psum(grads)
    return (output_rows[None], summed[0], summed[1], summed[2], summed[3])


def solution(mesh):
    in_specs = (
        P("tm", "dp", None),
        P("tm", "dp"),
        P("tm", "dp"),
        P("tm", "dp"),
        P("dp", "tm", None),
        P(),
        P(),
        P("tm", None),
        P(),
        P(),
        P(),
    )
    out_specs = (P("dp", "tm", None), P(), P(), P(), P())
    return jax.shard_map(
        on_device, mesh=mesh, in_specs=in_specs, out_specs=out_specs, check_vma=False
    )
```

```python
import jax
import jax.numpy as jnp
from jax import lax
from jax.sharding import PartitionSpec as P

KPRE = 7
UPSAMPLE_FACTOR = 8
DILATION_SIZE = 3


def with_halo(block, sides, width):
    for axis, dim in sides:
        count = lax.axis_size(axis)
        forward = [(i, i + 1) for i in range(count - 1)]
        backward = [(target, source) for source, target in forward]
        low = lax.ppermute(
            lax.slice_in_dim(block, block.shape[dim] - width, None, axis=dim), axis, forward
        )
        high = lax.ppermute(lax.slice_in_dim(block, 0, width, axis=dim), axis, backward)
        block = jnp.concatenate([low, block, high], axis=dim)
    return block


def leaky(value):
    return jnp.where(value > 0, value, 0.1 * value)


def negative_slope(value):
    return jnp.where(value > 0, 1.0, 0.1).astype(jnp.float32)


def contract_rows(left, right):
    return lax.dot_general(
        left, right, (((0,), (0,)), ((), ())), preferred_element_type=jnp.float32
    )


def contract_cols(left, right):
    return lax.dot_general(
        left, right, (((1,), (1,)), ((), ())), preferred_element_type=jnp.float32
    )


def local_pass(
    mel_ext,
    gradient_value,
    first_frame0,
    total,
    w_pre,
    b_pre,
    ups_forward,
    ups_backward,
    upsample_bias,
    w_res,
    b_res,
):
    mel_bins = mel_ext.shape[1]
    kpre = w_pre.shape[0] // mel_bins
    edge = kpre // 2 + 1
    frame_count = mel_ext.shape[0] - 2 * edge
    window_width = upsample_bias.shape[0]
    residual_kernel = w_res.shape[0] // window_width
    patches = jnp.concatenate([mel_ext[i : i + frame_count + 2] for i in range(kpre)], axis=1)
    pre = jnp.dot(patches, w_pre, preferred_element_type=jnp.float32) + b_pre
    frame_idx = first_frame0 - 1 + jnp.arange(frame_count + 2, dtype=jnp.int32)
    inside_f = ((frame_idx >= 0) & (frame_idx < total))[:, None]
    act = jnp.where(inside_f, leaky(pre), 0.0).astype(jnp.bfloat16)
    taps = ups_forward(act).reshape(frame_count + 2, 2 * UPSAMPLE_FACTOR, window_width)
    upper_output = taps[1:, :UPSAMPLE_FACTOR] + taps[:-1, UPSAMPLE_FACTOR:]
    sample_count = UPSAMPLE_FACTOR * frame_count
    start_offset = UPSAMPLE_FACTOR // 2 - DILATION_SIZE
    waveform = (
        upper_output.reshape(UPSAMPLE_FACTOR * (frame_count + 1), window_width)[
            start_offset : start_offset + sample_count + 2 * DILATION_SIZE
        ]
        + upsample_bias
    )
    step_index = (
        UPSAMPLE_FACTOR * first_frame0
        - DILATION_SIZE
        + jnp.arange(sample_count + 2 * DILATION_SIZE, dtype=jnp.int32)
    )
    inside_samples = ((step_index >= 0) & (step_index < UPSAMPLE_FACTOR * total))[:, None]
    hidden_state = jnp.where(inside_samples, leaky(waveform), 0.0).astype(jnp.bfloat16)
    column_block = jnp.concatenate(
        [
            hidden_state[kernel_index * DILATION_SIZE : kernel_index * DILATION_SIZE + sample_count]
            for kernel_index in range(residual_kernel)
        ],
        axis=1,
    )
    convolve_fn = jnp.dot(column_block, w_res, preferred_element_type=jnp.float32) + b_res
    output_rows = (waveform[DILATION_SIZE : DILATION_SIZE + sample_count] + convolve_fn).astype(
        jnp.bfloat16
    )
    g_wres = contract_rows(column_block, gradient_value)
    g_bres = jnp.sum(gradient_value.astype(jnp.float32), axis=0)
    backward_pass = contract_cols(gradient_value, w_res)
    hidden_gradient = jnp.zeros((sample_count + 2 * DILATION_SIZE, window_width), jnp.float32)
    for kernel_index in range(residual_kernel):
        hidden_gradient = hidden_gradient + jnp.pad(
            backward_pass[:, kernel_index * window_width : (kernel_index + 1) * window_width],
            (
                (
                    kernel_index * DILATION_SIZE,
                    (residual_kernel - 1 - kernel_index) * DILATION_SIZE,
                ),
                (0, 0),
            ),
        )
    waveform_gradient = jnp.where(
        inside_samples, hidden_gradient * negative_slope(waveform), 0.0
    ) + jnp.pad(gradient_value.astype(jnp.float32), ((DILATION_SIZE, DILATION_SIZE), (0, 0)))
    waveform_gradient = waveform_gradient.astype(jnp.bfloat16)
    d_upper = jnp.pad(waveform_gradient, ((start_offset, start_offset), (0, 0))).reshape(
        frame_count + 1, UPSAMPLE_FACTOR, window_width
    )
    zero_row = jnp.zeros((1, UPSAMPLE_FACTOR, window_width), jnp.bfloat16)
    d_taps = jnp.concatenate(
        [
            jnp.concatenate([zero_row, d_upper], axis=0),
            jnp.concatenate([d_upper, zero_row], axis=0),
        ],
        axis=1,
    )
    d_act = ups_backward(d_taps.reshape(frame_count + 2, 2 * UPSAMPLE_FACTOR * window_width))
    d_pre = jnp.where(inside_f, d_act * negative_slope(pre), 0.0).astype(jnp.bfloat16)
    g_wpre = contract_rows(patches, d_pre)
    g_bpre = jnp.sum(d_pre.astype(jnp.float32), axis=0)
    return (output_rows, (g_wpre, g_bpre, g_wres, g_bres))


def tile_rows(value):
    if value.ndim == 2 and value.shape[0] % 8 == 0 and value.shape[1] % 128 == 0:
        r, c = value.shape
        value = value.reshape(r // 8, 8, c // 128, 128).transpose(0, 2, 1, 3)
    return jnp.pad(value.reshape(-1), (0, -value.size % 128)).reshape(-1, 128)


def untile_rows(rows, shape):
    if len(shape) == 2 and shape[0] % 8 == 0 and shape[1] % 128 == 0:
        r, c = shape
        return rows.reshape(r // 8, c // 128, 8, 128).transpose(0, 2, 1, 3).reshape(shape)
    size = 1
    for n in shape:
        size *= n
    return rows.reshape(-1)[:size].reshape(shape)


def butterfly_psum(parts):
    dp_size = lax.axis_size("dp")
    tm_size = lax.axis_size("tm")
    axes = ("dp", "tm")
    levels = [("tm", 1 << k) for k in range(tm_size.bit_length() - 1)]
    levels += [("dp", 1 << k) for k in range(1, dp_size.bit_length() - 1)]
    groups = [levels[i : i + 2] for i in range(0, len(levels), 2)]
    orders = (groups, groups[::-1])
    count = dp_size * tm_size

    def perm_of(step, offset):
        out = []
        for d in range(dp_size):
            for t in range(tm_size):
                idx = {"dp": d, "tm": t}
                for j, (axis, bit) in enumerate(orders[d % 2][step]):
                    if (offset >> j) & 1:
                        idx[axis] = idx[axis] ^ bit
                out.append((d * tm_size + t, idx["dp"] * tm_size + idx["tm"]))
        return out

    core = lax.axis_index("dp") % 2
    position = {"dp": lax.axis_index("dp"), "tm": lax.axis_index("tm")}

    def slot_of(step):
        def one(group):
            return sum(((position[a] // b) % 2) << j for j, (a, b) in enumerate(group))

        return jnp.where(core == 0, one(orders[0][step]), one(orders[1][step]))

    tiles = [tile_rows(p) for p in parts]
    flat = jnp.concatenate([t.reshape(-1) for t in tiles])
    unit = 8 * 128 * count
    padded = -(-flat.shape[0] // unit) * unit
    x = jnp.pad(flat, (0, padded - flat.shape[0])).reshape(padded // 128, 128)
    core_perm = [(i, i ^ tm_size) for i in range(count)]
    half = x.shape[0] // 2
    send = lax.dynamic_slice_in_dim(x, (1 - core) * half, half)
    x = lax.dynamic_slice_in_dim(x, core * half, half) + lax.ppermute(send, axes, core_perm)
    for step in range(len(groups)):
        radix = 1 << len(groups[step])
        piece = x.shape[0] // radix
        slot = slot_of(step)
        total = lax.dynamic_slice_in_dim(x, slot * piece, piece)
        for offset in range(1, radix):
            send = lax.dynamic_slice_in_dim(x, (slot ^ offset) * piece, piece)
            total = total + lax.ppermute(send, axes, perm_of(step, offset))
        x = total
    for step in reversed(range(len(groups))):
        radix = 1 << len(groups[step])
        slot = slot_of(step)
        got = [x] + [lax.ppermute(x, axes, perm_of(step, o)) for o in range(1, radix)]
        pieces = []
        for q in range(radix):
            source = slot ^ q
            chosen = got[radix - 1]
            for o in range(radix - 2, -1, -1):
                chosen = jnp.where(source == o, got[o], chosen)
            pieces.append(chosen)
        x = jnp.concatenate(pieces)
    recv = lax.ppermute(x, axes, core_perm)
    x = jnp.where(core == 0, jnp.concatenate([x, recv]), jnp.concatenate([recv, x]))
    out, at = [], 0
    for p, t in zip(parts, tiles):
        out.append(untile_rows(x[at : at + t.shape[0]], p.shape))
        at += t.shape[0]
    return tuple(out)

def ups_functions(w_ups):
    dp_size = lax.axis_size("dp")
    if lax.axis_size("tm") != 2 or dp_size % 2:
        whole = lax.all_gather(w_ups, "tm", axis=0, tiled=True)
        return (
            lambda act: jnp.dot(act, whole, preferred_element_type=jnp.float32),
            lambda d_taps: contract_cols(d_taps, whole),
        )
    rows, width = w_ups.shape
    cols = width // 2
    core = lax.axis_index("dp") % 2
    tm = lax.axis_index("tm")
    mine = jnp.where(core == 0, w_ups[:, :cols], w_ups[:, cols:])
    split = rows // 2
    got_parts = [
        lax.ppermute(mine[:split], "tm", [(0, 1), (1, 0)]),
        lax.ppermute(mine[split:], "tm", [(0, 1), (1, 0)]),
    ]
    swap = [(i, i ^ 1) for i in range(dp_size)]
    partner = jnp.concatenate([lax.ppermute(part, "dp", swap) for part in got_parts])
    got = jnp.concatenate(got_parts)
    low = jnp.where(core == 0, got, partner)
    high = jnp.where(core == 0, partner, got)

    def forward(act):
        own_act = lax.dynamic_slice_in_dim(act, tm * rows, rows, axis=1)
        other_act = lax.dynamic_slice_in_dim(act, (1 - tm) * rows, rows, axis=1)
        own = jnp.dot(own_act, w_ups, preferred_element_type=jnp.float32)
        other = jnp.concatenate(
            [
                jnp.dot(other_act, low, preferred_element_type=jnp.float32),
                jnp.dot(other_act, high, preferred_element_type=jnp.float32),
            ],
            axis=1,
        )
        return own + other

    def backward(d_taps):
        own = contract_cols(d_taps, w_ups)
        other = contract_cols(d_taps[:, :cols], low) + contract_cols(d_taps[:, cols:], high)
        return jnp.where(
            tm == 0, jnp.concatenate([own, other], axis=1), jnp.concatenate([other, own], axis=1)
        )

    return forward, backward


def on_device(
    src_mel, owner, dst_pos, keep, cotangent, w_pre, b_pre, w_ups, upsample_bias, w_res, b_res
):
    owners_count = lax.axis_size("dp")
    seg_rows = src_mel[0]
    seg_count = seg_rows.shape[0]
    mel_bins = w_pre.shape[0] // KPRE
    pick = jnp.arange(owners_count, dtype=jnp.int32)[:, None] == owner[0][None, :]
    seg_width = seg_rows.shape[1]
    header = jnp.stack([dst_pos[0] + 1, keep[0]], axis=1).astype(jnp.bfloat16)
    seg_ext = jnp.concatenate([seg_rows, header], axis=1)
    outgoing = jnp.dot(
        pick.astype(jnp.bfloat16), seg_ext, preferred_element_type=jnp.float32
    ).astype(jnp.bfloat16)
    arrived = lax.all_to_all(outgoing, "dp", split_axis=0, concat_axis=0, tiled=True)
    slot_code = arrived[:, seg_width].astype(jnp.int32)
    keep_code = arrived[:, seg_width + 1].astype(jnp.int32)
    place = (slot_code - 1)[:, None] == jnp.arange(seg_count, dtype=jnp.int32)[None, :]
    mel_segs = contract_rows(place.astype(jnp.bfloat16), arrived[:, :seg_width]).astype(
        jnp.bfloat16
    )
    keep_segs = jnp.sum(jnp.where(place, keep_code[:, None], 0), axis=0)
    mel = mel_segs.reshape(seg_count * (mel_segs.shape[1] // mel_bins), mel_bins)
    frame_count = mel.shape[0]
    mel_ext = with_halo(mel, (("tm", 0),), KPRE // 2 + 1)
    first_frame0 = lax.axis_index("tm") * frame_count
    total = lax.axis_size("tm") * frame_count
    cot = cotangent[0]
    marks = jnp.repeat(keep_segs, cot.shape[0] // seg_count)
    gradient_value = jnp.where(marks[:, None] > 0, cot, jnp.zeros_like(cot))
    ups_forward, ups_backward = ups_functions(w_ups)

    output_rows, grads = local_pass(
        mel_ext,
        gradient_value,
        first_frame0,
        total,
        w_pre,
        b_pre,
        ups_forward,
        ups_backward,
        upsample_bias,
        w_res,
        b_res,
    )
    summed = butterfly_psum(grads)
    return (output_rows[None], summed[0], summed[1], summed[2], summed[3])


def solution(mesh):
    in_specs = (
        P("tm", "dp", None),
        P("tm", "dp"),
        P("tm", "dp"),
        P("tm", "dp"),
        P("dp", "tm", None),
        P(),
        P(),
        P("tm", None),
        P(),
        P(),
        P(),
    )
    out_specs = (P("dp", "tm", None), P(), P(), P(), P())
    return jax.shard_map(
        on_device, mesh=mesh, in_specs=in_specs, out_specs=out_specs, check_vma=False
    )
```

```python
import jax
import jax.numpy as jnp
from jax import lax
from jax.sharding import PartitionSpec as P

KPRE = 7
UPSAMPLE_FACTOR = 8
DILATION_SIZE = 3


def with_halo(block, sides, width):
    for axis, dim in sides:
        count = lax.axis_size(axis)
        forward = [(i, i + 1) for i in range(count - 1)]
        backward = [(target, source) for source, target in forward]
        low = lax.ppermute(
            lax.slice_in_dim(block, block.shape[dim] - width, None, axis=dim), axis, forward
        )
        high = lax.ppermute(lax.slice_in_dim(block, 0, width, axis=dim), axis, backward)
        block = jnp.concatenate([low, block, high], axis=dim)
    return block


def leaky(value):
    return jnp.where(value > 0, value, 0.1 * value)


def negative_slope(value):
    return jnp.where(value > 0, 1.0, 0.1).astype(jnp.float32)


def contract_rows(left, right):
    return lax.dot_general(
        left, right, (((0,), (0,)), ((), ())), preferred_element_type=jnp.float32
    )


def contract_cols(left, right):
    return lax.dot_general(
        left, right, (((1,), (1,)), ((), ())), preferred_element_type=jnp.float32
    )


def local_pass(
    mel_ext,
    gradient_value,
    first_frame0,
    total,
    w_pre,
    b_pre,
    ups_forward,
    ups_backward,
    upsample_bias,
    w_res,
    b_res,
):
    mel_bins = mel_ext.shape[1]
    kpre = w_pre.shape[0] // mel_bins
    edge = kpre // 2 + 1
    frame_count = mel_ext.shape[0] - 2 * edge
    window_width = upsample_bias.shape[0]
    residual_kernel = w_res.shape[0] // window_width
    patches = jnp.concatenate([mel_ext[i : i + frame_count + 2] for i in range(kpre)], axis=1)
    pre = jnp.dot(patches, w_pre, preferred_element_type=jnp.float32) + b_pre
    frame_idx = first_frame0 - 1 + jnp.arange(frame_count + 2, dtype=jnp.int32)
    inside_f = ((frame_idx >= 0) & (frame_idx < total))[:, None]
    act = jnp.where(inside_f, leaky(pre), 0.0).astype(jnp.bfloat16)
    taps = ups_forward(act).reshape(frame_count + 2, 2 * UPSAMPLE_FACTOR, window_width)
    upper_output = taps[1:, :UPSAMPLE_FACTOR] + taps[:-1, UPSAMPLE_FACTOR:]
    sample_count = UPSAMPLE_FACTOR * frame_count
    start_offset = UPSAMPLE_FACTOR // 2 - DILATION_SIZE
    waveform = (
        upper_output.reshape(UPSAMPLE_FACTOR * (frame_count + 1), window_width)[
            start_offset : start_offset + sample_count + 2 * DILATION_SIZE
        ]
        + upsample_bias
    )
    step_index = (
        UPSAMPLE_FACTOR * first_frame0
        - DILATION_SIZE
        + jnp.arange(sample_count + 2 * DILATION_SIZE, dtype=jnp.int32)
    )
    inside_samples = ((step_index >= 0) & (step_index < UPSAMPLE_FACTOR * total))[:, None]
    hidden_state = jnp.where(inside_samples, leaky(waveform), 0.0).astype(jnp.bfloat16)
    column_block = jnp.concatenate(
        [
            hidden_state[kernel_index * DILATION_SIZE : kernel_index * DILATION_SIZE + sample_count]
            for kernel_index in range(residual_kernel)
        ],
        axis=1,
    )
    convolve_fn = jnp.dot(column_block, w_res, preferred_element_type=jnp.float32) + b_res
    output_rows = (waveform[DILATION_SIZE : DILATION_SIZE + sample_count] + convolve_fn).astype(
        jnp.bfloat16
    )
    g_wres = contract_rows(column_block, gradient_value)
    g_bres = jnp.sum(gradient_value.astype(jnp.float32), axis=0)
    backward_pass = contract_cols(gradient_value, w_res)
    hidden_gradient = jnp.zeros((sample_count + 2 * DILATION_SIZE, window_width), jnp.float32)
    for kernel_index in range(residual_kernel):
        hidden_gradient = hidden_gradient + jnp.pad(
            backward_pass[:, kernel_index * window_width : (kernel_index + 1) * window_width],
            (
                (
                    kernel_index * DILATION_SIZE,
                    (residual_kernel - 1 - kernel_index) * DILATION_SIZE,
                ),
                (0, 0),
            ),
        )
    waveform_gradient = jnp.where(
        inside_samples, hidden_gradient * negative_slope(waveform), 0.0
    ) + jnp.pad(gradient_value.astype(jnp.float32), ((DILATION_SIZE, DILATION_SIZE), (0, 0)))
    waveform_gradient = waveform_gradient.astype(jnp.bfloat16)
    d_upper = jnp.pad(waveform_gradient, ((start_offset, start_offset), (0, 0))).reshape(
        frame_count + 1, UPSAMPLE_FACTOR, window_width
    )
    zero_row = jnp.zeros((1, UPSAMPLE_FACTOR, window_width), jnp.bfloat16)
    d_taps = jnp.concatenate(
        [
            jnp.concatenate([zero_row, d_upper], axis=0),
            jnp.concatenate([d_upper, zero_row], axis=0),
        ],
        axis=1,
    )
    d_act = ups_backward(d_taps.reshape(frame_count + 2, 2 * UPSAMPLE_FACTOR * window_width))
    d_pre = jnp.where(inside_f, d_act * negative_slope(pre), 0.0).astype(jnp.bfloat16)
    g_wpre = contract_rows(patches, d_pre)
    g_bpre = jnp.sum(d_pre.astype(jnp.float32), axis=0)
    return (output_rows, (g_wpre, g_bpre, g_wres, g_bres))


def tile_rows(value):
    if value.ndim == 2 and value.shape[0] % 8 == 0 and value.shape[1] % 128 == 0:
        r, c = value.shape
        value = value.reshape(r // 8, 8, c // 128, 128).transpose(0, 2, 1, 3)
    return jnp.pad(value.reshape(-1), (0, -value.size % 128)).reshape(-1, 128)


def untile_rows(rows, shape):
    if len(shape) == 2 and shape[0] % 8 == 0 and shape[1] % 128 == 0:
        r, c = shape
        return rows.reshape(r // 8, c // 128, 8, 128).transpose(0, 2, 1, 3).reshape(shape)
    size = 1
    for n in shape:
        size *= n
    return rows.reshape(-1)[:size].reshape(shape)


def butterfly_psum(parts):
    dp_size = lax.axis_size("dp")
    tm_size = lax.axis_size("tm")
    axes = ("dp", "tm")
    levels = [("tm", 1 << k) for k in range(tm_size.bit_length() - 1)]
    levels += [("dp", 1 << k) for k in range(1, dp_size.bit_length() - 1)]
    groups = [levels[i : i + 2] for i in range(0, len(levels), 2)]
    orders = (groups, groups[::-1])
    count = dp_size * tm_size

    def perm_of(step, offset):
        out = []
        for d in range(dp_size):
            for t in range(tm_size):
                idx = {"dp": d, "tm": t}
                for j, (axis, bit) in enumerate(orders[d % 2][step]):
                    if (offset >> j) & 1:
                        idx[axis] = idx[axis] ^ bit
                out.append((d * tm_size + t, idx["dp"] * tm_size + idx["tm"]))
        return out

    core = lax.axis_index("dp") % 2
    position = {"dp": lax.axis_index("dp"), "tm": lax.axis_index("tm")}

    def slot_of(step):
        def one(group):
            return sum(((position[a] // b) % 2) << j for j, (a, b) in enumerate(group))

        return jnp.where(core == 0, one(orders[0][step]), one(orders[1][step]))

    tiles = [tile_rows(p) for p in parts]
    flat = jnp.concatenate([t.reshape(-1) for t in tiles])
    unit = 8 * 128 * count
    padded = -(-flat.shape[0] // unit) * unit
    x = jnp.pad(flat, (0, padded - flat.shape[0])).reshape(padded // 128, 128)
    core_perm = [(i, i ^ tm_size) for i in range(count)]
    half = x.shape[0] // 2
    send = lax.dynamic_slice_in_dim(x, (1 - core) * half, half)
    x = lax.dynamic_slice_in_dim(x, core * half, half) + lax.ppermute(send, axes, core_perm)
    for step in range(len(groups)):
        radix = 1 << len(groups[step])
        piece = x.shape[0] // radix
        slot = slot_of(step)
        total = lax.dynamic_slice_in_dim(x, slot * piece, piece)
        for offset in range(1, radix):
            send = lax.dynamic_slice_in_dim(x, (slot ^ offset) * piece, piece)
            total = total + lax.ppermute(send, axes, perm_of(step, offset))
        x = total
    for step in reversed(range(len(groups))):
        radix = 1 << len(groups[step])
        slot = slot_of(step)
        got = [x] + [lax.ppermute(x, axes, perm_of(step, o)) for o in range(1, radix)]
        pieces = []
        for q in range(radix):
            source = slot ^ q
            chosen = got[radix - 1]
            for o in range(radix - 2, -1, -1):
                chosen = jnp.where(source == o, got[o], chosen)
            pieces.append(chosen)
        x = jnp.concatenate(pieces)
    recv = lax.ppermute(x, axes, core_perm)
    x = jnp.where(core == 0, jnp.concatenate([x, recv]), jnp.concatenate([recv, x]))
    out, at = [], 0
    for p, t in zip(parts, tiles):
        out.append(untile_rows(x[at : at + t.shape[0]], p.shape))
        at += t.shape[0]
    return tuple(out)

def ups_functions(w_ups):
    dp_size = lax.axis_size("dp")
    if lax.axis_size("tm") != 2 or dp_size % 2:
        whole = lax.all_gather(w_ups, "tm", axis=0, tiled=True)
        return (
            lambda act: jnp.dot(act, whole, preferred_element_type=jnp.float32),
            lambda d_taps: contract_cols(d_taps, whole),
            whole,
        )
    rows, width = w_ups.shape
    cols = width // 2
    core = lax.axis_index("dp") % 2
    tm = lax.axis_index("tm")
    mine = jnp.where(core == 0, w_ups[:, :cols], w_ups[:, cols:])
    split = rows // 2
    got_parts = [
        lax.ppermute(mine[:split], "tm", [(0, 1), (1, 0)]),
        lax.ppermute(mine[split:], "tm", [(0, 1), (1, 0)]),
    ]
    swap = [(i, i ^ 1) for i in range(dp_size)]
    partner = jnp.concatenate([lax.ppermute(part, "dp", swap) for part in got_parts])
    got = jnp.concatenate(got_parts)
    low = jnp.where(core == 0, got, partner)
    high = jnp.where(core == 0, partner, got)

    def forward(act):
        own_act = lax.dynamic_slice_in_dim(act, tm * rows, rows, axis=1)
        other_act = lax.dynamic_slice_in_dim(act, (1 - tm) * rows, rows, axis=1)
        own = jnp.dot(own_act, w_ups, preferred_element_type=jnp.float32)
        other = jnp.concatenate(
            [
                jnp.dot(other_act, low, preferred_element_type=jnp.float32),
                jnp.dot(other_act, high, preferred_element_type=jnp.float32),
            ],
            axis=1,
        )
        return own + other

    def backward(d_taps):
        own = contract_cols(d_taps, w_ups)
        other = contract_cols(d_taps[:, :cols], low) + contract_cols(d_taps[:, cols:], high)
        return jnp.where(
            tm == 0, jnp.concatenate([own, other], axis=1), jnp.concatenate([other, own], axis=1)
        )

    return forward, backward, got_parts[0]


def on_device(
    src_mel, owner, dst_pos, keep, cotangent, w_pre, b_pre, w_ups, upsample_bias, w_res, b_res
):
    owners_count = lax.axis_size("dp")
    ups_forward, ups_backward, ready = ups_functions(w_ups)
    src_mel, _ = lax.optimization_barrier((src_mel, ready))
    seg_rows = src_mel[0]
    seg_count = seg_rows.shape[0]
    mel_bins = w_pre.shape[0] // KPRE
    pick = jnp.arange(owners_count, dtype=jnp.int32)[:, None] == owner[0][None, :]
    seg_width = seg_rows.shape[1]
    header = jnp.stack([dst_pos[0] + 1, keep[0]], axis=1).astype(jnp.bfloat16)
    seg_ext = jnp.concatenate([seg_rows, header], axis=1)
    outgoing = jnp.dot(
        pick.astype(jnp.bfloat16), seg_ext, preferred_element_type=jnp.float32
    ).astype(jnp.bfloat16)
    arrived = lax.all_to_all(outgoing, "dp", split_axis=0, concat_axis=0, tiled=True)
    slot_code = arrived[:, seg_width].astype(jnp.int32)
    keep_code = arrived[:, seg_width + 1].astype(jnp.int32)
    place = (slot_code - 1)[:, None] == jnp.arange(seg_count, dtype=jnp.int32)[None, :]
    mel_segs = contract_rows(place.astype(jnp.bfloat16), arrived[:, :seg_width]).astype(
        jnp.bfloat16
    )
    keep_segs = jnp.sum(jnp.where(place, keep_code[:, None], 0), axis=0)
    mel = mel_segs.reshape(seg_count * (mel_segs.shape[1] // mel_bins), mel_bins)
    frame_count = mel.shape[0]
    mel_ext = with_halo(mel, (("tm", 0),), KPRE // 2 + 1)
    first_frame0 = lax.axis_index("tm") * frame_count
    total = lax.axis_size("tm") * frame_count
    cot = cotangent[0]
    marks = jnp.repeat(keep_segs, cot.shape[0] // seg_count)
    gradient_value = jnp.where(marks[:, None] > 0, cot, jnp.zeros_like(cot))
    output_rows, grads = local_pass(
        mel_ext,
        gradient_value,
        first_frame0,
        total,
        w_pre,
        b_pre,
        ups_forward,
        ups_backward,
        upsample_bias,
        w_res,
        b_res,
    )
    summed = butterfly_psum(grads)
    return (output_rows[None], summed[0], summed[1], summed[2], summed[3])


def solution(mesh):
    in_specs = (
        P("tm", "dp", None),
        P("tm", "dp"),
        P("tm", "dp"),
        P("tm", "dp"),
        P("dp", "tm", None),
        P(),
        P(),
        P("tm", None),
        P(),
        P(),
        P(),
    )
    out_specs = (P("dp", "tm", None), P(), P(), P(), P())
    return jax.shard_map(
        on_device, mesh=mesh, in_specs=in_specs, out_specs=out_specs, check_vma=False
    )
```

```python
import jax
import jax.numpy as jnp
from jax import lax
from jax.sharding import PartitionSpec as P

KPRE = 7
UPSAMPLE_FACTOR = 8
DILATION_SIZE = 3


def with_halo(block, sides, width):
    for axis, dim in sides:
        count = lax.axis_size(axis)
        forward = [(i, i + 1) for i in range(count - 1)]
        backward = [(target, source) for source, target in forward]
        low = lax.ppermute(
            lax.slice_in_dim(block, block.shape[dim] - width, None, axis=dim), axis, forward
        )
        high = lax.ppermute(lax.slice_in_dim(block, 0, width, axis=dim), axis, backward)
        block = jnp.concatenate([low, block, high], axis=dim)
    return block


def leaky(value):
    return jnp.where(value > 0, value, 0.1 * value)


def negative_slope(value):
    return jnp.where(value > 0, 1.0, 0.1).astype(jnp.float32)


def contract_rows(left, right):
    return lax.dot_general(
        left, right, (((0,), (0,)), ((), ())), preferred_element_type=jnp.float32
    )


def contract_cols(left, right):
    return lax.dot_general(
        left, right, (((1,), (1,)), ((), ())), preferred_element_type=jnp.float32
    )


def local_pass(
    mel_ext,
    gradient_value,
    first_frame0,
    total,
    w_pre,
    b_pre,
    ups_forward,
    ups_backward,
    upsample_bias,
    w_res,
    b_res,
):
    mel_bins = mel_ext.shape[1]
    kpre = w_pre.shape[0] // mel_bins
    edge = kpre // 2 + 1
    frame_count = mel_ext.shape[0] - 2 * edge
    window_width = upsample_bias.shape[0]
    residual_kernel = w_res.shape[0] // window_width
    patches = jnp.concatenate([mel_ext[i : i + frame_count + 2] for i in range(kpre)], axis=1)
    pre = jnp.dot(patches, w_pre, preferred_element_type=jnp.float32) + b_pre
    frame_idx = first_frame0 - 1 + jnp.arange(frame_count + 2, dtype=jnp.int32)
    inside_f = ((frame_idx >= 0) & (frame_idx < total))[:, None]
    act = jnp.where(inside_f, leaky(pre), 0.0).astype(jnp.bfloat16)
    taps = ups_forward(act).reshape(frame_count + 2, 2 * UPSAMPLE_FACTOR, window_width)
    upper_output = taps[1:, :UPSAMPLE_FACTOR] + taps[:-1, UPSAMPLE_FACTOR:]
    sample_count = UPSAMPLE_FACTOR * frame_count
    start_offset = UPSAMPLE_FACTOR // 2 - DILATION_SIZE
    waveform = (
        upper_output.reshape(UPSAMPLE_FACTOR * (frame_count + 1), window_width)[
            start_offset : start_offset + sample_count + 2 * DILATION_SIZE
        ]
        + upsample_bias
    )
    step_index = (
        UPSAMPLE_FACTOR * first_frame0
        - DILATION_SIZE
        + jnp.arange(sample_count + 2 * DILATION_SIZE, dtype=jnp.int32)
    )
    inside_samples = ((step_index >= 0) & (step_index < UPSAMPLE_FACTOR * total))[:, None]
    hidden_state = jnp.where(inside_samples, leaky(waveform), 0.0).astype(jnp.bfloat16)
    column_block = jnp.concatenate(
        [
            hidden_state[kernel_index * DILATION_SIZE : kernel_index * DILATION_SIZE + sample_count]
            for kernel_index in range(residual_kernel)
        ],
        axis=1,
    )
    convolve_fn = jnp.dot(column_block, w_res, preferred_element_type=jnp.float32) + b_res
    output_rows = (waveform[DILATION_SIZE : DILATION_SIZE + sample_count] + convolve_fn).astype(
        jnp.bfloat16
    )
    g_wres = contract_rows(column_block, gradient_value)
    g_bres = jnp.sum(gradient_value.astype(jnp.float32), axis=0)
    backward_pass = contract_cols(gradient_value, w_res)
    hidden_gradient = jnp.zeros((sample_count + 2 * DILATION_SIZE, window_width), jnp.float32)
    for kernel_index in range(residual_kernel):
        hidden_gradient = hidden_gradient + jnp.pad(
            backward_pass[:, kernel_index * window_width : (kernel_index + 1) * window_width],
            (
                (
                    kernel_index * DILATION_SIZE,
                    (residual_kernel - 1 - kernel_index) * DILATION_SIZE,
                ),
                (0, 0),
            ),
        )
    waveform_gradient = jnp.where(
        inside_samples, hidden_gradient * negative_slope(waveform), 0.0
    ) + jnp.pad(gradient_value.astype(jnp.float32), ((DILATION_SIZE, DILATION_SIZE), (0, 0)))
    waveform_gradient = waveform_gradient.astype(jnp.bfloat16)
    d_upper = jnp.pad(waveform_gradient, ((start_offset, start_offset), (0, 0))).reshape(
        frame_count + 1, UPSAMPLE_FACTOR, window_width
    )
    zero_row = jnp.zeros((1, UPSAMPLE_FACTOR, window_width), jnp.bfloat16)
    d_taps = jnp.concatenate(
        [
            jnp.concatenate([zero_row, d_upper], axis=0),
            jnp.concatenate([d_upper, zero_row], axis=0),
        ],
        axis=1,
    )
    d_act = ups_backward(d_taps.reshape(frame_count + 2, 2 * UPSAMPLE_FACTOR * window_width))
    d_pre = jnp.where(inside_f, d_act * negative_slope(pre), 0.0).astype(jnp.bfloat16)
    g_wpre = contract_rows(patches, d_pre)
    g_bpre = jnp.sum(d_pre.astype(jnp.float32), axis=0)
    return (output_rows, (g_wpre, g_bpre, g_wres, g_bres))


def tile_rows(value):
    if value.ndim == 2 and value.shape[0] % 8 == 0 and value.shape[1] % 128 == 0:
        r, c = value.shape
        value = value.reshape(r // 8, 8, c // 128, 128).transpose(0, 2, 1, 3)
    return jnp.pad(value.reshape(-1), (0, -value.size % 128)).reshape(-1, 128)


def untile_rows(rows, shape):
    if len(shape) == 2 and shape[0] % 8 == 0 and shape[1] % 128 == 0:
        r, c = shape
        return rows.reshape(r // 8, c // 128, 8, 128).transpose(0, 2, 1, 3).reshape(shape)
    size = 1
    for n in shape:
        size *= n
    return rows.reshape(-1)[:size].reshape(shape)


def butterfly_psum(parts):
    dp_size = lax.axis_size("dp")
    tm_size = lax.axis_size("tm")
    axes = ("dp", "tm")
    levels = [("tm", 1 << k) for k in range(tm_size.bit_length() - 1)]
    levels += [("dp", 1 << k) for k in range(1, dp_size.bit_length() - 1)]
    groups = [levels[i : i + 2] for i in range(0, len(levels), 2)]
    orders = (groups, groups[::-1])
    count = dp_size * tm_size

    def perm_of(step, offset):
        out = []
        for d in range(dp_size):
            for t in range(tm_size):
                idx = {"dp": d, "tm": t}
                for j, (axis, bit) in enumerate(orders[d % 2][step]):
                    if (offset >> j) & 1:
                        idx[axis] = idx[axis] ^ bit
                out.append((d * tm_size + t, idx["dp"] * tm_size + idx["tm"]))
        return out

    core = lax.axis_index("dp") % 2
    position = {"dp": lax.axis_index("dp"), "tm": lax.axis_index("tm")}

    def slot_of(step):
        def one(group):
            return sum(((position[a] // b) % 2) << j for j, (a, b) in enumerate(group))

        return jnp.where(core == 0, one(orders[0][step]), one(orders[1][step]))

    tiles = [tile_rows(p) for p in parts]
    flat = jnp.concatenate([t.reshape(-1) for t in tiles])
    unit = 8 * 128 * count
    padded = -(-flat.shape[0] // unit) * unit
    x = jnp.pad(flat, (0, padded - flat.shape[0])).reshape(padded // 128, 128)
    core_perm = [(i, i ^ tm_size) for i in range(count)]
    half = x.shape[0] // 2
    send = lax.dynamic_slice_in_dim(x, (1 - core) * half, half)
    x = lax.dynamic_slice_in_dim(x, core * half, half) + lax.ppermute(send, axes, core_perm)
    for step in range(len(groups)):
        radix = 1 << len(groups[step])
        piece = x.shape[0] // radix
        slot = slot_of(step)
        total = lax.dynamic_slice_in_dim(x, slot * piece, piece)
        for offset in range(1, radix):
            send = lax.dynamic_slice_in_dim(x, (slot ^ offset) * piece, piece)
            total = total + lax.ppermute(send, axes, perm_of(step, offset))
        x = total
    for step in reversed(range(len(groups))):
        radix = 1 << len(groups[step])
        slot = slot_of(step)
        got = [x] + [lax.ppermute(x, axes, perm_of(step, o)) for o in range(1, radix)]
        pieces = []
        for q in range(radix):
            source = slot ^ q
            chosen = got[radix - 1]
            for o in range(radix - 2, -1, -1):
                chosen = jnp.where(source == o, got[o], chosen)
            pieces.append(chosen)
        x = jnp.concatenate(pieces)
    recv = lax.ppermute(x, axes, core_perm)
    x = jnp.where(core == 0, jnp.concatenate([x, recv]), jnp.concatenate([recv, x]))
    out, at = [], 0
    for p, t in zip(parts, tiles):
        out.append(untile_rows(x[at : at + t.shape[0]], p.shape))
        at += t.shape[0]
    return tuple(out)

def ups_functions(w_ups):
    dp_size = lax.axis_size("dp")
    if lax.axis_size("tm") != 2 or dp_size % 2:
        whole = lax.all_gather(w_ups, "tm", axis=0, tiled=True)
        return (
            lambda act: jnp.dot(act, whole, preferred_element_type=jnp.float32),
            lambda d_taps: contract_cols(d_taps, whole),
            whole,
        )
    rows, width = w_ups.shape
    cols = width // 2
    core = lax.axis_index("dp") % 2
    tm = lax.axis_index("tm")
    mine = jnp.where(core == 0, w_ups[:, :cols], w_ups[:, cols:])
    bounds = [0, 16, rows // 2, rows] if rows % 32 == 0 and rows > 32 else [0, rows]
    got_parts = [
        lax.ppermute(mine[lo:hi], "tm", [(0, 1), (1, 0)]) for lo, hi in zip(bounds, bounds[1:])
    ]
    swap = [(i, i ^ 1) for i in range(dp_size)]
    partner = jnp.concatenate([lax.ppermute(part, "dp", swap) for part in got_parts])
    got = jnp.concatenate(got_parts)
    low = jnp.where(core == 0, got, partner)
    high = jnp.where(core == 0, partner, got)

    def forward(act):
        own_act = lax.dynamic_slice_in_dim(act, tm * rows, rows, axis=1)
        other_act = lax.dynamic_slice_in_dim(act, (1 - tm) * rows, rows, axis=1)
        own = jnp.dot(own_act, w_ups, preferred_element_type=jnp.float32)
        other = jnp.concatenate(
            [
                jnp.dot(other_act, low, preferred_element_type=jnp.float32),
                jnp.dot(other_act, high, preferred_element_type=jnp.float32),
            ],
            axis=1,
        )
        return own + other

    def backward(d_taps):
        own = contract_cols(d_taps, w_ups)
        other = contract_cols(d_taps[:, :cols], low) + contract_cols(d_taps[:, cols:], high)
        return jnp.where(
            tm == 0, jnp.concatenate([own, other], axis=1), jnp.concatenate([other, own], axis=1)
        )

    return forward, backward, got_parts[0]


def on_device(
    src_mel, owner, dst_pos, keep, cotangent, w_pre, b_pre, w_ups, upsample_bias, w_res, b_res
):
    owners_count = lax.axis_size("dp")
    ups_forward, ups_backward, ready = ups_functions(w_ups)
    src_mel, _ = lax.optimization_barrier((src_mel, ready))
    seg_rows = src_mel[0]
    seg_count = seg_rows.shape[0]
    mel_bins = w_pre.shape[0] // KPRE
    pick = jnp.arange(owners_count, dtype=jnp.int32)[:, None] == owner[0][None, :]
    seg_width = seg_rows.shape[1]
    header = jnp.stack([dst_pos[0] + 1, keep[0]], axis=1).astype(jnp.bfloat16)
    seg_ext = jnp.concatenate([seg_rows, header], axis=1)
    outgoing = jnp.dot(
        pick.astype(jnp.bfloat16), seg_ext, preferred_element_type=jnp.float32
    ).astype(jnp.bfloat16)
    arrived = lax.all_to_all(outgoing, "dp", split_axis=0, concat_axis=0, tiled=True)
    slot_code = arrived[:, seg_width].astype(jnp.int32)
    keep_code = arrived[:, seg_width + 1].astype(jnp.int32)
    place = (slot_code - 1)[:, None] == jnp.arange(seg_count, dtype=jnp.int32)[None, :]
    mel_segs = contract_rows(place.astype(jnp.bfloat16), arrived[:, :seg_width]).astype(
        jnp.bfloat16
    )
    keep_segs = jnp.sum(jnp.where(place, keep_code[:, None], 0), axis=0)
    mel = mel_segs.reshape(seg_count * (mel_segs.shape[1] // mel_bins), mel_bins)
    frame_count = mel.shape[0]
    mel_ext = with_halo(mel, (("tm", 0),), KPRE // 2 + 1)
    first_frame0 = lax.axis_index("tm") * frame_count
    total = lax.axis_size("tm") * frame_count
    cot = cotangent[0]
    marks = jnp.repeat(keep_segs, cot.shape[0] // seg_count)
    gradient_value = jnp.where(marks[:, None] > 0, cot, jnp.zeros_like(cot))
    output_rows, grads = local_pass(
        mel_ext,
        gradient_value,
        first_frame0,
        total,
        w_pre,
        b_pre,
        ups_forward,
        ups_backward,
        upsample_bias,
        w_res,
        b_res,
    )
    summed = butterfly_psum(grads)
    return (output_rows[None], summed[0], summed[1], summed[2], summed[3])


def solution(mesh):
    in_specs = (
        P("tm", "dp", None),
        P("tm", "dp"),
        P("tm", "dp"),
        P("tm", "dp"),
        P("dp", "tm", None),
        P(),
        P(),
        P("tm", None),
        P(),
        P(),
        P(),
    )
    out_specs = (P("dp", "tm", None), P(), P(), P(), P())
    return jax.shard_map(
        on_device, mesh=mesh, in_specs=in_specs, out_specs=out_specs, check_vma=False
    )
```

```python
import jax
import jax.numpy as jnp
from jax import lax
from jax.sharding import PartitionSpec as P

KPRE = 7
UPSAMPLE_FACTOR = 8
DILATION_SIZE = 3


def with_halo(block, sides, width):
    for axis, dim in sides:
        count = lax.axis_size(axis)
        forward = [(i, i + 1) for i in range(count - 1)]
        backward = [(target, source) for source, target in forward]
        low = lax.ppermute(
            lax.slice_in_dim(block, block.shape[dim] - width, None, axis=dim), axis, forward
        )
        high = lax.ppermute(lax.slice_in_dim(block, 0, width, axis=dim), axis, backward)
        block = jnp.concatenate([low, block, high], axis=dim)
    return block


def leaky(value):
    return jnp.where(value > 0, value, 0.1 * value)


def negative_slope(value):
    return jnp.where(value > 0, 1.0, 0.1).astype(jnp.float32)


def contract_rows(left, right):
    return lax.dot_general(
        left, right, (((0,), (0,)), ((), ())), preferred_element_type=jnp.float32
    )


def contract_cols(left, right):
    return lax.dot_general(
        left, right, (((1,), (1,)), ((), ())), preferred_element_type=jnp.float32
    )


def local_pass(
    mel_ext,
    gradient_value,
    first_frame0,
    total,
    w_pre,
    b_pre,
    ups_forward,
    ups_backward,
    upsample_bias,
    w_res,
    b_res,
):
    mel_bins = mel_ext.shape[1]
    kpre = w_pre.shape[0] // mel_bins
    edge = kpre // 2 + 1
    frame_count = mel_ext.shape[0] - 2 * edge
    window_width = upsample_bias.shape[0]
    residual_kernel = w_res.shape[0] // window_width
    patches = jnp.concatenate([mel_ext[i : i + frame_count + 2] for i in range(kpre)], axis=1)
    pre = jnp.dot(patches, w_pre, preferred_element_type=jnp.float32) + b_pre
    frame_idx = first_frame0 - 1 + jnp.arange(frame_count + 2, dtype=jnp.int32)
    inside_f = ((frame_idx >= 0) & (frame_idx < total))[:, None]
    act = jnp.where(inside_f, leaky(pre), 0.0).astype(jnp.bfloat16)
    taps = ups_forward(act).reshape(frame_count + 2, 2 * UPSAMPLE_FACTOR, window_width)
    upper_output = taps[1:, :UPSAMPLE_FACTOR] + taps[:-1, UPSAMPLE_FACTOR:]
    sample_count = UPSAMPLE_FACTOR * frame_count
    start_offset = UPSAMPLE_FACTOR // 2 - DILATION_SIZE
    waveform = (
        upper_output.reshape(UPSAMPLE_FACTOR * (frame_count + 1), window_width)[
            start_offset : start_offset + sample_count + 2 * DILATION_SIZE
        ]
        + upsample_bias
    )
    step_index = (
        UPSAMPLE_FACTOR * first_frame0
        - DILATION_SIZE
        + jnp.arange(sample_count + 2 * DILATION_SIZE, dtype=jnp.int32)
    )
    inside_samples = ((step_index >= 0) & (step_index < UPSAMPLE_FACTOR * total))[:, None]
    hidden_state = jnp.where(inside_samples, leaky(waveform), 0.0).astype(jnp.bfloat16)
    column_block = jnp.concatenate(
        [
            hidden_state[kernel_index * DILATION_SIZE : kernel_index * DILATION_SIZE + sample_count]
            for kernel_index in range(residual_kernel)
        ],
        axis=1,
    )
    convolve_fn = jnp.dot(column_block, w_res, preferred_element_type=jnp.float32) + b_res
    output_rows = (waveform[DILATION_SIZE : DILATION_SIZE + sample_count] + convolve_fn).astype(
        jnp.bfloat16
    )
    g_wres = contract_rows(column_block, gradient_value)
    g_bres = jnp.sum(gradient_value.astype(jnp.float32), axis=0)
    backward_pass = contract_cols(gradient_value, w_res)
    hidden_gradient = jnp.zeros((sample_count + 2 * DILATION_SIZE, window_width), jnp.float32)
    for kernel_index in range(residual_kernel):
        hidden_gradient = hidden_gradient + jnp.pad(
            backward_pass[:, kernel_index * window_width : (kernel_index + 1) * window_width],
            (
                (
                    kernel_index * DILATION_SIZE,
                    (residual_kernel - 1 - kernel_index) * DILATION_SIZE,
                ),
                (0, 0),
            ),
        )
    waveform_gradient = jnp.where(
        inside_samples, hidden_gradient * negative_slope(waveform), 0.0
    ) + jnp.pad(gradient_value.astype(jnp.float32), ((DILATION_SIZE, DILATION_SIZE), (0, 0)))
    waveform_gradient = waveform_gradient.astype(jnp.bfloat16)
    d_upper = jnp.pad(waveform_gradient, ((start_offset, start_offset), (0, 0))).reshape(
        frame_count + 1, UPSAMPLE_FACTOR, window_width
    )
    zero_row = jnp.zeros((1, UPSAMPLE_FACTOR, window_width), jnp.bfloat16)
    d_taps = jnp.concatenate(
        [
            jnp.concatenate([zero_row, d_upper], axis=0),
            jnp.concatenate([d_upper, zero_row], axis=0),
        ],
        axis=1,
    )
    d_act = ups_backward(d_taps.reshape(frame_count + 2, 2 * UPSAMPLE_FACTOR * window_width))
    d_pre = jnp.where(inside_f, d_act * negative_slope(pre), 0.0).astype(jnp.bfloat16)
    g_wpre = contract_rows(patches, d_pre)
    g_bpre = jnp.sum(d_pre.astype(jnp.float32), axis=0)
    return (output_rows, (g_wpre, g_bpre, g_wres, g_bres))


def tile_rows(value):
    if value.ndim == 2 and value.shape[0] % 8 == 0 and value.shape[1] % 128 == 0:
        r, c = value.shape
        value = value.reshape(r // 8, 8, c // 128, 128).transpose(0, 2, 1, 3)
    return jnp.pad(value.reshape(-1), (0, -value.size % 128)).reshape(-1, 128)


def untile_rows(rows, shape):
    if len(shape) == 2 and shape[0] % 8 == 0 and shape[1] % 128 == 0:
        r, c = shape
        return rows.reshape(r // 8, c // 128, 8, 128).transpose(0, 2, 1, 3).reshape(shape)
    size = 1
    for n in shape:
        size *= n
    return rows.reshape(-1)[:size].reshape(shape)


def butterfly_psum(parts):
    dp_size = lax.axis_size("dp")
    tm_size = lax.axis_size("tm")
    axes = ("dp", "tm")
    levels = [("tm", 1 << k) for k in range(tm_size.bit_length() - 1)]
    levels += [("dp", 1 << k) for k in range(1, dp_size.bit_length() - 1)]
    groups = [levels[i : i + 2] for i in range(0, len(levels), 2)]
    orders = (groups, groups[::-1])
    count = dp_size * tm_size

    def perm_of(step, offset):
        out = []
        for d in range(dp_size):
            for t in range(tm_size):
                idx = {"dp": d, "tm": t}
                for j, (axis, bit) in enumerate(orders[d % 2][step]):
                    if (offset >> j) & 1:
                        idx[axis] = idx[axis] ^ bit
                out.append((d * tm_size + t, idx["dp"] * tm_size + idx["tm"]))
        return out

    core = lax.axis_index("dp") % 2
    position = {"dp": lax.axis_index("dp"), "tm": lax.axis_index("tm")}

    def slot_of(step):
        def one(group):
            return sum(((position[a] // b) % 2) << j for j, (a, b) in enumerate(group))

        return jnp.where(core == 0, one(orders[0][step]), one(orders[1][step]))

    tiles = [tile_rows(p) for p in parts]
    flat = jnp.concatenate([t.reshape(-1) for t in tiles])
    unit = 8 * 128 * count
    padded = -(-flat.shape[0] // unit) * unit
    x = jnp.pad(flat, (0, padded - flat.shape[0])).reshape(padded // 128, 128)
    core_perm = [(i, i ^ tm_size) for i in range(count)]
    half = x.shape[0] // 2
    send = lax.dynamic_slice_in_dim(x, (1 - core) * half, half)
    x = lax.dynamic_slice_in_dim(x, core * half, half) + lax.ppermute(send, axes, core_perm)
    for step in range(len(groups)):
        radix = 1 << len(groups[step])
        piece = x.shape[0] // radix
        slot = slot_of(step)
        total = lax.dynamic_slice_in_dim(x, slot * piece, piece)
        for offset in range(1, radix):
            send = lax.dynamic_slice_in_dim(x, (slot ^ offset) * piece, piece)
            total = total + lax.ppermute(send, axes, perm_of(step, offset))
        x = total
    for step in reversed(range(len(groups))):
        radix = 1 << len(groups[step])
        slot = slot_of(step)
        got = [x] + [lax.ppermute(x, axes, perm_of(step, o)) for o in range(1, radix)]
        pieces = []
        for q in range(radix):
            source = slot ^ q
            chosen = got[radix - 1]
            for o in range(radix - 2, -1, -1):
                chosen = jnp.where(source == o, got[o], chosen)
            pieces.append(chosen)
        x = jnp.concatenate(pieces)
    recv = lax.ppermute(x, axes, core_perm)
    x = jnp.where(core == 0, jnp.concatenate([x, recv]), jnp.concatenate([recv, x]))
    out, at = [], 0
    for p, t in zip(parts, tiles):
        out.append(untile_rows(x[at : at + t.shape[0]], p.shape))
        at += t.shape[0]
    return tuple(out)

def ups_functions(w_ups):
    dp_size = lax.axis_size("dp")
    if lax.axis_size("tm") != 2 or dp_size % 2:
        whole = lax.all_gather(w_ups, "tm", axis=0, tiled=True)
        return (
            lambda act: jnp.dot(act, whole, preferred_element_type=jnp.float32),
            lambda d_taps: contract_cols(d_taps, whole),
            whole,
        )
    rows, width = w_ups.shape
    cols = width // 2
    core = lax.axis_index("dp") % 2
    tm = lax.axis_index("tm")
    bounds = [0, 16, rows // 2, rows] if rows % 32 == 0 and rows > 32 else [0, rows]
    swap = [(i, i ^ 1) for i in range(dp_size)]
    got_parts, partner_parts = [], []
    for lo, hi in zip(bounds, bounds[1:]):
        block = w_ups[lo:hi]
        mine = jnp.where(core == 0, block[:, :cols], block[:, cols:])
        got_parts.append(lax.ppermute(mine, "tm", [(0, 1), (1, 0)]))
        partner_parts.append(lax.ppermute(got_parts[-1], "dp", swap))
    low = jnp.concatenate(
        [jnp.where(core == 0, g, p) for g, p in zip(got_parts, partner_parts)]
    )
    high = jnp.concatenate(
        [jnp.where(core == 0, p, g) for g, p in zip(got_parts, partner_parts)]
    )

    def forward(act):
        own_act = lax.dynamic_slice_in_dim(act, tm * rows, rows, axis=1)
        other_act = lax.dynamic_slice_in_dim(act, (1 - tm) * rows, rows, axis=1)
        own = jnp.dot(own_act, w_ups, preferred_element_type=jnp.float32)
        other = jnp.concatenate(
            [
                jnp.dot(other_act, low, preferred_element_type=jnp.float32),
                jnp.dot(other_act, high, preferred_element_type=jnp.float32),
            ],
            axis=1,
        )
        return own + other

    def backward(d_taps):
        own = contract_cols(d_taps, w_ups)
        other = contract_cols(d_taps[:, :cols], low) + contract_cols(d_taps[:, cols:], high)
        return jnp.where(
            tm == 0, jnp.concatenate([own, other], axis=1), jnp.concatenate([other, own], axis=1)
        )

    return forward, backward, got_parts[0]


def on_device(
    src_mel, owner, dst_pos, keep, cotangent, w_pre, b_pre, w_ups, upsample_bias, w_res, b_res
):
    owners_count = lax.axis_size("dp")
    ups_forward, ups_backward, ready = ups_functions(w_ups)
    src_mel, _ = lax.optimization_barrier((src_mel, ready))
    seg_rows = src_mel[0]
    seg_count = seg_rows.shape[0]
    mel_bins = w_pre.shape[0] // KPRE
    pick = jnp.arange(owners_count, dtype=jnp.int32)[:, None] == owner[0][None, :]
    seg_width = seg_rows.shape[1]
    header = jnp.stack([dst_pos[0] + 1, keep[0]], axis=1).astype(jnp.bfloat16)
    seg_ext = jnp.concatenate([seg_rows, header], axis=1)
    outgoing = jnp.dot(
        pick.astype(jnp.bfloat16), seg_ext, preferred_element_type=jnp.float32
    ).astype(jnp.bfloat16)
    arrived = lax.all_to_all(outgoing, "dp", split_axis=0, concat_axis=0, tiled=True)
    slot_code = arrived[:, seg_width].astype(jnp.int32)
    keep_code = arrived[:, seg_width + 1].astype(jnp.int32)
    place = (slot_code - 1)[:, None] == jnp.arange(seg_count, dtype=jnp.int32)[None, :]
    mel_segs = contract_rows(place.astype(jnp.bfloat16), arrived[:, :seg_width]).astype(
        jnp.bfloat16
    )
    keep_segs = jnp.sum(jnp.where(place, keep_code[:, None], 0), axis=0)
    mel = mel_segs.reshape(seg_count * (mel_segs.shape[1] // mel_bins), mel_bins)
    frame_count = mel.shape[0]
    mel_ext = with_halo(mel, (("tm", 0),), KPRE // 2 + 1)
    first_frame0 = lax.axis_index("tm") * frame_count
    total = lax.axis_size("tm") * frame_count
    cot = cotangent[0]
    marks = jnp.repeat(keep_segs, cot.shape[0] // seg_count)
    gradient_value = jnp.where(marks[:, None] > 0, cot, jnp.zeros_like(cot))
    output_rows, grads = local_pass(
        mel_ext,
        gradient_value,
        first_frame0,
        total,
        w_pre,
        b_pre,
        ups_forward,
        ups_backward,
        upsample_bias,
        w_res,
        b_res,
    )
    summed = butterfly_psum(grads)
    return (output_rows[None], summed[0], summed[1], summed[2], summed[3])


def solution(mesh):
    in_specs = (
        P("tm", "dp", None),
        P("tm", "dp"),
        P("tm", "dp"),
        P("tm", "dp"),
        P("dp", "tm", None),
        P(),
        P(),
        P("tm", None),
        P(),
        P(),
        P(),
    )
    out_specs = (P("dp", "tm", None), P(), P(), P(), P())
    return jax.shard_map(
        on_device, mesh=mesh, in_specs=in_specs, out_specs=out_specs, check_vma=False
    )
```

```python
import jax
import jax.numpy as jnp
from jax import lax
from jax.sharding import PartitionSpec as P

KPRE = 7
UPSAMPLE_FACTOR = 8
DILATION_SIZE = 3


def with_halo(block, sides, width):
    for axis, dim in sides:
        count = lax.axis_size(axis)
        forward = [(i, i + 1) for i in range(count - 1)]
        backward = [(target, source) for source, target in forward]
        low = lax.ppermute(
            lax.slice_in_dim(block, block.shape[dim] - width, None, axis=dim), axis, forward
        )
        high = lax.ppermute(lax.slice_in_dim(block, 0, width, axis=dim), axis, backward)
        block = jnp.concatenate([low, block, high], axis=dim)
    return block


def leaky(value):
    return jnp.where(value > 0, value, 0.1 * value)


def negative_slope(value):
    return jnp.where(value > 0, 1.0, 0.1).astype(jnp.float32)


def contract_rows(left, right):
    return lax.dot_general(
        left, right, (((0,), (0,)), ((), ())), preferred_element_type=jnp.float32
    )


def contract_cols(left, right):
    return lax.dot_general(
        left, right, (((1,), (1,)), ((), ())), preferred_element_type=jnp.float32
    )


def local_pass(
    mel_ext,
    gradient_value,
    first_frame0,
    total,
    w_pre,
    b_pre,
    ups_forward,
    ups_backward,
    upsample_bias,
    w_res,
    b_res,
):
    mel_bins = mel_ext.shape[1]
    kpre = w_pre.shape[0] // mel_bins
    edge = kpre // 2 + 1
    frame_count = mel_ext.shape[0] - 2 * edge
    window_width = upsample_bias.shape[0]
    residual_kernel = w_res.shape[0] // window_width
    patches = jnp.concatenate([mel_ext[i : i + frame_count + 2] for i in range(kpre)], axis=1)
    pre = jnp.dot(patches, w_pre, preferred_element_type=jnp.float32) + b_pre
    frame_idx = first_frame0 - 1 + jnp.arange(frame_count + 2, dtype=jnp.int32)
    inside_f = ((frame_idx >= 0) & (frame_idx < total))[:, None]
    act = jnp.where(inside_f, leaky(pre), 0.0).astype(jnp.bfloat16)
    taps = ups_forward(act).reshape(frame_count + 2, 2 * UPSAMPLE_FACTOR, window_width)
    upper_output = taps[1:, :UPSAMPLE_FACTOR] + taps[:-1, UPSAMPLE_FACTOR:]
    sample_count = UPSAMPLE_FACTOR * frame_count
    start_offset = UPSAMPLE_FACTOR // 2 - DILATION_SIZE
    waveform = (
        upper_output.reshape(UPSAMPLE_FACTOR * (frame_count + 1), window_width)[
            start_offset : start_offset + sample_count + 2 * DILATION_SIZE
        ]
        + upsample_bias
    )
    step_index = (
        UPSAMPLE_FACTOR * first_frame0
        - DILATION_SIZE
        + jnp.arange(sample_count + 2 * DILATION_SIZE, dtype=jnp.int32)
    )
    inside_samples = ((step_index >= 0) & (step_index < UPSAMPLE_FACTOR * total))[:, None]
    hidden_state = jnp.where(inside_samples, leaky(waveform), 0.0).astype(jnp.bfloat16)
    column_block = jnp.concatenate(
        [
            hidden_state[kernel_index * DILATION_SIZE : kernel_index * DILATION_SIZE + sample_count]
            for kernel_index in range(residual_kernel)
        ],
        axis=1,
    )
    convolve_fn = jnp.dot(column_block, w_res, preferred_element_type=jnp.float32) + b_res
    output_rows = (waveform[DILATION_SIZE : DILATION_SIZE + sample_count] + convolve_fn).astype(
        jnp.bfloat16
    )
    g_wres = contract_rows(column_block, gradient_value)
    g_bres = jnp.sum(gradient_value.astype(jnp.float32), axis=0)
    backward_pass = contract_cols(gradient_value, w_res)
    hidden_gradient = jnp.zeros((sample_count + 2 * DILATION_SIZE, window_width), jnp.float32)
    for kernel_index in range(residual_kernel):
        hidden_gradient = hidden_gradient + jnp.pad(
            backward_pass[:, kernel_index * window_width : (kernel_index + 1) * window_width],
            (
                (
                    kernel_index * DILATION_SIZE,
                    (residual_kernel - 1 - kernel_index) * DILATION_SIZE,
                ),
                (0, 0),
            ),
        )
    waveform_gradient = jnp.where(
        inside_samples, hidden_gradient * negative_slope(waveform), 0.0
    ) + jnp.pad(gradient_value.astype(jnp.float32), ((DILATION_SIZE, DILATION_SIZE), (0, 0)))
    waveform_gradient = waveform_gradient.astype(jnp.bfloat16)
    d_upper = jnp.pad(waveform_gradient, ((start_offset, start_offset), (0, 0))).reshape(
        frame_count + 1, UPSAMPLE_FACTOR, window_width
    )
    zero_row = jnp.zeros((1, UPSAMPLE_FACTOR, window_width), jnp.bfloat16)
    d_taps = jnp.concatenate(
        [
            jnp.concatenate([zero_row, d_upper], axis=0),
            jnp.concatenate([d_upper, zero_row], axis=0),
        ],
        axis=1,
    )
    d_act = ups_backward(d_taps.reshape(frame_count + 2, 2 * UPSAMPLE_FACTOR * window_width))
    d_pre = jnp.where(inside_f, d_act * negative_slope(pre), 0.0).astype(jnp.bfloat16)
    g_wpre = contract_rows(patches, d_pre)
    g_bpre = jnp.sum(d_pre.astype(jnp.float32), axis=0)
    return (output_rows, (g_wpre, g_bpre, g_wres, g_bres))


def tile_rows(value):
    if value.ndim == 2 and value.shape[0] % 8 == 0 and value.shape[1] % 128 == 0:
        r, c = value.shape
        value = value.reshape(r // 8, 8, c // 128, 128).transpose(0, 2, 1, 3)
    return jnp.pad(value.reshape(-1), (0, -value.size % 128)).reshape(-1, 128)


def untile_rows(rows, shape):
    if len(shape) == 2 and shape[0] % 8 == 0 and shape[1] % 128 == 0:
        r, c = shape
        return rows.reshape(r // 8, c // 128, 8, 128).transpose(0, 2, 1, 3).reshape(shape)
    size = 1
    for n in shape:
        size *= n
    return rows.reshape(-1)[:size].reshape(shape)


def butterfly_psum(parts):
    dp_size = lax.axis_size("dp")
    tm_size = lax.axis_size("tm")
    axes = ("dp", "tm")
    levels = [("tm", 1 << k) for k in range(tm_size.bit_length() - 1)]
    levels += [("dp", 1 << k) for k in range(1, dp_size.bit_length() - 1)]
    groups = [levels[i : i + 2] for i in range(0, len(levels), 2)]
    orders = (groups, groups[::-1])
    count = dp_size * tm_size

    def perm_of(step, offset):
        out = []
        for d in range(dp_size):
            for t in range(tm_size):
                idx = {"dp": d, "tm": t}
                for j, (axis, bit) in enumerate(orders[d % 2][step]):
                    if (offset >> j) & 1:
                        idx[axis] = idx[axis] ^ bit
                out.append((d * tm_size + t, idx["dp"] * tm_size + idx["tm"]))
        return out

    core = lax.axis_index("dp") % 2
    position = {"dp": lax.axis_index("dp"), "tm": lax.axis_index("tm")}

    def slot_of(step):
        def one(group):
            return sum(((position[a] // b) % 2) << j for j, (a, b) in enumerate(group))

        return jnp.where(core == 0, one(orders[0][step]), one(orders[1][step]))

    tiles = [tile_rows(p) for p in parts]
    flat = jnp.concatenate([t.reshape(-1) for t in tiles])
    unit = 8 * 128 * count
    padded = -(-flat.shape[0] // unit) * unit
    x = jnp.pad(flat, (0, padded - flat.shape[0])).reshape(padded // 128, 128)
    core_perm = [(i, i ^ tm_size) for i in range(count)]
    half = x.shape[0] // 2
    send = lax.dynamic_slice_in_dim(x, (1 - core) * half, half)
    x = lax.dynamic_slice_in_dim(x, core * half, half) + lax.ppermute(send, axes, core_perm)
    for step in range(len(groups)):
        radix = 1 << len(groups[step])
        piece = x.shape[0] // radix
        slot = slot_of(step)
        total = lax.dynamic_slice_in_dim(x, slot * piece, piece)
        for offset in range(1, radix):
            send = lax.dynamic_slice_in_dim(x, (slot ^ offset) * piece, piece)
            total = total + lax.ppermute(send, axes, perm_of(step, offset))
        x = total
    x = x.astype(jnp.bfloat16)
    for step in reversed(range(len(groups))):
        radix = 1 << len(groups[step])
        slot = slot_of(step)
        got = [x] + [lax.ppermute(x, axes, perm_of(step, o)) for o in range(1, radix)]
        pieces = []
        for q in range(radix):
            source = slot ^ q
            chosen = got[radix - 1]
            for o in range(radix - 2, -1, -1):
                chosen = jnp.where(source == o, got[o], chosen)
            pieces.append(chosen)
        x = jnp.concatenate(pieces)
    recv = lax.ppermute(x, axes, core_perm)
    x = jnp.where(core == 0, jnp.concatenate([x, recv]), jnp.concatenate([recv, x]))
    x = x.astype(jnp.float32)
    out, at = [], 0
    for p, t in zip(parts, tiles):
        out.append(untile_rows(x[at : at + t.shape[0]], p.shape))
        at += t.shape[0]
    return tuple(out)

def ups_functions(w_ups):
    dp_size = lax.axis_size("dp")
    if lax.axis_size("tm") != 2 or dp_size % 2:
        whole = lax.all_gather(w_ups, "tm", axis=0, tiled=True)
        return (
            lambda act: jnp.dot(act, whole, preferred_element_type=jnp.float32),
            lambda d_taps: contract_cols(d_taps, whole),
            whole,
        )
    rows, width = w_ups.shape
    cols = width // 2
    core = lax.axis_index("dp") % 2
    tm = lax.axis_index("tm")
    bounds = [0, 16, rows // 2, rows] if rows % 32 == 0 and rows > 32 else [0, rows]
    swap = [(i, i ^ 1) for i in range(dp_size)]
    got_parts, partner_parts = [], []
    for lo, hi in zip(bounds, bounds[1:]):
        block = w_ups[lo:hi]
        mine = jnp.where(core == 0, block[:, :cols], block[:, cols:])
        got_parts.append(lax.ppermute(mine, "tm", [(0, 1), (1, 0)]))
        partner_parts.append(lax.ppermute(got_parts[-1], "dp", swap))
    low = jnp.concatenate(
        [jnp.where(core == 0, g, p) for g, p in zip(got_parts, partner_parts)]
    )
    high = jnp.concatenate(
        [jnp.where(core == 0, p, g) for g, p in zip(got_parts, partner_parts)]
    )

    def forward(act):
        own_act = lax.dynamic_slice_in_dim(act, tm * rows, rows, axis=1)
        other_act = lax.dynamic_slice_in_dim(act, (1 - tm) * rows, rows, axis=1)
        own = jnp.dot(own_act, w_ups, preferred_element_type=jnp.float32)
        other = jnp.concatenate(
            [
                jnp.dot(other_act, low, preferred_element_type=jnp.float32),
                jnp.dot(other_act, high, preferred_element_type=jnp.float32),
            ],
            axis=1,
        )
        return own + other

    def backward(d_taps):
        own = contract_cols(d_taps, w_ups)
        other = contract_cols(d_taps[:, :cols], low) + contract_cols(d_taps[:, cols:], high)
        return jnp.where(
            tm == 0, jnp.concatenate([own, other], axis=1), jnp.concatenate([other, own], axis=1)
        )

    return forward, backward, got_parts[0]


def on_device(
    src_mel, owner, dst_pos, keep, cotangent, w_pre, b_pre, w_ups, upsample_bias, w_res, b_res
):
    owners_count = lax.axis_size("dp")
    ups_forward, ups_backward, ready = ups_functions(w_ups)
    src_mel, _ = lax.optimization_barrier((src_mel, ready))
    seg_rows = src_mel[0]
    seg_count = seg_rows.shape[0]
    mel_bins = w_pre.shape[0] // KPRE
    pick = jnp.arange(owners_count, dtype=jnp.int32)[:, None] == owner[0][None, :]
    seg_width = seg_rows.shape[1]
    header = jnp.stack([dst_pos[0] + 1, keep[0]], axis=1).astype(jnp.bfloat16)
    seg_ext = jnp.concatenate([seg_rows, header], axis=1)
    outgoing = jnp.dot(
        pick.astype(jnp.bfloat16), seg_ext, preferred_element_type=jnp.float32
    ).astype(jnp.bfloat16)
    arrived = lax.all_to_all(outgoing, "dp", split_axis=0, concat_axis=0, tiled=True)
    slot_code = arrived[:, seg_width].astype(jnp.int32)
    keep_code = arrived[:, seg_width + 1].astype(jnp.int32)
    place = (slot_code - 1)[:, None] == jnp.arange(seg_count, dtype=jnp.int32)[None, :]
    mel_segs = contract_rows(place.astype(jnp.bfloat16), arrived[:, :seg_width]).astype(
        jnp.bfloat16
    )
    keep_segs = jnp.sum(jnp.where(place, keep_code[:, None], 0), axis=0)
    mel = mel_segs.reshape(seg_count * (mel_segs.shape[1] // mel_bins), mel_bins)
    frame_count = mel.shape[0]
    mel_ext = with_halo(mel, (("tm", 0),), KPRE // 2 + 1)
    first_frame0 = lax.axis_index("tm") * frame_count
    total = lax.axis_size("tm") * frame_count
    cot = cotangent[0]
    marks = jnp.repeat(keep_segs, cot.shape[0] // seg_count)
    gradient_value = jnp.where(marks[:, None] > 0, cot, jnp.zeros_like(cot))
    output_rows, grads = local_pass(
        mel_ext,
        gradient_value,
        first_frame0,
        total,
        w_pre,
        b_pre,
        ups_forward,
        ups_backward,
        upsample_bias,
        w_res,
        b_res,
    )
    summed = butterfly_psum(grads)
    return (output_rows[None], summed[0], summed[1], summed[2], summed[3])


def solution(mesh):
    in_specs = (
        P("tm", "dp", None),
        P("tm", "dp"),
        P("tm", "dp"),
        P("tm", "dp"),
        P("dp", "tm", None),
        P(),
        P(),
        P("tm", None),
        P(),
        P(),
        P(),
    )
    out_specs = (P("dp", "tm", None), P(), P(), P(), P())
    return jax.shard_map(
        on_device, mesh=mesh, in_specs=in_specs, out_specs=out_specs, check_vma=False
    )
```

```python
import jax
import jax.numpy as jnp
from jax import lax
from jax.sharding import PartitionSpec as P

KPRE = 7
UPSAMPLE_FACTOR = 8
DILATION_SIZE = 3


def with_halo(block, sides, width):
    for axis, dim in sides:
        count = lax.axis_size(axis)
        forward = [(i, i + 1) for i in range(count - 1)]
        backward = [(target, source) for source, target in forward]
        low = lax.ppermute(
            lax.slice_in_dim(block, block.shape[dim] - width, None, axis=dim), axis, forward
        )
        high = lax.ppermute(lax.slice_in_dim(block, 0, width, axis=dim), axis, backward)
        block = jnp.concatenate([low, block, high], axis=dim)
    return block


def leaky(value):
    return jnp.where(value > 0, value, 0.1 * value)


def negative_slope(value):
    return jnp.where(value > 0, 1.0, 0.1).astype(jnp.float32)


def contract_rows(left, right):
    return lax.dot_general(
        left, right, (((0,), (0,)), ((), ())), preferred_element_type=jnp.float32
    )


def contract_cols(left, right):
    return lax.dot_general(
        left, right, (((1,), (1,)), ((), ())), preferred_element_type=jnp.float32
    )


def local_pass(
    mel_ext,
    gradient_value,
    first_frame0,
    total,
    w_pre,
    b_pre,
    ups_forward,
    ups_backward,
    upsample_bias,
    w_res,
    b_res,
):
    mel_bins = mel_ext.shape[1]
    kpre = w_pre.shape[0] // mel_bins
    edge = kpre // 2 + 1
    frame_count = mel_ext.shape[0] - 2 * edge
    window_width = upsample_bias.shape[0]
    residual_kernel = w_res.shape[0] // window_width
    patches = jnp.concatenate([mel_ext[i : i + frame_count + 2] for i in range(kpre)], axis=1)
    pre = jnp.dot(patches, w_pre, preferred_element_type=jnp.float32) + b_pre
    frame_idx = first_frame0 - 1 + jnp.arange(frame_count + 2, dtype=jnp.int32)
    inside_f = ((frame_idx >= 0) & (frame_idx < total))[:, None]
    act = jnp.where(inside_f, leaky(pre), 0.0).astype(jnp.bfloat16)
    taps = ups_forward(act).reshape(frame_count + 2, 2 * UPSAMPLE_FACTOR, window_width)
    upper_output = taps[1:, :UPSAMPLE_FACTOR] + taps[:-1, UPSAMPLE_FACTOR:]
    sample_count = UPSAMPLE_FACTOR * frame_count
    start_offset = UPSAMPLE_FACTOR // 2 - DILATION_SIZE
    waveform = (
        upper_output.reshape(UPSAMPLE_FACTOR * (frame_count + 1), window_width)[
            start_offset : start_offset + sample_count + 2 * DILATION_SIZE
        ]
        + upsample_bias
    )
    step_index = (
        UPSAMPLE_FACTOR * first_frame0
        - DILATION_SIZE
        + jnp.arange(sample_count + 2 * DILATION_SIZE, dtype=jnp.int32)
    )
    inside_samples = ((step_index >= 0) & (step_index < UPSAMPLE_FACTOR * total))[:, None]
    hidden_state = jnp.where(inside_samples, leaky(waveform), 0.0).astype(jnp.bfloat16)
    column_block = jnp.concatenate(
        [
            hidden_state[kernel_index * DILATION_SIZE : kernel_index * DILATION_SIZE + sample_count]
            for kernel_index in range(residual_kernel)
        ],
        axis=1,
    )
    convolve_fn = jnp.dot(column_block, w_res, preferred_element_type=jnp.float32) + b_res
    output_rows = (waveform[DILATION_SIZE : DILATION_SIZE + sample_count] + convolve_fn).astype(
        jnp.bfloat16
    )
    g_wres = contract_rows(column_block, gradient_value)
    g_bres = jnp.sum(gradient_value.astype(jnp.float32), axis=0)
    backward_pass = contract_cols(gradient_value, w_res)
    hidden_gradient = jnp.zeros((sample_count + 2 * DILATION_SIZE, window_width), jnp.float32)
    for kernel_index in range(residual_kernel):
        hidden_gradient = hidden_gradient + jnp.pad(
            backward_pass[:, kernel_index * window_width : (kernel_index + 1) * window_width],
            (
                (
                    kernel_index * DILATION_SIZE,
                    (residual_kernel - 1 - kernel_index) * DILATION_SIZE,
                ),
                (0, 0),
            ),
        )
    waveform_gradient = jnp.where(
        inside_samples, hidden_gradient * negative_slope(waveform), 0.0
    ) + jnp.pad(gradient_value.astype(jnp.float32), ((DILATION_SIZE, DILATION_SIZE), (0, 0)))
    waveform_gradient = waveform_gradient.astype(jnp.bfloat16)
    d_upper = jnp.pad(waveform_gradient, ((start_offset, start_offset), (0, 0))).reshape(
        frame_count + 1, UPSAMPLE_FACTOR, window_width
    )
    zero_row = jnp.zeros((1, UPSAMPLE_FACTOR, window_width), jnp.bfloat16)
    d_taps = jnp.concatenate(
        [
            jnp.concatenate([zero_row, d_upper], axis=0),
            jnp.concatenate([d_upper, zero_row], axis=0),
        ],
        axis=1,
    )
    d_act = ups_backward(d_taps.reshape(frame_count + 2, 2 * UPSAMPLE_FACTOR * window_width))
    d_pre = jnp.where(inside_f, d_act * negative_slope(pre), 0.0).astype(jnp.bfloat16)
    g_wpre = contract_rows(patches, d_pre)
    g_bpre = jnp.sum(d_pre.astype(jnp.float32), axis=0)
    return (output_rows, (g_wpre, g_bpre, g_wres, g_bres))


def tile_rows(value):
    if value.ndim == 2 and value.shape[0] % 8 == 0 and value.shape[1] % 128 == 0:
        r, c = value.shape
        value = value.reshape(r // 8, 8, c // 128, 128).transpose(0, 2, 1, 3)
    return jnp.pad(value.reshape(-1), (0, -value.size % 128)).reshape(-1, 128)


def untile_rows(rows, shape):
    if len(shape) == 2 and shape[0] % 8 == 0 and shape[1] % 128 == 0:
        r, c = shape
        return rows.reshape(r // 8, c // 128, 8, 128).transpose(0, 2, 1, 3).reshape(shape)
    size = 1
    for n in shape:
        size *= n
    return rows.reshape(-1)[:size].reshape(shape)


def butterfly_psum(parts):
    dp_size = lax.axis_size("dp")
    tm_size = lax.axis_size("tm")
    axes = ("dp", "tm")
    levels = [("tm", 1 << k) for k in range(tm_size.bit_length() - 1)]
    levels += [("dp", 1 << k) for k in range(1, dp_size.bit_length() - 1)]
    groups = [levels[i : i + 2] for i in range(0, len(levels), 2)]
    orders = (groups, groups)
    count = dp_size * tm_size

    def perm_of(step, offset):
        out = []
        for d in range(dp_size):
            for t in range(tm_size):
                idx = {"dp": d, "tm": t}
                for j, (axis, bit) in enumerate(orders[d % 2][step]):
                    if (offset >> j) & 1:
                        idx[axis] = idx[axis] ^ bit
                out.append((d * tm_size + t, idx["dp"] * tm_size + idx["tm"]))
        return out

    core = lax.axis_index("dp") % 2
    position = {"dp": lax.axis_index("dp"), "tm": lax.axis_index("tm")}

    def slot_of(step):
        def one(group):
            return sum(((position[a] // b) % 2) << j for j, (a, b) in enumerate(group))

        return jnp.where(core == 0, one(orders[0][step]), one(orders[1][step]))

    tiles = [tile_rows(p) for p in parts]
    flat = jnp.concatenate([t.reshape(-1) for t in tiles])
    unit = 8 * 128 * count
    padded = -(-flat.shape[0] // unit) * unit
    x = jnp.pad(flat, (0, padded - flat.shape[0])).reshape(padded // 128, 128)
    core_perm = [(i, i ^ tm_size) for i in range(count)]
    half = x.shape[0] // 2
    send = lax.dynamic_slice_in_dim(x, (1 - core) * half, half)
    x = lax.dynamic_slice_in_dim(x, core * half, half) + lax.ppermute(send, axes, core_perm)
    for step in range(len(groups)):
        radix = 1 << len(groups[step])
        piece = x.shape[0] // radix
        slot = slot_of(step)
        total = lax.dynamic_slice_in_dim(x, slot * piece, piece)
        for offset in range(1, radix):
            send = lax.dynamic_slice_in_dim(x, (slot ^ offset) * piece, piece)
            total = total + lax.ppermute(send, axes, perm_of(step, offset))
        x = total
    for step in reversed(range(len(groups))):
        radix = 1 << len(groups[step])
        slot = slot_of(step)
        got = [x] + [lax.ppermute(x, axes, perm_of(step, o)) for o in range(1, radix)]
        pieces = []
        for q in range(radix):
            source = slot ^ q
            chosen = got[radix - 1]
            for o in range(radix - 2, -1, -1):
                chosen = jnp.where(source == o, got[o], chosen)
            pieces.append(chosen)
        x = jnp.concatenate(pieces)
    recv = lax.ppermute(x, axes, core_perm)
    x = jnp.where(core == 0, jnp.concatenate([x, recv]), jnp.concatenate([recv, x]))
    out, at = [], 0
    for p, t in zip(parts, tiles):
        out.append(untile_rows(x[at : at + t.shape[0]], p.shape))
        at += t.shape[0]
    return tuple(out)

def ups_functions(w_ups):
    dp_size = lax.axis_size("dp")
    if lax.axis_size("tm") != 2 or dp_size % 2:
        whole = lax.all_gather(w_ups, "tm", axis=0, tiled=True)
        return (
            lambda act: jnp.dot(act, whole, preferred_element_type=jnp.float32),
            lambda d_taps: contract_cols(d_taps, whole),
            whole,
        )
    rows, width = w_ups.shape
    cols = width // 2
    core = lax.axis_index("dp") % 2
    tm = lax.axis_index("tm")
    bounds = [0, 16, rows // 2, rows] if rows % 32 == 0 and rows > 32 else [0, rows]
    swap = [(i, i ^ 1) for i in range(dp_size)]
    got_parts, partner_parts = [], []
    for lo, hi in zip(bounds, bounds[1:]):
        block = w_ups[lo:hi]
        mine = jnp.where(core == 0, block[:, :cols], block[:, cols:])
        got_parts.append(lax.ppermute(mine, "tm", [(0, 1), (1, 0)]))
        partner_parts.append(lax.ppermute(got_parts[-1], "dp", swap))
    low = jnp.concatenate(
        [jnp.where(core == 0, g, p) for g, p in zip(got_parts, partner_parts)]
    )
    high = jnp.concatenate(
        [jnp.where(core == 0, p, g) for g, p in zip(got_parts, partner_parts)]
    )

    def forward(act):
        own_act = lax.dynamic_slice_in_dim(act, tm * rows, rows, axis=1)
        other_act = lax.dynamic_slice_in_dim(act, (1 - tm) * rows, rows, axis=1)
        own = jnp.dot(own_act, w_ups, preferred_element_type=jnp.float32)
        other = jnp.concatenate(
            [
                jnp.dot(other_act, low, preferred_element_type=jnp.float32),
                jnp.dot(other_act, high, preferred_element_type=jnp.float32),
            ],
            axis=1,
        )
        return own + other

    def backward(d_taps):
        own = contract_cols(d_taps, w_ups)
        other = contract_cols(d_taps[:, :cols], low) + contract_cols(d_taps[:, cols:], high)
        return jnp.where(
            tm == 0, jnp.concatenate([own, other], axis=1), jnp.concatenate([other, own], axis=1)
        )

    return forward, backward, got_parts[0]


def on_device(
    src_mel, owner, dst_pos, keep, cotangent, w_pre, b_pre, w_ups, upsample_bias, w_res, b_res
):
    owners_count = lax.axis_size("dp")
    ups_forward, ups_backward, ready = ups_functions(w_ups)
    src_mel, _ = lax.optimization_barrier((src_mel, ready))
    seg_rows = src_mel[0]
    seg_count = seg_rows.shape[0]
    mel_bins = w_pre.shape[0] // KPRE
    pick = jnp.arange(owners_count, dtype=jnp.int32)[:, None] == owner[0][None, :]
    seg_width = seg_rows.shape[1]
    header = jnp.stack([dst_pos[0] + 1, keep[0]], axis=1).astype(jnp.bfloat16)
    seg_ext = jnp.concatenate([seg_rows, header], axis=1)
    outgoing = jnp.dot(
        pick.astype(jnp.bfloat16), seg_ext, preferred_element_type=jnp.float32
    ).astype(jnp.bfloat16)
    arrived = lax.all_to_all(outgoing, "dp", split_axis=0, concat_axis=0, tiled=True)
    slot_code = arrived[:, seg_width].astype(jnp.int32)
    keep_code = arrived[:, seg_width + 1].astype(jnp.int32)
    place = (slot_code - 1)[:, None] == jnp.arange(seg_count, dtype=jnp.int32)[None, :]
    mel_segs = contract_rows(place.astype(jnp.bfloat16), arrived[:, :seg_width]).astype(
        jnp.bfloat16
    )
    keep_segs = jnp.sum(jnp.where(place, keep_code[:, None], 0), axis=0)
    mel = mel_segs.reshape(seg_count * (mel_segs.shape[1] // mel_bins), mel_bins)
    frame_count = mel.shape[0]
    mel_ext = with_halo(mel, (("tm", 0),), KPRE // 2 + 1)
    first_frame0 = lax.axis_index("tm") * frame_count
    total = lax.axis_size("tm") * frame_count
    cot = cotangent[0]
    marks = jnp.repeat(keep_segs, cot.shape[0] // seg_count)
    gradient_value = jnp.where(marks[:, None] > 0, cot, jnp.zeros_like(cot))
    output_rows, grads = local_pass(
        mel_ext,
        gradient_value,
        first_frame0,
        total,
        w_pre,
        b_pre,
        ups_forward,
        ups_backward,
        upsample_bias,
        w_res,
        b_res,
    )
    summed = butterfly_psum(grads)
    return (output_rows[None], summed[0], summed[1], summed[2], summed[3])


def solution(mesh):
    in_specs = (
        P("tm", "dp", None),
        P("tm", "dp"),
        P("tm", "dp"),
        P("tm", "dp"),
        P("dp", "tm", None),
        P(),
        P(),
        P("tm", None),
        P(),
        P(),
        P(),
    )
    out_specs = (P("dp", "tm", None), P(), P(), P(), P())
    return jax.shard_map(
        on_device, mesh=mesh, in_specs=in_specs, out_specs=out_specs, check_vma=False
    )
```

```python
import jax
import jax.numpy as jnp
from jax import lax
from jax.sharding import PartitionSpec as P

KPRE = 7
UPSAMPLE_FACTOR = 8
DILATION_SIZE = 3


def with_halo(block, sides, width):
    for axis, dim in sides:
        count = lax.axis_size(axis)
        forward = [(i, i + 1) for i in range(count - 1)]
        backward = [(target, source) for source, target in forward]
        low = lax.ppermute(
            lax.slice_in_dim(block, block.shape[dim] - width, None, axis=dim), axis, forward
        )
        high = lax.ppermute(lax.slice_in_dim(block, 0, width, axis=dim), axis, backward)
        block = jnp.concatenate([low, block, high], axis=dim)
    return block


def leaky(value):
    return jnp.where(value > 0, value, 0.1 * value)


def negative_slope(value):
    return jnp.where(value > 0, 1.0, 0.1).astype(jnp.float32)


def contract_rows(left, right):
    return lax.dot_general(
        left, right, (((0,), (0,)), ((), ())), preferred_element_type=jnp.float32
    )


def contract_cols(left, right):
    return lax.dot_general(
        left, right, (((1,), (1,)), ((), ())), preferred_element_type=jnp.float32
    )


def local_pass(
    mel_ext,
    gradient_value,
    first_frame0,
    total,
    w_pre,
    b_pre,
    ups_forward,
    ups_backward,
    upsample_bias,
    w_res,
    b_res,
):
    mel_bins = mel_ext.shape[1]
    kpre = w_pre.shape[0] // mel_bins
    edge = kpre // 2 + 1
    frame_count = mel_ext.shape[0] - 2 * edge
    window_width = upsample_bias.shape[0]
    residual_kernel = w_res.shape[0] // window_width
    patches = jnp.concatenate([mel_ext[i : i + frame_count + 2] for i in range(kpre)], axis=1)
    pre = jnp.dot(patches, w_pre, preferred_element_type=jnp.float32) + b_pre
    frame_idx = first_frame0 - 1 + jnp.arange(frame_count + 2, dtype=jnp.int32)
    inside_f = ((frame_idx >= 0) & (frame_idx < total))[:, None]
    act = jnp.where(inside_f, leaky(pre), 0.0).astype(jnp.bfloat16)
    taps = ups_forward(act).reshape(frame_count + 2, 2 * UPSAMPLE_FACTOR, window_width)
    upper_output = taps[1:, :UPSAMPLE_FACTOR] + taps[:-1, UPSAMPLE_FACTOR:]
    sample_count = UPSAMPLE_FACTOR * frame_count
    start_offset = UPSAMPLE_FACTOR // 2 - DILATION_SIZE
    waveform = (
        upper_output.reshape(UPSAMPLE_FACTOR * (frame_count + 1), window_width)[
            start_offset : start_offset + sample_count + 2 * DILATION_SIZE
        ]
        + upsample_bias
    )
    step_index = (
        UPSAMPLE_FACTOR * first_frame0
        - DILATION_SIZE
        + jnp.arange(sample_count + 2 * DILATION_SIZE, dtype=jnp.int32)
    )
    inside_samples = ((step_index >= 0) & (step_index < UPSAMPLE_FACTOR * total))[:, None]
    hidden_state = jnp.where(inside_samples, leaky(waveform), 0.0).astype(jnp.bfloat16)
    column_block = jnp.concatenate(
        [
            hidden_state[kernel_index * DILATION_SIZE : kernel_index * DILATION_SIZE + sample_count]
            for kernel_index in range(residual_kernel)
        ],
        axis=1,
    )
    convolve_fn = jnp.dot(column_block, w_res, preferred_element_type=jnp.float32) + b_res
    output_rows = (waveform[DILATION_SIZE : DILATION_SIZE + sample_count] + convolve_fn).astype(
        jnp.bfloat16
    )
    g_wres = contract_rows(column_block, gradient_value)
    g_bres = jnp.sum(gradient_value.astype(jnp.float32), axis=0)
    backward_pass = contract_cols(gradient_value, w_res)
    hidden_gradient = jnp.zeros((sample_count + 2 * DILATION_SIZE, window_width), jnp.float32)
    for kernel_index in range(residual_kernel):
        hidden_gradient = hidden_gradient + jnp.pad(
            backward_pass[:, kernel_index * window_width : (kernel_index + 1) * window_width],
            (
                (
                    kernel_index * DILATION_SIZE,
                    (residual_kernel - 1 - kernel_index) * DILATION_SIZE,
                ),
                (0, 0),
            ),
        )
    waveform_gradient = jnp.where(
        inside_samples, hidden_gradient * negative_slope(waveform), 0.0
    ) + jnp.pad(gradient_value.astype(jnp.float32), ((DILATION_SIZE, DILATION_SIZE), (0, 0)))
    waveform_gradient = waveform_gradient.astype(jnp.bfloat16)
    d_upper = jnp.pad(waveform_gradient, ((start_offset, start_offset), (0, 0))).reshape(
        frame_count + 1, UPSAMPLE_FACTOR, window_width
    )
    zero_row = jnp.zeros((1, UPSAMPLE_FACTOR, window_width), jnp.bfloat16)
    d_taps = jnp.concatenate(
        [
            jnp.concatenate([zero_row, d_upper], axis=0),
            jnp.concatenate([d_upper, zero_row], axis=0),
        ],
        axis=1,
    )
    d_act = ups_backward(d_taps.reshape(frame_count + 2, 2 * UPSAMPLE_FACTOR * window_width))
    d_pre = jnp.where(inside_f, d_act * negative_slope(pre), 0.0).astype(jnp.bfloat16)
    g_wpre = contract_rows(patches, d_pre)
    g_bpre = jnp.sum(d_pre.astype(jnp.float32), axis=0)
    return (output_rows, (g_wpre, g_bpre, g_wres, g_bres))


def tile_rows(value):
    if value.ndim == 2 and value.shape[0] % 8 == 0 and value.shape[1] % 128 == 0:
        r, c = value.shape
        value = value.reshape(r // 8, 8, c // 128, 128).transpose(0, 2, 1, 3)
    return jnp.pad(value.reshape(-1), (0, -value.size % 128)).reshape(-1, 128)


def untile_rows(rows, shape):
    if len(shape) == 2 and shape[0] % 8 == 0 and shape[1] % 128 == 0:
        r, c = shape
        return rows.reshape(r // 8, c // 128, 8, 128).transpose(0, 2, 1, 3).reshape(shape)
    size = 1
    for n in shape:
        size *= n
    return rows.reshape(-1)[:size].reshape(shape)


def butterfly_psum(parts):
    dp_size = lax.axis_size("dp")
    tm_size = lax.axis_size("tm")
    axes = ("dp", "tm")
    levels = [("tm", 1 << k) for k in range(tm_size.bit_length() - 1)]
    levels += [("dp", 1 << k) for k in range(1, dp_size.bit_length() - 1)]
    groups = [levels[i : i + 2] for i in range(0, len(levels), 2)]
    orders = (groups, groups[::-1])
    count = dp_size * tm_size

    def perm_of(step, offset):
        out = []
        for d in range(dp_size):
            for t in range(tm_size):
                idx = {"dp": d, "tm": t}
                for j, (axis, bit) in enumerate(orders[d % 2][step]):
                    if (offset >> j) & 1:
                        idx[axis] = idx[axis] ^ bit
                out.append((d * tm_size + t, idx["dp"] * tm_size + idx["tm"]))
        return out

    core = lax.axis_index("dp") % 2
    position = {"dp": lax.axis_index("dp"), "tm": lax.axis_index("tm")}

    def slot_of(step):
        def one(group):
            return sum(((position[a] // b) % 2) << j for j, (a, b) in enumerate(group))

        return jnp.where(core == 0, one(orders[0][step]), one(orders[1][step]))

    tiles = [tile_rows(p) for p in parts]
    flat = jnp.concatenate([t.reshape(-1) for t in tiles])
    unit = 8 * 128 * count
    padded = -(-flat.shape[0] // unit) * unit
    x = jnp.pad(flat, (0, padded - flat.shape[0])).reshape(padded // 128, 128)
    core_perm = [(i, i ^ tm_size) for i in range(count)]
    half = x.shape[0] // 2
    send = lax.dynamic_slice_in_dim(x, (1 - core) * half, half)
    x = lax.dynamic_slice_in_dim(x, core * half, half) + lax.ppermute(send, axes, core_perm)
    for step in range(len(groups)):
        radix = 1 << len(groups[step])
        piece = x.shape[0] // radix
        slot = slot_of(step)
        total = lax.dynamic_slice_in_dim(x, slot * piece, piece)
        for offset in range(1, radix):
            send = lax.dynamic_slice_in_dim(x, (slot ^ offset) * piece, piece)
            total = total + lax.ppermute(send, axes, perm_of(step, offset))
        x = total
    for step in reversed(range(len(groups))):
        radix = 1 << len(groups[step])
        slot = slot_of(step)
        got = [x] + [lax.ppermute(x, axes, perm_of(step, o)) for o in range(1, radix)]
        pieces = []
        for q in range(radix):
            source = slot ^ q
            chosen = got[radix - 1]
            for o in range(radix - 2, -1, -1):
                chosen = jnp.where(source == o, got[o], chosen)
            pieces.append(chosen)
        x = jnp.concatenate(pieces)
    recv = lax.ppermute(x, axes, core_perm)
    x = jnp.where(core == 0, jnp.concatenate([x, recv]), jnp.concatenate([recv, x]))
    out, at = [], 0
    for p, t in zip(parts, tiles):
        out.append(untile_rows(x[at : at + t.shape[0]], p.shape))
        at += t.shape[0]
    return tuple(out)

def ups_functions(w_ups):
    dp_size = lax.axis_size("dp")
    if lax.axis_size("tm") != 2 or dp_size % 2:
        whole = lax.all_gather(w_ups, "tm", axis=0, tiled=True)
        return (
            lambda act: jnp.dot(act, whole, preferred_element_type=jnp.float32),
            lambda d_taps: contract_cols(d_taps, whole),
            whole,
        )
    rows, width = w_ups.shape
    core = lax.axis_index("dp") % 2
    tm = lax.axis_index("tm")
    half = rows // 2
    bounds = [0, 16, half // 2, half] if half % 32 == 0 and half > 32 else [0, half]
    swap = [(i, i ^ 1) for i in range(dp_size)]
    got_parts, partner_parts = [], []
    for lo, hi in zip(bounds, bounds[1:]):
        mine = lax.dynamic_slice_in_dim(w_ups, core * half + lo, hi - lo, axis=0)
        got_parts.append(lax.ppermute(mine, "tm", [(0, 1), (1, 0)]))
        partner_parts.append(lax.ppermute(got_parts[-1], "dp", swap))
    low = jnp.concatenate(
        [jnp.where(core == 0, g, p) for g, p in zip(got_parts, partner_parts)]
    )
    high = jnp.concatenate(
        [jnp.where(core == 0, p, g) for g, p in zip(got_parts, partner_parts)]
    )

    def forward(act):
        own_act = lax.dynamic_slice_in_dim(act, tm * rows, rows, axis=1)
        other_act = lax.dynamic_slice_in_dim(act, (1 - tm) * rows, rows, axis=1)
        own = jnp.dot(own_act, w_ups, preferred_element_type=jnp.float32)
        other = jnp.dot(
            other_act[:, :half], low, preferred_element_type=jnp.float32
        ) + jnp.dot(other_act[:, half:], high, preferred_element_type=jnp.float32)
        return own + other

    def backward(d_taps):
        own = contract_cols(d_taps, w_ups)
        other = jnp.concatenate([contract_cols(d_taps, low), contract_cols(d_taps, high)], axis=1)
        return jnp.where(
            tm == 0, jnp.concatenate([own, other], axis=1), jnp.concatenate([other, own], axis=1)
        )

    return forward, backward, got_parts[0]


def on_device(
    src_mel, owner, dst_pos, keep, cotangent, w_pre, b_pre, w_ups, upsample_bias, w_res, b_res
):
    owners_count = lax.axis_size("dp")
    ups_forward, ups_backward, ready = ups_functions(w_ups)
    src_mel, _ = lax.optimization_barrier((src_mel, ready))
    seg_rows = src_mel[0]
    seg_count = seg_rows.shape[0]
    mel_bins = w_pre.shape[0] // KPRE
    pick = jnp.arange(owners_count, dtype=jnp.int32)[:, None] == owner[0][None, :]
    seg_width = seg_rows.shape[1]
    header = jnp.stack([dst_pos[0] + 1, keep[0]], axis=1).astype(jnp.bfloat16)
    seg_ext = jnp.concatenate([seg_rows, header], axis=1)
    outgoing = jnp.dot(
        pick.astype(jnp.bfloat16), seg_ext, preferred_element_type=jnp.float32
    ).astype(jnp.bfloat16)
    arrived = lax.all_to_all(outgoing, "dp", split_axis=0, concat_axis=0, tiled=True)
    slot_code = arrived[:, seg_width].astype(jnp.int32)
    keep_code = arrived[:, seg_width + 1].astype(jnp.int32)
    place = (slot_code - 1)[:, None] == jnp.arange(seg_count, dtype=jnp.int32)[None, :]
    mel_segs = contract_rows(place.astype(jnp.bfloat16), arrived[:, :seg_width]).astype(
        jnp.bfloat16
    )
    keep_segs = jnp.sum(jnp.where(place, keep_code[:, None], 0), axis=0)
    mel = mel_segs.reshape(seg_count * (mel_segs.shape[1] // mel_bins), mel_bins)
    frame_count = mel.shape[0]
    mel_ext = with_halo(mel, (("tm", 0),), KPRE // 2 + 1)
    first_frame0 = lax.axis_index("tm") * frame_count
    total = lax.axis_size("tm") * frame_count
    cot = cotangent[0]
    marks = jnp.repeat(keep_segs, cot.shape[0] // seg_count)
    gradient_value = jnp.where(marks[:, None] > 0, cot, jnp.zeros_like(cot))
    output_rows, grads = local_pass(
        mel_ext,
        gradient_value,
        first_frame0,
        total,
        w_pre,
        b_pre,
        ups_forward,
        ups_backward,
        upsample_bias,
        w_res,
        b_res,
    )
    summed = butterfly_psum(grads)
    return (output_rows[None], summed[0], summed[1], summed[2], summed[3])


def solution(mesh):
    in_specs = (
        P("tm", "dp", None),
        P("tm", "dp"),
        P("tm", "dp"),
        P("tm", "dp"),
        P("dp", "tm", None),
        P(),
        P(),
        P("tm", None),
        P(),
        P(),
        P(),
    )
    out_specs = (P("dp", "tm", None), P(), P(), P(), P())
    return jax.shard_map(
        on_device, mesh=mesh, in_specs=in_specs, out_specs=out_specs, check_vma=False
    )
```

```python
import jax
import jax.numpy as jnp
from jax import lax
from jax.sharding import PartitionSpec as P

KPRE = 7
UPSAMPLE_FACTOR = 8
DILATION_SIZE = 3


def with_halo(block, sides, width):
    for axis, dim in sides:
        count = lax.axis_size(axis)
        forward = [(i, i + 1) for i in range(count - 1)]
        backward = [(target, source) for source, target in forward]
        low = lax.ppermute(
            lax.slice_in_dim(block, block.shape[dim] - width, None, axis=dim), axis, forward
        )
        high = lax.ppermute(lax.slice_in_dim(block, 0, width, axis=dim), axis, backward)
        block = jnp.concatenate([low, block, high], axis=dim)
    return block


def leaky(value):
    return jnp.where(value > 0, value, 0.1 * value)


def negative_slope(value):
    return jnp.where(value > 0, 1.0, 0.1).astype(jnp.float32)


def contract_rows(left, right):
    return lax.dot_general(
        left, right, (((0,), (0,)), ((), ())), preferred_element_type=jnp.float32
    )


def contract_cols(left, right):
    return lax.dot_general(
        left, right, (((1,), (1,)), ((), ())), preferred_element_type=jnp.float32
    )


def local_pass(
    mel_ext,
    gradient_value,
    first_frame0,
    total,
    w_pre,
    b_pre,
    ups_forward,
    ups_backward,
    upsample_bias,
    w_res,
    b_res,
):
    mel_bins = mel_ext.shape[1]
    kpre = w_pre.shape[0] // mel_bins
    edge = kpre // 2 + 1
    frame_count = mel_ext.shape[0] - 2 * edge
    window_width = upsample_bias.shape[0]
    residual_kernel = w_res.shape[0] // window_width
    patches = jnp.concatenate([mel_ext[i : i + frame_count + 2] for i in range(kpre)], axis=1)
    pre = jnp.dot(patches, w_pre, preferred_element_type=jnp.float32) + b_pre
    frame_idx = first_frame0 - 1 + jnp.arange(frame_count + 2, dtype=jnp.int32)
    inside_f = ((frame_idx >= 0) & (frame_idx < total))[:, None]
    act = jnp.where(inside_f, leaky(pre), 0.0).astype(jnp.bfloat16)
    taps = ups_forward(act).reshape(frame_count + 2, 2 * UPSAMPLE_FACTOR, window_width)
    upper_output = taps[1:, :UPSAMPLE_FACTOR] + taps[:-1, UPSAMPLE_FACTOR:]
    sample_count = UPSAMPLE_FACTOR * frame_count
    start_offset = UPSAMPLE_FACTOR // 2 - DILATION_SIZE
    waveform = (
        upper_output.reshape(UPSAMPLE_FACTOR * (frame_count + 1), window_width)[
            start_offset : start_offset + sample_count + 2 * DILATION_SIZE
        ]
        + upsample_bias
    )
    step_index = (
        UPSAMPLE_FACTOR * first_frame0
        - DILATION_SIZE
        + jnp.arange(sample_count + 2 * DILATION_SIZE, dtype=jnp.int32)
    )
    inside_samples = ((step_index >= 0) & (step_index < UPSAMPLE_FACTOR * total))[:, None]
    hidden_state = jnp.where(inside_samples, leaky(waveform), 0.0).astype(jnp.bfloat16)
    column_block = jnp.concatenate(
        [
            hidden_state[kernel_index * DILATION_SIZE : kernel_index * DILATION_SIZE + sample_count]
            for kernel_index in range(residual_kernel)
        ],
        axis=1,
    )
    convolve_fn = jnp.dot(column_block, w_res, preferred_element_type=jnp.float32) + b_res
    output_rows = (waveform[DILATION_SIZE : DILATION_SIZE + sample_count] + convolve_fn).astype(
        jnp.bfloat16
    )
    g_wres = contract_rows(column_block, gradient_value)
    g_bres = jnp.sum(gradient_value.astype(jnp.float32), axis=0)
    backward_pass = contract_cols(gradient_value, w_res)
    hidden_gradient = jnp.zeros((sample_count + 2 * DILATION_SIZE, window_width), jnp.float32)
    for kernel_index in range(residual_kernel):
        hidden_gradient = hidden_gradient + jnp.pad(
            backward_pass[:, kernel_index * window_width : (kernel_index + 1) * window_width],
            (
                (
                    kernel_index * DILATION_SIZE,
                    (residual_kernel - 1 - kernel_index) * DILATION_SIZE,
                ),
                (0, 0),
            ),
        )
    waveform_gradient = jnp.where(
        inside_samples, hidden_gradient * negative_slope(waveform), 0.0
    ) + jnp.pad(gradient_value.astype(jnp.float32), ((DILATION_SIZE, DILATION_SIZE), (0, 0)))
    waveform_gradient = waveform_gradient.astype(jnp.bfloat16)
    d_upper = jnp.pad(waveform_gradient, ((start_offset, start_offset), (0, 0))).reshape(
        frame_count + 1, UPSAMPLE_FACTOR, window_width
    )
    zero_row = jnp.zeros((1, UPSAMPLE_FACTOR, window_width), jnp.bfloat16)
    d_taps = jnp.concatenate(
        [
            jnp.concatenate([zero_row, d_upper], axis=0),
            jnp.concatenate([d_upper, zero_row], axis=0),
        ],
        axis=1,
    )
    d_act = ups_backward(d_taps.reshape(frame_count + 2, 2 * UPSAMPLE_FACTOR * window_width))
    d_pre = jnp.where(inside_f, d_act * negative_slope(pre), 0.0).astype(jnp.bfloat16)
    g_wpre = contract_rows(patches, d_pre)
    g_bpre = jnp.sum(d_pre.astype(jnp.float32), axis=0)
    return (output_rows, (g_wpre, g_bpre, g_wres, g_bres))


def tile_rows(value):
    if value.ndim == 2 and value.shape[0] % 8 == 0 and value.shape[1] % 128 == 0:
        r, c = value.shape
        value = value.reshape(r // 8, 8, c // 128, 128).transpose(0, 2, 1, 3)
    return jnp.pad(value.reshape(-1), (0, -value.size % 128)).reshape(-1, 128)


def untile_rows(rows, shape):
    if len(shape) == 2 and shape[0] % 8 == 0 and shape[1] % 128 == 0:
        r, c = shape
        return rows.reshape(r // 8, c // 128, 8, 128).transpose(0, 2, 1, 3).reshape(shape)
    size = 1
    for n in shape:
        size *= n
    return rows.reshape(-1)[:size].reshape(shape)


def butterfly_psum(parts):
    dp_size = lax.axis_size("dp")
    tm_size = lax.axis_size("tm")
    axes = ("dp", "tm")
    levels = [("tm", 1 << k) for k in range(tm_size.bit_length() - 1)]
    levels += [("dp", 1 << k) for k in range(1, dp_size.bit_length() - 1)]
    groups = [levels[i : i + 2] for i in range(0, len(levels), 2)]
    orders = (groups, groups[::-1])
    count = dp_size * tm_size

    def perm_of(step, offset):
        out = []
        for d in range(dp_size):
            for t in range(tm_size):
                idx = {"dp": d, "tm": t}
                for j, (axis, bit) in enumerate(orders[d % 2][step]):
                    if (offset >> j) & 1:
                        idx[axis] = idx[axis] ^ bit
                out.append((d * tm_size + t, idx["dp"] * tm_size + idx["tm"]))
        return out

    core = lax.axis_index("dp") % 2
    position = {"dp": lax.axis_index("dp"), "tm": lax.axis_index("tm")}

    def slot_of(step):
        def one(group):
            return sum(((position[a] // b) % 2) << j for j, (a, b) in enumerate(group))

        return jnp.where(core == 0, one(orders[0][step]), one(orders[1][step]))

    tiles = [tile_rows(p) for p in parts]
    flat = jnp.concatenate([t.reshape(-1) for t in tiles])
    unit = 8 * 128 * count
    padded = -(-flat.shape[0] // unit) * unit
    x = jnp.pad(flat, (0, padded - flat.shape[0])).reshape(padded // 128, 128)
    core_perm = [(i, i ^ tm_size) for i in range(count)]
    half = x.shape[0] // 2
    send = lax.dynamic_slice_in_dim(x, (1 - core) * half, half)
    x = lax.dynamic_slice_in_dim(x, core * half, half) + lax.ppermute(send, axes, core_perm)
    for step in range(len(groups)):
        radix = 1 << len(groups[step])
        piece = x.shape[0] // radix
        slot = slot_of(step)
        total = lax.dynamic_slice_in_dim(x, slot * piece, piece)
        for offset in range(1, radix):
            send = lax.dynamic_slice_in_dim(x, (slot ^ offset) * piece, piece)
            total = total + lax.ppermute(send, axes, perm_of(step, offset))
        x = total
    for step in reversed(range(len(groups))):
        radix = 1 << len(groups[step])
        slot = slot_of(step)
        got = [x] + [lax.ppermute(x, axes, perm_of(step, o)) for o in range(1, radix)]
        pieces = []
        for q in range(radix):
            source = slot ^ q
            chosen = got[radix - 1]
            for o in range(radix - 2, -1, -1):
                chosen = jnp.where(source == o, got[o], chosen)
            pieces.append(chosen)
        x = jnp.concatenate(pieces)
    recv = lax.ppermute(x, axes, core_perm)
    x = jnp.where(core == 0, jnp.concatenate([x, recv]), jnp.concatenate([recv, x]))
    out, at = [], 0
    for p, t in zip(parts, tiles):
        out.append(untile_rows(x[at : at + t.shape[0]], p.shape))
        at += t.shape[0]
    return tuple(out)

def ups_functions(w_ups):
    dp_size = lax.axis_size("dp")
    if lax.axis_size("tm") != 2 or dp_size % 2:
        whole = lax.all_gather(w_ups, "tm", axis=0, tiled=True)
        return (
            lambda act: jnp.dot(act, whole, preferred_element_type=jnp.float32),
            lambda d_taps: contract_cols(d_taps, whole),
            whole,
        )
    rows, width = w_ups.shape
    cols = width // 2
    core = lax.axis_index("dp") % 2
    tm = lax.axis_index("tm")
    bounds = [0, 16, rows // 2, rows] if rows % 32 == 0 and rows > 32 else [0, rows]
    swap = [(i, i ^ 1) for i in range(dp_size)]
    got_parts, partner_parts = [], []
    mine = jnp.where(core == 0, w_ups[:, :cols], w_ups[:, cols:])
    for lo, hi in zip(bounds, bounds[1:]):
        got_parts.append(lax.ppermute(mine[lo:hi], "tm", [(0, 1), (1, 0)]))
        partner_parts.append(lax.ppermute(got_parts[-1], "dp", swap))
    low = jnp.concatenate(
        [jnp.where(core == 0, g, p) for g, p in zip(got_parts, partner_parts)]
    )
    high = jnp.concatenate(
        [jnp.where(core == 0, p, g) for g, p in zip(got_parts, partner_parts)]
    )

    def forward(act):
        own_act = lax.dynamic_slice_in_dim(act, tm * rows, rows, axis=1)
        other_act = lax.dynamic_slice_in_dim(act, (1 - tm) * rows, rows, axis=1)
        own = jnp.dot(own_act, w_ups, preferred_element_type=jnp.float32)
        other = jnp.concatenate(
            [
                jnp.dot(other_act, low, preferred_element_type=jnp.float32),
                jnp.dot(other_act, high, preferred_element_type=jnp.float32),
            ],
            axis=1,
        )
        return own + other

    def backward(d_taps):
        own = contract_cols(d_taps, w_ups)
        other = contract_cols(d_taps[:, :cols], low) + contract_cols(d_taps[:, cols:], high)
        return jnp.where(
            tm == 0, jnp.concatenate([own, other], axis=1), jnp.concatenate([other, own], axis=1)
        )

    return forward, backward, got_parts[0]


def on_device(
    src_mel, owner, dst_pos, keep, cotangent, w_pre, b_pre, w_ups, upsample_bias, w_res, b_res
):
    owners_count = lax.axis_size("dp")
    ups_forward, ups_backward, ready = ups_functions(w_ups)
    src_mel, _ = lax.optimization_barrier((src_mel, ready))
    seg_rows = src_mel[0]
    seg_count = seg_rows.shape[0]
    mel_bins = w_pre.shape[0] // KPRE
    pick = jnp.arange(owners_count, dtype=jnp.int32)[:, None] == owner[0][None, :]
    seg_width = seg_rows.shape[1]
    header = jnp.stack([dst_pos[0] + 1, keep[0]], axis=1).astype(jnp.bfloat16)
    seg_ext = jnp.concatenate([seg_rows, header], axis=1)
    outgoing = jnp.dot(
        pick.astype(jnp.bfloat16), seg_ext, preferred_element_type=jnp.float32
    ).astype(jnp.bfloat16)
    arrived = lax.all_to_all(outgoing, "dp", split_axis=0, concat_axis=0, tiled=True)
    slot_code = arrived[:, seg_width].astype(jnp.int32)
    keep_code = arrived[:, seg_width + 1].astype(jnp.int32)
    place = (slot_code - 1)[:, None] == jnp.arange(seg_count, dtype=jnp.int32)[None, :]
    mel_segs = contract_rows(place.astype(jnp.bfloat16), arrived[:, :seg_width]).astype(
        jnp.bfloat16
    )
    keep_segs = jnp.sum(jnp.where(place, keep_code[:, None], 0), axis=0)
    mel = mel_segs.reshape(seg_count * (mel_segs.shape[1] // mel_bins), mel_bins)
    frame_count = mel.shape[0]
    mel_ext = with_halo(mel, (("tm", 0),), KPRE // 2 + 1)
    first_frame0 = lax.axis_index("tm") * frame_count
    total = lax.axis_size("tm") * frame_count
    cot = cotangent[0]
    marks = jnp.repeat(keep_segs, cot.shape[0] // seg_count)
    gradient_value = jnp.where(marks[:, None] > 0, cot, jnp.zeros_like(cot))
    output_rows, grads = local_pass(
        mel_ext,
        gradient_value,
        first_frame0,
        total,
        w_pre,
        b_pre,
        ups_forward,
        ups_backward,
        upsample_bias,
        w_res,
        b_res,
    )
    summed = butterfly_psum(grads)
    return (output_rows[None], summed[0], summed[1], summed[2], summed[3])


def solution(mesh):
    in_specs = (
        P("tm", "dp", None),
        P("tm", "dp"),
        P("tm", "dp"),
        P("tm", "dp"),
        P("dp", "tm", None),
        P(),
        P(),
        P("tm", None),
        P(),
        P(),
        P(),
    )
    out_specs = (P("dp", "tm", None), P(), P(), P(), P())
    return jax.shard_map(
        on_device, mesh=mesh, in_specs=in_specs, out_specs=out_specs, check_vma=False
    )
```

```python
import jax
import jax.numpy as jnp
from jax import lax
from jax.sharding import PartitionSpec as P

KPRE = 7
UPSAMPLE_FACTOR = 8
DILATION_SIZE = 3


def with_halo(block, sides, width):
    for axis, dim in sides:
        count = lax.axis_size(axis)
        forward = [(i, i + 1) for i in range(count - 1)]
        backward = [(target, source) for source, target in forward]
        low = lax.ppermute(
            lax.slice_in_dim(block, block.shape[dim] - width, None, axis=dim), axis, forward
        )
        high = lax.ppermute(lax.slice_in_dim(block, 0, width, axis=dim), axis, backward)
        block = jnp.concatenate([low, block, high], axis=dim)
    return block


def leaky(value):
    return jnp.where(value > 0, value, 0.1 * value)


def negative_slope(value):
    return jnp.where(value > 0, 1.0, 0.1).astype(jnp.float32)


def contract_rows(left, right):
    return lax.dot_general(
        left, right, (((0,), (0,)), ((), ())), preferred_element_type=jnp.float32
    )


def contract_cols(left, right):
    return lax.dot_general(
        left, right, (((1,), (1,)), ((), ())), preferred_element_type=jnp.float32
    )


def local_pass(
    mel_ext,
    gradient_value,
    first_frame0,
    total,
    w_pre,
    b_pre,
    ups_forward,
    ups_backward,
    upsample_bias,
    w_res,
    b_res,
):
    mel_bins = mel_ext.shape[1]
    kpre = w_pre.shape[0] // mel_bins
    edge = kpre // 2 + 1
    frame_count = mel_ext.shape[0] - 2 * edge
    window_width = upsample_bias.shape[0]
    residual_kernel = w_res.shape[0] // window_width
    patches = jnp.concatenate([mel_ext[i : i + frame_count + 2] for i in range(kpre)], axis=1)
    pre = jnp.dot(patches, w_pre, preferred_element_type=jnp.float32) + b_pre
    frame_idx = first_frame0 - 1 + jnp.arange(frame_count + 2, dtype=jnp.int32)
    inside_f = ((frame_idx >= 0) & (frame_idx < total))[:, None]
    act = jnp.where(inside_f, leaky(pre), 0.0).astype(jnp.bfloat16)
    taps = ups_forward(act).reshape(frame_count + 2, 2 * UPSAMPLE_FACTOR, window_width)
    upper_output = taps[1:, :UPSAMPLE_FACTOR] + taps[:-1, UPSAMPLE_FACTOR:]
    sample_count = UPSAMPLE_FACTOR * frame_count
    start_offset = UPSAMPLE_FACTOR // 2 - DILATION_SIZE
    waveform = (
        upper_output.reshape(UPSAMPLE_FACTOR * (frame_count + 1), window_width)[
            start_offset : start_offset + sample_count + 2 * DILATION_SIZE
        ]
        + upsample_bias
    )
    step_index = (
        UPSAMPLE_FACTOR * first_frame0
        - DILATION_SIZE
        + jnp.arange(sample_count + 2 * DILATION_SIZE, dtype=jnp.int32)
    )
    inside_samples = ((step_index >= 0) & (step_index < UPSAMPLE_FACTOR * total))[:, None]
    hidden_state = jnp.where(inside_samples, leaky(waveform), 0.0).astype(jnp.bfloat16)
    column_block = jnp.concatenate(
        [
            hidden_state[kernel_index * DILATION_SIZE : kernel_index * DILATION_SIZE + sample_count]
            for kernel_index in range(residual_kernel)
        ],
        axis=1,
    )
    convolve_fn = jnp.dot(column_block, w_res, preferred_element_type=jnp.float32) + b_res
    output_rows = (waveform[DILATION_SIZE : DILATION_SIZE + sample_count] + convolve_fn).astype(
        jnp.bfloat16
    )
    g_wres = contract_rows(column_block, gradient_value)
    g_bres = jnp.sum(gradient_value.astype(jnp.float32), axis=0)
    backward_pass = contract_cols(gradient_value, w_res)
    hidden_gradient = jnp.zeros((sample_count + 2 * DILATION_SIZE, window_width), jnp.float32)
    for kernel_index in range(residual_kernel):
        hidden_gradient = hidden_gradient + jnp.pad(
            backward_pass[:, kernel_index * window_width : (kernel_index + 1) * window_width],
            (
                (
                    kernel_index * DILATION_SIZE,
                    (residual_kernel - 1 - kernel_index) * DILATION_SIZE,
                ),
                (0, 0),
            ),
        )
    waveform_gradient = jnp.where(
        inside_samples, hidden_gradient * negative_slope(waveform), 0.0
    ) + jnp.pad(gradient_value.astype(jnp.float32), ((DILATION_SIZE, DILATION_SIZE), (0, 0)))
    waveform_gradient = waveform_gradient.astype(jnp.bfloat16)
    d_upper = jnp.pad(waveform_gradient, ((start_offset, start_offset), (0, 0))).reshape(
        frame_count + 1, UPSAMPLE_FACTOR, window_width
    )
    zero_row = jnp.zeros((1, UPSAMPLE_FACTOR, window_width), jnp.bfloat16)
    d_taps = jnp.concatenate(
        [
            jnp.concatenate([zero_row, d_upper], axis=0),
            jnp.concatenate([d_upper, zero_row], axis=0),
        ],
        axis=1,
    )
    d_act = ups_backward(d_taps.reshape(frame_count + 2, 2 * UPSAMPLE_FACTOR * window_width))
    d_pre = jnp.where(inside_f, d_act * negative_slope(pre), 0.0).astype(jnp.bfloat16)
    g_wpre = contract_rows(patches, d_pre)
    g_bpre = jnp.sum(d_pre.astype(jnp.float32), axis=0)
    return (output_rows, (g_wpre, g_bpre, g_wres, g_bres))


def tile_rows(value):
    if value.ndim == 2 and value.shape[0] % 8 == 0 and value.shape[1] % 128 == 0:
        r, c = value.shape
        value = value.reshape(r // 8, 8, c // 128, 128).transpose(0, 2, 1, 3)
    return jnp.pad(value.reshape(-1), (0, -value.size % 128)).reshape(-1, 128)


def untile_rows(rows, shape):
    if len(shape) == 2 and shape[0] % 8 == 0 and shape[1] % 128 == 0:
        r, c = shape
        return rows.reshape(r // 8, c // 128, 8, 128).transpose(0, 2, 1, 3).reshape(shape)
    size = 1
    for n in shape:
        size *= n
    return rows.reshape(-1)[:size].reshape(shape)


def butterfly_psum(parts):
    dp_size = lax.axis_size("dp")
    tm_size = lax.axis_size("tm")
    axes = ("dp", "tm")
    levels = [("tm", 1 << k) for k in range(tm_size.bit_length() - 1)]
    levels += [("dp", 1 << k) for k in range(1, dp_size.bit_length() - 1)]
    groups = [levels[i : i + 2] for i in range(0, len(levels), 2)]
    orders = (groups, groups[::-1])
    count = dp_size * tm_size

    def perm_of(step, offset):
        out = []
        for d in range(dp_size):
            for t in range(tm_size):
                idx = {"dp": d, "tm": t}
                for j, (axis, bit) in enumerate(orders[d % 2][step]):
                    if (offset >> j) & 1:
                        idx[axis] = idx[axis] ^ bit
                out.append((d * tm_size + t, idx["dp"] * tm_size + idx["tm"]))
        return out

    core = lax.axis_index("dp") % 2
    position = {"dp": lax.axis_index("dp"), "tm": lax.axis_index("tm")}

    def slot_of(step):
        def one(group):
            return sum(((position[a] // b) % 2) << j for j, (a, b) in enumerate(group))

        return jnp.where(core == 0, one(orders[0][step]), one(orders[1][step]))

    tiles = [tile_rows(p) for p in parts]
    flat = jnp.concatenate([t.reshape(-1) for t in tiles])
    unit = 8 * 128 * count
    padded = -(-flat.shape[0] // unit) * unit
    x = jnp.pad(flat, (0, padded - flat.shape[0])).reshape(padded // 128, 128)
    core_perm = [(i, i ^ tm_size) for i in range(count)]
    half = x.shape[0] // 2
    send = lax.dynamic_slice_in_dim(x, (1 - core) * half, half)
    x = lax.dynamic_slice_in_dim(x, core * half, half) + lax.ppermute(send, axes, core_perm)
    for step in range(len(groups)):
        radix = 1 << len(groups[step])
        piece = x.shape[0] // radix
        slot = slot_of(step)
        total = lax.dynamic_slice_in_dim(x, slot * piece, piece)
        for offset in range(1, radix):
            send = lax.dynamic_slice_in_dim(x, (slot ^ offset) * piece, piece)
            total = total + lax.ppermute(send, axes, perm_of(step, offset))
        x = total
    for step in reversed(range(len(groups))):
        radix = 1 << len(groups[step])
        slot = slot_of(step)
        got = [x] + [lax.ppermute(x, axes, perm_of(step, o)) for o in range(1, radix)]
        pieces = []
        for q in range(radix):
            source = slot ^ q
            chosen = got[radix - 1]
            for o in range(radix - 2, -1, -1):
                chosen = jnp.where(source == o, got[o], chosen)
            pieces.append(chosen)
        x = jnp.concatenate(pieces)
    recv = lax.ppermute(x, axes, core_perm)
    x = jnp.where(core == 0, jnp.concatenate([x, recv]), jnp.concatenate([recv, x]))
    out, at = [], 0
    for p, t in zip(parts, tiles):
        out.append(untile_rows(x[at : at + t.shape[0]], p.shape))
        at += t.shape[0]
    return tuple(out)

def ups_functions(w_ups):
    dp_size = lax.axis_size("dp")
    if lax.axis_size("tm") != 2 or dp_size % 2:
        whole = lax.all_gather(w_ups, "tm", axis=0, tiled=True)
        return (
            lambda act: jnp.dot(act, whole, preferred_element_type=jnp.float32),
            lambda d_taps: contract_cols(d_taps, whole),
            whole,
        )
    rows, width = w_ups.shape
    cols = width // 2
    core = lax.axis_index("dp") % 2
    tm = lax.axis_index("tm")
    bounds = [0, 16, rows // 2, rows] if rows % 32 == 0 and rows > 32 else [0, rows]
    swap = [(i, i ^ 1) for i in range(dp_size)]
    got_parts, partner_parts = [], []
    mine = jnp.where(core == 0, w_ups[:, :cols], w_ups[:, cols:])
    for lo, hi in zip(bounds, bounds[1:]):
        piece = mine[lo:hi]
        if len(got_parts) > 1:
            piece, _ = lax.optimization_barrier((piece, got_parts[-1]))
        got_parts.append(lax.ppermute(piece, "tm", [(0, 1), (1, 0)]))
        partner_parts.append(lax.ppermute(got_parts[-1], "dp", swap))
    low = jnp.concatenate(
        [jnp.where(core == 0, g, p) for g, p in zip(got_parts, partner_parts)]
    )
    high = jnp.concatenate(
        [jnp.where(core == 0, p, g) for g, p in zip(got_parts, partner_parts)]
    )

    def forward(act):
        own_act = lax.dynamic_slice_in_dim(act, tm * rows, rows, axis=1)
        other_act = lax.dynamic_slice_in_dim(act, (1 - tm) * rows, rows, axis=1)
        own = jnp.dot(own_act, w_ups, preferred_element_type=jnp.float32)
        other = jnp.concatenate(
            [
                jnp.dot(other_act, low, preferred_element_type=jnp.float32),
                jnp.dot(other_act, high, preferred_element_type=jnp.float32),
            ],
            axis=1,
        )
        return own + other

    def backward(d_taps):
        own = contract_cols(d_taps, w_ups)
        other = contract_cols(d_taps[:, :cols], low) + contract_cols(d_taps[:, cols:], high)
        return jnp.where(
            tm == 0, jnp.concatenate([own, other], axis=1), jnp.concatenate([other, own], axis=1)
        )

    return forward, backward, got_parts[0]


def on_device(
    src_mel, owner, dst_pos, keep, cotangent, w_pre, b_pre, w_ups, upsample_bias, w_res, b_res
):
    owners_count = lax.axis_size("dp")
    ups_forward, ups_backward, ready = ups_functions(w_ups)
    src_mel, _ = lax.optimization_barrier((src_mel, ready))
    seg_rows = src_mel[0]
    seg_count = seg_rows.shape[0]
    mel_bins = w_pre.shape[0] // KPRE
    pick = jnp.arange(owners_count, dtype=jnp.int32)[:, None] == owner[0][None, :]
    seg_width = seg_rows.shape[1]
    header = jnp.stack([dst_pos[0] + 1, keep[0]], axis=1).astype(jnp.bfloat16)
    seg_ext = jnp.concatenate([seg_rows, header], axis=1)
    outgoing = jnp.dot(
        pick.astype(jnp.bfloat16), seg_ext, preferred_element_type=jnp.float32
    ).astype(jnp.bfloat16)
    arrived = lax.all_to_all(outgoing, "dp", split_axis=0, concat_axis=0, tiled=True)
    slot_code = arrived[:, seg_width].astype(jnp.int32)
    keep_code = arrived[:, seg_width + 1].astype(jnp.int32)
    place = (slot_code - 1)[:, None] == jnp.arange(seg_count, dtype=jnp.int32)[None, :]
    mel_segs = contract_rows(place.astype(jnp.bfloat16), arrived[:, :seg_width]).astype(
        jnp.bfloat16
    )
    keep_segs = jnp.sum(jnp.where(place, keep_code[:, None], 0), axis=0)
    mel = mel_segs.reshape(seg_count * (mel_segs.shape[1] // mel_bins), mel_bins)
    frame_count = mel.shape[0]
    mel_ext = with_halo(mel, (("tm", 0),), KPRE // 2 + 1)
    first_frame0 = lax.axis_index("tm") * frame_count
    total = lax.axis_size("tm") * frame_count
    cot = cotangent[0]
    marks = jnp.repeat(keep_segs, cot.shape[0] // seg_count)
    gradient_value = jnp.where(marks[:, None] > 0, cot, jnp.zeros_like(cot))
    output_rows, grads = local_pass(
        mel_ext,
        gradient_value,
        first_frame0,
        total,
        w_pre,
        b_pre,
        ups_forward,
        ups_backward,
        upsample_bias,
        w_res,
        b_res,
    )
    summed = butterfly_psum(grads)
    return (output_rows[None], summed[0], summed[1], summed[2], summed[3])


def solution(mesh):
    in_specs = (
        P("tm", "dp", None),
        P("tm", "dp"),
        P("tm", "dp"),
        P("tm", "dp"),
        P("dp", "tm", None),
        P(),
        P(),
        P("tm", None),
        P(),
        P(),
        P(),
    )
    out_specs = (P("dp", "tm", None), P(), P(), P(), P())
    return jax.shard_map(
        on_device, mesh=mesh, in_specs=in_specs, out_specs=out_specs, check_vma=False
    )
```

```python
import jax
import jax.numpy as jnp
from jax import lax
from jax.sharding import PartitionSpec as P

KPRE = 7
UPSAMPLE_FACTOR = 8
DILATION_SIZE = 3


def with_halo(block, sides, width):
    for axis, dim in sides:
        count = lax.axis_size(axis)
        forward = [(i, i + 1) for i in range(count - 1)]
        backward = [(target, source) for source, target in forward]
        low = lax.ppermute(
            lax.slice_in_dim(block, block.shape[dim] - width, None, axis=dim), axis, forward
        )
        high = lax.ppermute(lax.slice_in_dim(block, 0, width, axis=dim), axis, backward)
        block = jnp.concatenate([low, block, high], axis=dim)
    return block


def leaky(value):
    return jnp.where(value > 0, value, 0.1 * value)


def negative_slope(value):
    return jnp.where(value > 0, 1.0, 0.1).astype(jnp.float32)


def contract_rows(left, right):
    return lax.dot_general(
        left, right, (((0,), (0,)), ((), ())), preferred_element_type=jnp.float32
    )


def contract_cols(left, right):
    return lax.dot_general(
        left, right, (((1,), (1,)), ((), ())), preferred_element_type=jnp.float32
    )


def local_pass(
    mel_ext,
    gradient_value,
    first_frame0,
    total,
    w_pre,
    b_pre,
    ups_forward,
    ups_backward,
    upsample_bias,
    w_res,
    b_res,
):
    mel_bins = mel_ext.shape[1]
    kpre = w_pre.shape[0] // mel_bins
    edge = kpre // 2 + 1
    frame_count = mel_ext.shape[0] - 2 * edge
    window_width = upsample_bias.shape[0]
    residual_kernel = w_res.shape[0] // window_width
    patches = jnp.concatenate([mel_ext[i : i + frame_count + 2] for i in range(kpre)], axis=1)
    pre = jnp.dot(patches, w_pre, preferred_element_type=jnp.float32) + b_pre
    frame_idx = first_frame0 - 1 + jnp.arange(frame_count + 2, dtype=jnp.int32)
    inside_f = ((frame_idx >= 0) & (frame_idx < total))[:, None]
    act = jnp.where(inside_f, leaky(pre), 0.0).astype(jnp.bfloat16)
    taps = ups_forward(act).reshape(frame_count + 2, 2 * UPSAMPLE_FACTOR, window_width)
    upper_output = taps[1:, :UPSAMPLE_FACTOR] + taps[:-1, UPSAMPLE_FACTOR:]
    sample_count = UPSAMPLE_FACTOR * frame_count
    start_offset = UPSAMPLE_FACTOR // 2 - DILATION_SIZE
    waveform = (
        upper_output.reshape(UPSAMPLE_FACTOR * (frame_count + 1), window_width)[
            start_offset : start_offset + sample_count + 2 * DILATION_SIZE
        ]
        + upsample_bias
    )
    step_index = (
        UPSAMPLE_FACTOR * first_frame0
        - DILATION_SIZE
        + jnp.arange(sample_count + 2 * DILATION_SIZE, dtype=jnp.int32)
    )
    inside_samples = ((step_index >= 0) & (step_index < UPSAMPLE_FACTOR * total))[:, None]
    hidden_state = jnp.where(inside_samples, leaky(waveform), 0.0).astype(jnp.bfloat16)
    column_block = jnp.concatenate(
        [
            hidden_state[kernel_index * DILATION_SIZE : kernel_index * DILATION_SIZE + sample_count]
            for kernel_index in range(residual_kernel)
        ],
        axis=1,
    )
    convolve_fn = jnp.dot(column_block, w_res, preferred_element_type=jnp.float32) + b_res
    output_rows = (waveform[DILATION_SIZE : DILATION_SIZE + sample_count] + convolve_fn).astype(
        jnp.bfloat16
    )
    g_wres = contract_rows(column_block, gradient_value)
    g_bres = jnp.sum(gradient_value.astype(jnp.float32), axis=0)
    backward_pass = contract_cols(gradient_value, w_res)
    hidden_gradient = jnp.zeros((sample_count + 2 * DILATION_SIZE, window_width), jnp.float32)
    for kernel_index in range(residual_kernel):
        hidden_gradient = hidden_gradient + jnp.pad(
            backward_pass[:, kernel_index * window_width : (kernel_index + 1) * window_width],
            (
                (
                    kernel_index * DILATION_SIZE,
                    (residual_kernel - 1 - kernel_index) * DILATION_SIZE,
                ),
                (0, 0),
            ),
        )
    waveform_gradient = jnp.where(
        inside_samples, hidden_gradient * negative_slope(waveform), 0.0
    ) + jnp.pad(gradient_value.astype(jnp.float32), ((DILATION_SIZE, DILATION_SIZE), (0, 0)))
    waveform_gradient = waveform_gradient.astype(jnp.bfloat16)
    d_upper = jnp.pad(waveform_gradient, ((start_offset, start_offset), (0, 0))).reshape(
        frame_count + 1, UPSAMPLE_FACTOR, window_width
    )
    zero_row = jnp.zeros((1, UPSAMPLE_FACTOR, window_width), jnp.bfloat16)
    d_taps = jnp.concatenate(
        [
            jnp.concatenate([zero_row, d_upper], axis=0),
            jnp.concatenate([d_upper, zero_row], axis=0),
        ],
        axis=1,
    )
    d_act = ups_backward(d_taps.reshape(frame_count + 2, 2 * UPSAMPLE_FACTOR * window_width))
    d_pre = jnp.where(inside_f, d_act * negative_slope(pre), 0.0).astype(jnp.bfloat16)
    g_wpre = contract_rows(patches, d_pre)
    g_bpre = jnp.sum(d_pre.astype(jnp.float32), axis=0)
    return (output_rows, (g_wpre, g_bpre, g_wres, g_bres))


def tile_rows(value):
    if value.ndim == 2 and value.shape[0] % 8 == 0 and value.shape[1] % 128 == 0:
        r, c = value.shape
        value = value.reshape(r // 8, 8, c // 128, 128).transpose(0, 2, 1, 3)
    return jnp.pad(value.reshape(-1), (0, -value.size % 128)).reshape(-1, 128)


def untile_rows(rows, shape):
    if len(shape) == 2 and shape[0] % 8 == 0 and shape[1] % 128 == 0:
        r, c = shape
        return rows.reshape(r // 8, c // 128, 8, 128).transpose(0, 2, 1, 3).reshape(shape)
    size = 1
    for n in shape:
        size *= n
    return rows.reshape(-1)[:size].reshape(shape)


def butterfly_psum(parts):
    dp_size = lax.axis_size("dp")
    tm_size = lax.axis_size("tm")
    axes = ("dp", "tm")
    levels = [("tm", 1 << k) for k in range(tm_size.bit_length() - 1)]
    levels += [("dp", 1 << k) for k in range(1, dp_size.bit_length() - 1)]
    groups = [levels[i : i + 2] for i in range(0, len(levels), 2)]
    orders = (groups, groups[::-1])
    count = dp_size * tm_size

    def perm_of(step, offset):
        out = []
        for d in range(dp_size):
            for t in range(tm_size):
                idx = {"dp": d, "tm": t}
                for j, (axis, bit) in enumerate(orders[d % 2][step]):
                    if (offset >> j) & 1:
                        idx[axis] = idx[axis] ^ bit
                out.append((d * tm_size + t, idx["dp"] * tm_size + idx["tm"]))
        return out

    core = lax.axis_index("dp") % 2
    position = {"dp": lax.axis_index("dp"), "tm": lax.axis_index("tm")}

    def slot_of(step):
        def one(group):
            return sum(((position[a] // b) % 2) << j for j, (a, b) in enumerate(group))

        return jnp.where(core == 0, one(orders[0][step]), one(orders[1][step]))

    tiles = [tile_rows(p) for p in parts]
    flat = jnp.concatenate([t.reshape(-1) for t in tiles])
    unit = 8 * 128 * count
    padded = -(-flat.shape[0] // unit) * unit
    x = jnp.pad(flat, (0, padded - flat.shape[0])).reshape(padded // 128, 128)
    core_perm = [(i, i ^ tm_size) for i in range(count)]
    half = x.shape[0] // 2
    send = lax.dynamic_slice_in_dim(x, (1 - core) * half, half)
    x = lax.dynamic_slice_in_dim(x, core * half, half) + lax.ppermute(send, axes, core_perm)
    for step in range(len(groups) - 1):
        radix = 1 << len(groups[step])
        piece = x.shape[0] // radix
        slot = slot_of(step)
        total = lax.dynamic_slice_in_dim(x, slot * piece, piece)
        for offset in range(1, radix):
            send = lax.dynamic_slice_in_dim(x, (slot ^ offset) * piece, piece)
            total = total + lax.ppermute(send, axes, perm_of(step, offset))
        x = total
    if groups:
        last = len(groups) - 1
        radix = 1 << len(groups[last])
        slot = slot_of(last)
        got = [x] + [lax.ppermute(x, axes, perm_of(last, o)) for o in range(1, radix)]
        pieces = []
        for q in range(radix):
            source = slot ^ q
            chosen = got[radix - 1]
            for o in range(radix - 2, -1, -1):
                chosen = jnp.where(source == o, got[o], chosen)
            pieces.append(chosen)
        while len(pieces) > 1:
            pieces = [pieces[i] + pieces[i + 1] for i in range(0, len(pieces), 2)]
        x = pieces[0]
    for step in reversed(range(len(groups) - 1)):
        radix = 1 << len(groups[step])
        slot = slot_of(step)
        got = [x] + [lax.ppermute(x, axes, perm_of(step, o)) for o in range(1, radix)]
        pieces = []
        for q in range(radix):
            source = slot ^ q
            chosen = got[radix - 1]
            for o in range(radix - 2, -1, -1):
                chosen = jnp.where(source == o, got[o], chosen)
            pieces.append(chosen)
        x = jnp.concatenate(pieces)
    recv = lax.ppermute(x, axes, core_perm)
    x = jnp.where(core == 0, jnp.concatenate([x, recv]), jnp.concatenate([recv, x]))
    out, at = [], 0
    for p, t in zip(parts, tiles):
        out.append(untile_rows(x[at : at + t.shape[0]], p.shape))
        at += t.shape[0]
    return tuple(out)

def ups_functions(w_ups):
    dp_size = lax.axis_size("dp")
    if lax.axis_size("tm") != 2 or dp_size % 2:
        whole = lax.all_gather(w_ups, "tm", axis=0, tiled=True)
        return (
            lambda act: jnp.dot(act, whole, preferred_element_type=jnp.float32),
            lambda d_taps: contract_cols(d_taps, whole),
            whole,
        )
    rows, width = w_ups.shape
    cols = width // 2
    core = lax.axis_index("dp") % 2
    tm = lax.axis_index("tm")
    bounds = [0, 16, rows // 2, rows] if rows % 32 == 0 and rows > 32 else [0, rows]
    swap = [(i, i ^ 1) for i in range(dp_size)]
    got_parts, partner_parts = [], []
    mine = jnp.where(core == 0, w_ups[:, :cols], w_ups[:, cols:])
    for lo, hi in zip(bounds, bounds[1:]):
        got_parts.append(lax.ppermute(mine[lo:hi], "tm", [(0, 1), (1, 0)]))
        partner_parts.append(lax.ppermute(got_parts[-1], "dp", swap))
    low = jnp.concatenate(
        [jnp.where(core == 0, g, p) for g, p in zip(got_parts, partner_parts)]
    )
    high = jnp.concatenate(
        [jnp.where(core == 0, p, g) for g, p in zip(got_parts, partner_parts)]
    )

    def forward(act):
        own_act = lax.dynamic_slice_in_dim(act, tm * rows, rows, axis=1)
        other_act = lax.dynamic_slice_in_dim(act, (1 - tm) * rows, rows, axis=1)
        own = jnp.dot(own_act, w_ups, preferred_element_type=jnp.float32)
        other = jnp.concatenate(
            [
                jnp.dot(other_act, low, preferred_element_type=jnp.float32),
                jnp.dot(other_act, high, preferred_element_type=jnp.float32),
            ],
            axis=1,
        )
        return own + other

    def backward(d_taps):
        own = contract_cols(d_taps, w_ups)
        other = contract_cols(d_taps[:, :cols], low) + contract_cols(d_taps[:, cols:], high)
        return jnp.where(
            tm == 0, jnp.concatenate([own, other], axis=1), jnp.concatenate([other, own], axis=1)
        )

    return forward, backward, got_parts[0]


def on_device(
    src_mel, owner, dst_pos, keep, cotangent, w_pre, b_pre, w_ups, upsample_bias, w_res, b_res
):
    owners_count = lax.axis_size("dp")
    ups_forward, ups_backward, ready = ups_functions(w_ups)
    src_mel, _ = lax.optimization_barrier((src_mel, ready))
    seg_rows = src_mel[0]
    seg_count = seg_rows.shape[0]
    mel_bins = w_pre.shape[0] // KPRE
    pick = jnp.arange(owners_count, dtype=jnp.int32)[:, None] == owner[0][None, :]
    seg_width = seg_rows.shape[1]
    header = jnp.stack([dst_pos[0] + 1, keep[0]], axis=1).astype(jnp.bfloat16)
    seg_ext = jnp.concatenate([seg_rows, header], axis=1)
    outgoing = jnp.dot(
        pick.astype(jnp.bfloat16), seg_ext, preferred_element_type=jnp.float32
    ).astype(jnp.bfloat16)
    arrived = lax.all_to_all(outgoing, "dp", split_axis=0, concat_axis=0, tiled=True)
    slot_code = arrived[:, seg_width].astype(jnp.int32)
    keep_code = arrived[:, seg_width + 1].astype(jnp.int32)
    place = (slot_code - 1)[:, None] == jnp.arange(seg_count, dtype=jnp.int32)[None, :]
    mel_segs = contract_rows(place.astype(jnp.bfloat16), arrived[:, :seg_width]).astype(
        jnp.bfloat16
    )
    keep_segs = jnp.sum(jnp.where(place, keep_code[:, None], 0), axis=0)
    mel = mel_segs.reshape(seg_count * (mel_segs.shape[1] // mel_bins), mel_bins)
    frame_count = mel.shape[0]
    mel_ext = with_halo(mel, (("tm", 0),), KPRE // 2 + 1)
    first_frame0 = lax.axis_index("tm") * frame_count
    total = lax.axis_size("tm") * frame_count
    cot = cotangent[0]
    marks = jnp.repeat(keep_segs, cot.shape[0] // seg_count)
    gradient_value = jnp.where(marks[:, None] > 0, cot, jnp.zeros_like(cot))
    output_rows, grads = local_pass(
        mel_ext,
        gradient_value,
        first_frame0,
        total,
        w_pre,
        b_pre,
        ups_forward,
        ups_backward,
        upsample_bias,
        w_res,
        b_res,
    )
    summed = butterfly_psum(grads)
    return (output_rows[None], summed[0], summed[1], summed[2], summed[3])


def solution(mesh):
    in_specs = (
        P("tm", "dp", None),
        P("tm", "dp"),
        P("tm", "dp"),
        P("tm", "dp"),
        P("dp", "tm", None),
        P(),
        P(),
        P("tm", None),
        P(),
        P(),
        P(),
    )
    out_specs = (P("dp", "tm", None), P(), P(), P(), P())
    return jax.shard_map(
        on_device, mesh=mesh, in_specs=in_specs, out_specs=out_specs, check_vma=False
    )
```

```python
import jax
import jax.numpy as jnp
from jax import lax
from jax.sharding import PartitionSpec as P

KPRE = 7
UPSAMPLE_FACTOR = 8
DILATION_SIZE = 3


def with_halo(block, sides, width):
    for axis, dim in sides:
        count = lax.axis_size(axis)
        forward = [(i, i + 1) for i in range(count - 1)]
        backward = [(target, source) for source, target in forward]
        low = lax.ppermute(
            lax.slice_in_dim(block, block.shape[dim] - width, None, axis=dim), axis, forward
        )
        high = lax.ppermute(lax.slice_in_dim(block, 0, width, axis=dim), axis, backward)
        block = jnp.concatenate([low, block, high], axis=dim)
    return block


def leaky(value):
    return jnp.where(value > 0, value, 0.1 * value)


def negative_slope(value):
    return jnp.where(value > 0, 1.0, 0.1).astype(jnp.float32)


def contract_rows(left, right):
    return lax.dot_general(
        left, right, (((0,), (0,)), ((), ())), preferred_element_type=jnp.float32
    )


def contract_cols(left, right):
    return lax.dot_general(
        left, right, (((1,), (1,)), ((), ())), preferred_element_type=jnp.float32
    )


def local_pass(
    mel_ext,
    gradient_value,
    first_frame0,
    total,
    w_pre,
    b_pre,
    ups_forward,
    ups_backward,
    upsample_bias,
    w_res,
    b_res,
):
    mel_bins = mel_ext.shape[1]
    kpre = w_pre.shape[0] // mel_bins
    edge = kpre // 2 + 1
    frame_count = mel_ext.shape[0] - 2 * edge
    window_width = upsample_bias.shape[0]
    residual_kernel = w_res.shape[0] // window_width
    patches = jnp.concatenate([mel_ext[i : i + frame_count + 2] for i in range(kpre)], axis=1)
    pre = jnp.dot(patches, w_pre, preferred_element_type=jnp.float32) + b_pre
    frame_idx = first_frame0 - 1 + jnp.arange(frame_count + 2, dtype=jnp.int32)
    inside_f = ((frame_idx >= 0) & (frame_idx < total))[:, None]
    act = jnp.where(inside_f, leaky(pre), 0.0).astype(jnp.bfloat16)
    taps = ups_forward(act).reshape(frame_count + 2, 2 * UPSAMPLE_FACTOR, window_width)
    upper_output = taps[1:, :UPSAMPLE_FACTOR] + taps[:-1, UPSAMPLE_FACTOR:]
    sample_count = UPSAMPLE_FACTOR * frame_count
    start_offset = UPSAMPLE_FACTOR // 2 - DILATION_SIZE
    waveform = (
        upper_output.reshape(UPSAMPLE_FACTOR * (frame_count + 1), window_width)[
            start_offset : start_offset + sample_count + 2 * DILATION_SIZE
        ]
        + upsample_bias
    )
    step_index = (
        UPSAMPLE_FACTOR * first_frame0
        - DILATION_SIZE
        + jnp.arange(sample_count + 2 * DILATION_SIZE, dtype=jnp.int32)
    )
    inside_samples = ((step_index >= 0) & (step_index < UPSAMPLE_FACTOR * total))[:, None]
    hidden_state = jnp.where(inside_samples, leaky(waveform), 0.0).astype(jnp.bfloat16)
    column_block = jnp.concatenate(
        [
            hidden_state[kernel_index * DILATION_SIZE : kernel_index * DILATION_SIZE + sample_count]
            for kernel_index in range(residual_kernel)
        ],
        axis=1,
    )
    convolve_fn = jnp.dot(column_block, w_res, preferred_element_type=jnp.float32) + b_res
    output_rows = (waveform[DILATION_SIZE : DILATION_SIZE + sample_count] + convolve_fn).astype(
        jnp.bfloat16
    )
    g_wres = contract_rows(column_block, gradient_value)
    g_bres = jnp.sum(gradient_value.astype(jnp.float32), axis=0)
    backward_pass = contract_cols(gradient_value, w_res)
    hidden_gradient = jnp.zeros((sample_count + 2 * DILATION_SIZE, window_width), jnp.float32)
    for kernel_index in range(residual_kernel):
        hidden_gradient = hidden_gradient + jnp.pad(
            backward_pass[:, kernel_index * window_width : (kernel_index + 1) * window_width],
            (
                (
                    kernel_index * DILATION_SIZE,
                    (residual_kernel - 1 - kernel_index) * DILATION_SIZE,
                ),
                (0, 0),
            ),
        )
    waveform_gradient = jnp.where(
        inside_samples, hidden_gradient * negative_slope(waveform), 0.0
    ) + jnp.pad(gradient_value.astype(jnp.float32), ((DILATION_SIZE, DILATION_SIZE), (0, 0)))
    waveform_gradient = waveform_gradient.astype(jnp.bfloat16)
    d_upper = jnp.pad(waveform_gradient, ((start_offset, start_offset), (0, 0))).reshape(
        frame_count + 1, UPSAMPLE_FACTOR, window_width
    )
    zero_row = jnp.zeros((1, UPSAMPLE_FACTOR, window_width), jnp.bfloat16)
    d_taps = jnp.concatenate(
        [
            jnp.concatenate([zero_row, d_upper], axis=0),
            jnp.concatenate([d_upper, zero_row], axis=0),
        ],
        axis=1,
    )
    d_act = ups_backward(d_taps.reshape(frame_count + 2, 2 * UPSAMPLE_FACTOR * window_width))
    d_pre = jnp.where(inside_f, d_act * negative_slope(pre), 0.0).astype(jnp.bfloat16)
    g_wpre = contract_rows(patches, d_pre)
    g_bpre = jnp.sum(d_pre.astype(jnp.float32), axis=0)
    return (output_rows, (g_wpre, g_bpre, g_wres, g_bres))


def tile_rows(value):
    if value.ndim == 2 and value.shape[0] % 8 == 0 and value.shape[1] % 128 == 0:
        r, c = value.shape
        value = value.reshape(r // 8, 8, c // 128, 128).transpose(0, 2, 1, 3)
    return jnp.pad(value.reshape(-1), (0, -value.size % 128)).reshape(-1, 128)


def untile_rows(rows, shape):
    if len(shape) == 2 and shape[0] % 8 == 0 and shape[1] % 128 == 0:
        r, c = shape
        return rows.reshape(r // 8, c // 128, 8, 128).transpose(0, 2, 1, 3).reshape(shape)
    size = 1
    for n in shape:
        size *= n
    return rows.reshape(-1)[:size].reshape(shape)


def butterfly_psum(parts):
    dp_size = lax.axis_size("dp")
    tm_size = lax.axis_size("tm")
    axes = ("dp", "tm")
    levels = [("tm", 1 << k) for k in range(tm_size.bit_length() - 1)]
    levels += [("dp", 1 << k) for k in range(1, dp_size.bit_length() - 1)]
    groups = [levels[i : i + 2] for i in range(0, len(levels), 2)]
    orders = (groups, groups[::-1])
    count = dp_size * tm_size

    def perm_of(step, offset):
        out = []
        for d in range(dp_size):
            for t in range(tm_size):
                idx = {"dp": d, "tm": t}
                for j, (axis, bit) in enumerate(orders[d % 2][step]):
                    if (offset >> j) & 1:
                        idx[axis] = idx[axis] ^ bit
                out.append((d * tm_size + t, idx["dp"] * tm_size + idx["tm"]))
        return out

    core = lax.axis_index("dp") % 2
    position = {"dp": lax.axis_index("dp"), "tm": lax.axis_index("tm")}

    def slot_of(step):
        def one(group):
            return sum(((position[a] // b) % 2) << j for j, (a, b) in enumerate(group))

        return jnp.where(core == 0, one(orders[0][step]), one(orders[1][step]))

    tiles = [tile_rows(p) for p in parts]
    flat = jnp.concatenate([t.reshape(-1) for t in tiles])
    unit = 8 * 128 * count
    padded = -(-flat.shape[0] // unit) * unit
    x = jnp.pad(flat, (0, padded - flat.shape[0])).reshape(padded // 128, 128)
    core_perm = [(i, i ^ tm_size) for i in range(count)]
    half = x.shape[0] // 2
    send = lax.dynamic_slice_in_dim(x, (1 - core) * half, half)
    x = lax.dynamic_slice_in_dim(x, core * half, half) + lax.ppermute(send, axes, core_perm)
    for step in range(len(groups) - 1):
        radix = 1 << len(groups[step])
        piece = x.shape[0] // radix
        slot = slot_of(step)
        total = lax.dynamic_slice_in_dim(x, slot * piece, piece)
        for offset in range(1, radix):
            send = lax.dynamic_slice_in_dim(x, (slot ^ offset) * piece, piece)
            total = total + lax.ppermute(send, axes, perm_of(step, offset))
        x = total
    if groups:
        last = len(groups) - 1
        radix = 1 << len(groups[last])
        slot = slot_of(last)
        got = [x] + [lax.ppermute(x, axes, perm_of(last, o)) for o in range(1, radix)]
        pieces = []
        for q in range(radix):
            source = slot ^ q
            chosen = got[radix - 1]
            for o in range(radix - 2, -1, -1):
                chosen = jnp.where(source == o, got[o], chosen)
            pieces.append(chosen)
        while len(pieces) > 1:
            pieces = [pieces[i] + pieces[i + 1] for i in range(0, len(pieces), 2)]
        x = pieces[0]
    for step in reversed(range(len(groups) - 1)):
        radix = 1 << len(groups[step])
        slot = slot_of(step)
        got = [x] + [lax.ppermute(x, axes, perm_of(step, o)) for o in range(1, radix)]
        pieces = []
        for q in range(radix):
            source = slot ^ q
            chosen = got[radix - 1]
            for o in range(radix - 2, -1, -1):
                chosen = jnp.where(source == o, got[o], chosen)
            pieces.append(chosen)
        x = jnp.concatenate(pieces)
    recv = lax.ppermute(x, axes, core_perm)
    x = jnp.where(core == 0, jnp.concatenate([x, recv]), jnp.concatenate([recv, x]))
    out, at = [], 0
    for p, t in zip(parts, tiles):
        out.append(untile_rows(x[at : at + t.shape[0]], p.shape))
        at += t.shape[0]
    return tuple(out)

def ups_functions(w_ups):
    dp_size = lax.axis_size("dp")
    if lax.axis_size("tm") != 2 or dp_size % 2:
        whole = lax.all_gather(w_ups, "tm", axis=0, tiled=True)
        return (
            lambda act: jnp.dot(act, whole, preferred_element_type=jnp.float32),
            lambda d_taps: contract_cols(d_taps, whole),
            whole,
        )
    rows, width = w_ups.shape
    cols = width // 2
    core = lax.axis_index("dp") % 2
    tm = lax.axis_index("tm")
    bounds = [0, 16, rows] if rows % 32 == 0 and rows > 32 else [0, rows]
    swap = [(i, i ^ 1) for i in range(dp_size)]
    got_parts, partner_parts = [], []
    mine = jnp.where(core == 0, w_ups[:, :cols], w_ups[:, cols:])
    for lo, hi in zip(bounds, bounds[1:]):
        got_parts.append(lax.ppermute(mine[lo:hi], "tm", [(0, 1), (1, 0)]))
        partner_parts.append(lax.ppermute(got_parts[-1], "dp", swap))
    low = jnp.concatenate(
        [jnp.where(core == 0, g, p) for g, p in zip(got_parts, partner_parts)]
    )
    high = jnp.concatenate(
        [jnp.where(core == 0, p, g) for g, p in zip(got_parts, partner_parts)]
    )

    def forward(act):
        own_act = lax.dynamic_slice_in_dim(act, tm * rows, rows, axis=1)
        other_act = lax.dynamic_slice_in_dim(act, (1 - tm) * rows, rows, axis=1)
        own = jnp.dot(own_act, w_ups, preferred_element_type=jnp.float32)
        other = jnp.concatenate(
            [
                jnp.dot(other_act, low, preferred_element_type=jnp.float32),
                jnp.dot(other_act, high, preferred_element_type=jnp.float32),
            ],
            axis=1,
        )
        return own + other

    def backward(d_taps):
        own = contract_cols(d_taps, w_ups)
        other = contract_cols(d_taps[:, :cols], low) + contract_cols(d_taps[:, cols:], high)
        return jnp.where(
            tm == 0, jnp.concatenate([own, other], axis=1), jnp.concatenate([other, own], axis=1)
        )

    return forward, backward, got_parts[0]


def on_device(
    src_mel, owner, dst_pos, keep, cotangent, w_pre, b_pre, w_ups, upsample_bias, w_res, b_res
):
    owners_count = lax.axis_size("dp")
    ups_forward, ups_backward, ready = ups_functions(w_ups)
    src_mel, _ = lax.optimization_barrier((src_mel, ready))
    seg_rows = src_mel[0]
    seg_count = seg_rows.shape[0]
    mel_bins = w_pre.shape[0] // KPRE
    pick = jnp.arange(owners_count, dtype=jnp.int32)[:, None] == owner[0][None, :]
    seg_width = seg_rows.shape[1]
    header = jnp.stack([dst_pos[0] + 1, keep[0]], axis=1).astype(jnp.bfloat16)
    seg_ext = jnp.concatenate([seg_rows, header], axis=1)
    outgoing = jnp.dot(
        pick.astype(jnp.bfloat16), seg_ext, preferred_element_type=jnp.float32
    ).astype(jnp.bfloat16)
    arrived = lax.all_to_all(outgoing, "dp", split_axis=0, concat_axis=0, tiled=True)
    slot_code = arrived[:, seg_width].astype(jnp.int32)
    keep_code = arrived[:, seg_width + 1].astype(jnp.int32)
    place = (slot_code - 1)[:, None] == jnp.arange(seg_count, dtype=jnp.int32)[None, :]
    mel_segs = contract_rows(place.astype(jnp.bfloat16), arrived[:, :seg_width]).astype(
        jnp.bfloat16
    )
    keep_segs = jnp.sum(jnp.where(place, keep_code[:, None], 0), axis=0)
    mel = mel_segs.reshape(seg_count * (mel_segs.shape[1] // mel_bins), mel_bins)
    frame_count = mel.shape[0]
    mel_ext = with_halo(mel, (("tm", 0),), KPRE // 2 + 1)
    first_frame0 = lax.axis_index("tm") * frame_count
    total = lax.axis_size("tm") * frame_count
    cot = cotangent[0]
    marks = jnp.repeat(keep_segs, cot.shape[0] // seg_count)
    gradient_value = jnp.where(marks[:, None] > 0, cot, jnp.zeros_like(cot))
    output_rows, grads = local_pass(
        mel_ext,
        gradient_value,
        first_frame0,
        total,
        w_pre,
        b_pre,
        ups_forward,
        ups_backward,
        upsample_bias,
        w_res,
        b_res,
    )
    summed = butterfly_psum(grads)
    return (output_rows[None], summed[0], summed[1], summed[2], summed[3])


def solution(mesh):
    in_specs = (
        P("tm", "dp", None),
        P("tm", "dp"),
        P("tm", "dp"),
        P("tm", "dp"),
        P("dp", "tm", None),
        P(),
        P(),
        P("tm", None),
        P(),
        P(),
        P(),
    )
    out_specs = (P("dp", "tm", None), P(), P(), P(), P())
    return jax.shard_map(
        on_device, mesh=mesh, in_specs=in_specs, out_specs=out_specs, check_vma=False
    )
```

```python
import jax
import jax.numpy as jnp
from jax import lax
from jax.sharding import PartitionSpec as P

KPRE = 7
UPSAMPLE_FACTOR = 8
DILATION_SIZE = 3


def with_halo(block, sides, width):
    for axis, dim in sides:
        count = lax.axis_size(axis)
        forward = [(i, i + 1) for i in range(count - 1)]
        backward = [(target, source) for source, target in forward]
        low = lax.ppermute(
            lax.slice_in_dim(block, block.shape[dim] - width, None, axis=dim), axis, forward
        )
        high = lax.ppermute(lax.slice_in_dim(block, 0, width, axis=dim), axis, backward)
        block = jnp.concatenate([low, block, high], axis=dim)
    return block


def leaky(value):
    return jnp.where(value > 0, value, 0.1 * value)


def negative_slope(value):
    return jnp.where(value > 0, 1.0, 0.1).astype(jnp.float32)


def contract_rows(left, right):
    return lax.dot_general(
        left, right, (((0,), (0,)), ((), ())), preferred_element_type=jnp.float32
    )


def contract_cols(left, right):
    return lax.dot_general(
        left, right, (((1,), (1,)), ((), ())), preferred_element_type=jnp.float32
    )


def local_pass(
    mel_ext,
    gradient_value,
    first_frame0,
    total,
    w_pre,
    b_pre,
    ups_forward,
    ups_backward,
    upsample_bias,
    w_res,
    b_res,
):
    mel_bins = mel_ext.shape[1]
    kpre = w_pre.shape[0] // mel_bins
    edge = kpre // 2 + 1
    frame_count = mel_ext.shape[0] - 2 * edge
    window_width = upsample_bias.shape[0]
    residual_kernel = w_res.shape[0] // window_width
    patches = jnp.concatenate([mel_ext[i : i + frame_count + 2] for i in range(kpre)], axis=1)
    pre = jnp.dot(patches, w_pre, preferred_element_type=jnp.float32) + b_pre
    frame_idx = first_frame0 - 1 + jnp.arange(frame_count + 2, dtype=jnp.int32)
    inside_f = ((frame_idx >= 0) & (frame_idx < total))[:, None]
    act = jnp.where(inside_f, leaky(pre), 0.0).astype(jnp.bfloat16)
    taps = ups_forward(act).reshape(frame_count + 2, 2 * UPSAMPLE_FACTOR, window_width)
    upper_output = taps[1:, :UPSAMPLE_FACTOR] + taps[:-1, UPSAMPLE_FACTOR:]
    sample_count = UPSAMPLE_FACTOR * frame_count
    start_offset = UPSAMPLE_FACTOR // 2 - DILATION_SIZE
    waveform = (
        upper_output.reshape(UPSAMPLE_FACTOR * (frame_count + 1), window_width)[
            start_offset : start_offset + sample_count + 2 * DILATION_SIZE
        ]
        + upsample_bias
    )
    step_index = (
        UPSAMPLE_FACTOR * first_frame0
        - DILATION_SIZE
        + jnp.arange(sample_count + 2 * DILATION_SIZE, dtype=jnp.int32)
    )
    inside_samples = ((step_index >= 0) & (step_index < UPSAMPLE_FACTOR * total))[:, None]
    hidden_state = jnp.where(inside_samples, leaky(waveform), 0.0).astype(jnp.bfloat16)
    column_block = jnp.concatenate(
        [
            hidden_state[kernel_index * DILATION_SIZE : kernel_index * DILATION_SIZE + sample_count]
            for kernel_index in range(residual_kernel)
        ],
        axis=1,
    )
    convolve_fn = jnp.dot(column_block, w_res, preferred_element_type=jnp.float32) + b_res
    output_rows = (waveform[DILATION_SIZE : DILATION_SIZE + sample_count] + convolve_fn).astype(
        jnp.bfloat16
    )
    g_wres = contract_rows(column_block, gradient_value)
    g_bres = jnp.sum(gradient_value.astype(jnp.float32), axis=0)
    backward_pass = contract_cols(gradient_value, w_res)
    hidden_gradient = jnp.zeros((sample_count + 2 * DILATION_SIZE, window_width), jnp.float32)
    for kernel_index in range(residual_kernel):
        hidden_gradient = hidden_gradient + jnp.pad(
            backward_pass[:, kernel_index * window_width : (kernel_index + 1) * window_width],
            (
                (
                    kernel_index * DILATION_SIZE,
                    (residual_kernel - 1 - kernel_index) * DILATION_SIZE,
                ),
                (0, 0),
            ),
        )
    waveform_gradient = jnp.where(
        inside_samples, hidden_gradient * negative_slope(waveform), 0.0
    ) + jnp.pad(gradient_value.astype(jnp.float32), ((DILATION_SIZE, DILATION_SIZE), (0, 0)))
    waveform_gradient = waveform_gradient.astype(jnp.bfloat16)
    d_upper = jnp.pad(waveform_gradient, ((start_offset, start_offset), (0, 0))).reshape(
        frame_count + 1, UPSAMPLE_FACTOR, window_width
    )
    zero_row = jnp.zeros((1, UPSAMPLE_FACTOR, window_width), jnp.bfloat16)
    d_taps = jnp.concatenate(
        [
            jnp.concatenate([zero_row, d_upper], axis=0),
            jnp.concatenate([d_upper, zero_row], axis=0),
        ],
        axis=1,
    )
    d_act = ups_backward(d_taps.reshape(frame_count + 2, 2 * UPSAMPLE_FACTOR * window_width))
    d_pre = jnp.where(inside_f, d_act * negative_slope(pre), 0.0).astype(jnp.bfloat16)
    g_wpre = contract_rows(patches, d_pre)
    g_bpre = jnp.sum(d_pre.astype(jnp.float32), axis=0)
    return (output_rows, (g_wpre, g_bpre, g_wres, g_bres))


def tile_rows(value):
    if value.ndim == 2 and value.shape[0] % 8 == 0 and value.shape[1] % 128 == 0:
        r, c = value.shape
        value = value.reshape(r // 8, 8, c // 128, 128).transpose(0, 2, 1, 3)
    return jnp.pad(value.reshape(-1), (0, -value.size % 128)).reshape(-1, 128)


def untile_rows(rows, shape):
    if len(shape) == 2 and shape[0] % 8 == 0 and shape[1] % 128 == 0:
        r, c = shape
        return rows.reshape(r // 8, c // 128, 8, 128).transpose(0, 2, 1, 3).reshape(shape)
    size = 1
    for n in shape:
        size *= n
    return rows.reshape(-1)[:size].reshape(shape)


def butterfly_psum(parts):
    dp_size = lax.axis_size("dp")
    tm_size = lax.axis_size("tm")
    axes = ("dp", "tm")
    levels = [("tm", 1 << k) for k in range(tm_size.bit_length() - 1)]
    levels += [("dp", 1 << k) for k in range(1, dp_size.bit_length() - 1)]
    groups = [levels[i : i + 2] for i in range(0, len(levels), 2)]
    orders = (groups, groups[::-1])
    count = dp_size * tm_size

    def perm_of(step, offset):
        out = []
        for d in range(dp_size):
            for t in range(tm_size):
                idx = {"dp": d, "tm": t}
                for j, (axis, bit) in enumerate(orders[d % 2][step]):
                    if (offset >> j) & 1:
                        idx[axis] = idx[axis] ^ bit
                out.append((d * tm_size + t, idx["dp"] * tm_size + idx["tm"]))
        return out

    core = lax.axis_index("dp") % 2
    position = {"dp": lax.axis_index("dp"), "tm": lax.axis_index("tm")}

    def slot_of(step):
        def one(group):
            return sum(((position[a] // b) % 2) << j for j, (a, b) in enumerate(group))

        return jnp.where(core == 0, one(orders[0][step]), one(orders[1][step]))

    tiles = [tile_rows(p) for p in parts]
    flat = jnp.concatenate([t.reshape(-1) for t in tiles])
    unit = 8 * 128 * count
    padded = -(-flat.shape[0] // unit) * unit
    x = jnp.pad(flat, (0, padded - flat.shape[0])).reshape(padded // 128, 128)
    core_perm = [(i, i ^ tm_size) for i in range(count)]
    half = x.shape[0] // 2
    send = lax.dynamic_slice_in_dim(x, (1 - core) * half, half)
    x = lax.dynamic_slice_in_dim(x, core * half, half) + lax.ppermute(send, axes, core_perm)
    for step in range(len(groups) - 1):
        radix = 1 << len(groups[step])
        piece = x.shape[0] // radix
        slot = slot_of(step)
        total = lax.dynamic_slice_in_dim(x, slot * piece, piece)
        for offset in range(1, radix):
            send = lax.dynamic_slice_in_dim(x, (slot ^ offset) * piece, piece)
            total = total + lax.ppermute(send, axes, perm_of(step, offset))
        x = total
    if groups:
        last = len(groups) - 1
        radix = 1 << len(groups[last])
        slot = slot_of(last)
        got = [x] + [lax.ppermute(x, axes, perm_of(last, o)) for o in range(1, radix)]
        pieces = []
        for q in range(radix):
            source = slot ^ q
            chosen = got[radix - 1]
            for o in range(radix - 2, -1, -1):
                chosen = jnp.where(source == o, got[o], chosen)
            pieces.append(chosen)
        while len(pieces) > 1:
            pieces = [pieces[i] + pieces[i + 1] for i in range(0, len(pieces), 2)]
        x = pieces[0]
    for step in reversed(range(len(groups) - 1)):
        radix = 1 << len(groups[step])
        slot = slot_of(step)
        got = [x] + [lax.ppermute(x, axes, perm_of(step, o)) for o in range(1, radix)]
        pieces = []
        for q in range(radix):
            source = slot ^ q
            chosen = got[radix - 1]
            for o in range(radix - 2, -1, -1):
                chosen = jnp.where(source == o, got[o], chosen)
            pieces.append(chosen)
        x = jnp.concatenate(pieces)
    recv = lax.ppermute(x, axes, core_perm)
    x = jnp.where(core == 0, jnp.concatenate([x, recv]), jnp.concatenate([recv, x]))
    out, at = [], 0
    for p, t in zip(parts, tiles):
        out.append(untile_rows(x[at : at + t.shape[0]], p.shape))
        at += t.shape[0]
    return tuple(out)

def ups_functions(w_ups):
    dp_size = lax.axis_size("dp")
    if lax.axis_size("tm") != 2 or dp_size % 2:
        whole = lax.all_gather(w_ups, "tm", axis=0, tiled=True)
        return (
            lambda act: jnp.dot(act, whole, preferred_element_type=jnp.float32),
            lambda d_taps: contract_cols(d_taps, whole),
            whole,
        )
    rows, width = w_ups.shape
    cols = width // 2
    core = lax.axis_index("dp") % 2
    tm = lax.axis_index("tm")
    head = 16 if rows % 32 == 0 and rows > 32 else 0
    swap = [(i, i ^ 1) for i in range(dp_size)]
    mine = jnp.where(core == 0, w_ups[head:, :cols], w_ups[head:, cols:])
    got = lax.ppermute(mine, "tm", [(0, 1), (1, 0)])
    partner = lax.ppermute(got, "dp", swap)
    low = jnp.where(core == 0, got, partner)
    high = jnp.where(core == 0, partner, got)
    got_parts = [got]
    if head:
        first = lax.ppermute(w_ups[:head], "tm", [(0, 1), (1, 0)])
        got_parts = [first]
        low = jnp.concatenate([first[:, :cols], low])
        high = jnp.concatenate([first[:, cols:], high])

    def forward(act):
        own_act = lax.dynamic_slice_in_dim(act, tm * rows, rows, axis=1)
        other_act = lax.dynamic_slice_in_dim(act, (1 - tm) * rows, rows, axis=1)
        own = jnp.dot(own_act, w_ups, preferred_element_type=jnp.float32)
        other = jnp.concatenate(
            [
                jnp.dot(other_act, low, preferred_element_type=jnp.float32),
                jnp.dot(other_act, high, preferred_element_type=jnp.float32),
            ],
            axis=1,
        )
        return own + other

    def backward(d_taps):
        own = contract_cols(d_taps, w_ups)
        other = contract_cols(d_taps[:, :cols], low) + contract_cols(d_taps[:, cols:], high)
        return jnp.where(
            tm == 0, jnp.concatenate([own, other], axis=1), jnp.concatenate([other, own], axis=1)
        )

    return forward, backward, got_parts[0]


def on_device(
    src_mel, owner, dst_pos, keep, cotangent, w_pre, b_pre, w_ups, upsample_bias, w_res, b_res
):
    owners_count = lax.axis_size("dp")
    ups_forward, ups_backward, ready = ups_functions(w_ups)
    src_mel, _ = lax.optimization_barrier((src_mel, ready))
    seg_rows = src_mel[0]
    seg_count = seg_rows.shape[0]
    mel_bins = w_pre.shape[0] // KPRE
    pick = jnp.arange(owners_count, dtype=jnp.int32)[:, None] == owner[0][None, :]
    seg_width = seg_rows.shape[1]
    header = jnp.stack([dst_pos[0] + 1, keep[0]], axis=1).astype(jnp.bfloat16)
    seg_ext = jnp.concatenate([seg_rows, header], axis=1)
    outgoing = jnp.dot(
        pick.astype(jnp.bfloat16), seg_ext, preferred_element_type=jnp.float32
    ).astype(jnp.bfloat16)
    arrived = lax.all_to_all(outgoing, "dp", split_axis=0, concat_axis=0, tiled=True)
    slot_code = arrived[:, seg_width].astype(jnp.int32)
    keep_code = arrived[:, seg_width + 1].astype(jnp.int32)
    place = (slot_code - 1)[:, None] == jnp.arange(seg_count, dtype=jnp.int32)[None, :]
    mel_segs = contract_rows(place.astype(jnp.bfloat16), arrived[:, :seg_width]).astype(
        jnp.bfloat16
    )
    keep_segs = jnp.sum(jnp.where(place, keep_code[:, None], 0), axis=0)
    mel = mel_segs.reshape(seg_count * (mel_segs.shape[1] // mel_bins), mel_bins)
    frame_count = mel.shape[0]
    mel_ext = with_halo(mel, (("tm", 0),), KPRE // 2 + 1)
    first_frame0 = lax.axis_index("tm") * frame_count
    total = lax.axis_size("tm") * frame_count
    cot = cotangent[0]
    marks = jnp.repeat(keep_segs, cot.shape[0] // seg_count)
    gradient_value = jnp.where(marks[:, None] > 0, cot, jnp.zeros_like(cot))
    output_rows, grads = local_pass(
        mel_ext,
        gradient_value,
        first_frame0,
        total,
        w_pre,
        b_pre,
        ups_forward,
        ups_backward,
        upsample_bias,
        w_res,
        b_res,
    )
    summed = butterfly_psum(grads)
    return (output_rows[None], summed[0], summed[1], summed[2], summed[3])


def solution(mesh):
    in_specs = (
        P("tm", "dp", None),
        P("tm", "dp"),
        P("tm", "dp"),
        P("tm", "dp"),
        P("dp", "tm", None),
        P(),
        P(),
        P("tm", None),
        P(),
        P(),
        P(),
    )
    out_specs = (P("dp", "tm", None), P(), P(), P(), P())
    return jax.shard_map(
        on_device, mesh=mesh, in_specs=in_specs, out_specs=out_specs, check_vma=False
    )
```
